32 devices in a mesh: ctx: 8 (over y, x, core), fsdp: 4 (over z).
Axes of the slice: x: 2, y: 2, z: 4, core: 2. Of those that a mesh axis runs over, the one named last changes fastest.
Arguments:
- hidden_in: float32 [4, 1024, 2048], P('fsdp', 'ctx'), may hold values from -6 to 6
- block_map: int32 [16], replicated, may hold values from 0 to 15, each once
- doc_ids: int32 [4, 1024], P('fsdp'), may hold values from 0 to 3, never falling along the last dimension, each value on 1 to 512 neighbouring positions
- routes: int32 [4, 1024, 8], P('fsdp', 'ctx'), may hold values from 0 to 15, all different within a row; in each aligned block of 128 rows (0 to 127, 128 to 255, ..., all dimensions but the last counted through in order) at most 96 rows name the same one
- attn_gain: float32 [2048], replicated, may hold values from 0.5 to 1.5
- query_proj: bfloat16 [2048, 4096], P('fsdp'), may hold values from -0.125 to 0.125
- key_proj: bfloat16 [2048, 512], P('fsdp'), may hold values from -0.125 to 0.125
- value_proj: bfloat16 [2048, 512], P('fsdp'), may hold values from -0.125 to 0.125
- query_gain: float32 [128], replicated, may hold values from 0.1 to 1.9
- key_gain: float32 [128], replicated, may hold values from 0.1 to 1.9
- out_proj: bfloat16 [4096, 2048], P('fsdp'), may hold values from -0.375 to 0.375
- ffn_gain: float32 [2048], replicated, may hold values from 0.5 to 1.5
- router_proj: bfloat16 [2048, 16], P('fsdp'), may hold values from -0.125 to 0.125
- expert_gate: bfloat16 [16, 2048, 768], P('ctx', 'fsdp'), may hold values from -0.125 to 0.125
- expert_up: bfloat16 [16, 2048, 768], P('ctx', 'fsdp'), may hold values from -0.125 to 0.125
- expert_down: bfloat16 [16, 768, 2048], P('ctx', 'fsdp'), may hold values from -0.4375 to 0.4375
- cotangent: float32 [4, 1024, 2048], P('fsdp', 'ctx'), may hold values from -6 to 6
Outputs:
- layer_out: float32 [4, 1024, 2048], P('fsdp', 'ctx')
- input_grad: float32 [4, 1024, 2048], P('fsdp', 'ctx')
- attn_gain_grad: float32 [2048], replicated
- query_proj_grad: float32 [2048, 4096], P('fsdp')
- key_proj_grad: float32 [2048, 512], P('fsdp')
- value_proj_grad: float32 [2048, 512], P('fsdp')
- query_gain_grad: float32 [128], replicated
- key_gain_grad: float32 [128], replicated
- out_proj_grad: float32 [4096, 2048], P('fsdp')
- ffn_gain_grad: float32 [2048], replicated
- router_grad: float32 [2048, 16], P('fsdp')
- gate_grad: float32 [16, 2048, 768], P('ctx', 'fsdp')
- up_grad: float32 [16, 2048, 768], P('ctx', 'fsdp')
- down_grad: float32 [16, 768, 2048], P('ctx', 'fsdp')
The draws below stay inside these ranges and needn't reach their ends.
Inputs may be any that keep to these rules, and one draw needn't show every extreme that they name: `block_map`: A permutation: every block of positions is held by exactly one stored block. `doc_ids`: along the positions of a sequence the document numbers never fall; each document is 1 to 512 positions long and one is exactly that long. `routes`: each token names 8 different experts. Within the 128 stored rows of one device (aligned blocks of rows), no expert is named by more than 96 of them, and in every draw some expert is named by exactly 96.
All inputs are finite; a program needn't handle non-finite values.
Results may differ from the reference program's by a relative error of at most 0.024.
Values may be sent and summed in bfloat16 or wider, within the bound.
No kernel may reach another device: no remote copies, remote signals or barrier semaphores. Data moves between devices by JAX's collectives and lax.ppermute only.
A program may use at most 320 MiB of HBM per device.

```python
import math
import jax
import jax.numpy as jnp
import numpy as np
from jax import lax

D = 2048
HEADS = 32
KV_HEADS = 4
HEAD_DIM = 128
FF = 768
TOP = 8
TOK_DEV = 128
DOCS = 4
QD = 4096
KVD = 512
SEQ_LEN = 1024
SEQS = 4
BLOCKS = 16
EXPERTS = 16
CAP = 96


def shard_levels(stream_key, dims, shards, least, top_value):
    gain = 1.0
    for axis_at, blocks in shards:
        steps = jax.random.uniform(jax.random.fold_in(jax.random.fold_in(stream_key, 6), axis_at), (blocks,), jnp.float32, least / len(shards), top_value / len(shards))
        gain = gain * jnp.repeat(jnp.exp(steps), dims[axis_at] // blocks).reshape((-1,) + (1,) * (len(dims) - 1 - axis_at))
    return gain


def split_up(count, total, reach, lean):
    weights = [(1 << 20) // math.isqrt(rank ** lean) + 1 for rank in range(2, count + 1)]
    rest, given = total - reach - (count - 1), [1] * (count - 1)
    while rest > 0:
        candidates = [i for i in range(count - 1) if given[i] < reach]
        whole, left = sum([weights[i] for i in candidates]), rest
        for i in candidates:
            extra = min(reach - given[i], max(1, left * weights[i] // whole), rest)
            given[i] = given[i] + extra
            rest = rest - extra
    return np.array([reach] + given)


def uneven_parts(own_key, count, total, bound, slope):
    if count == 2:
        one = jax.random.randint(own_key, (), max(1, total - bound), min(bound, total - 1) + 1)
        return jnp.stack([one, total - one])
    tallies = jnp.asarray(split_up(count, total, bound, slope), jnp.int32)
    couples = (count - 1) // 2
    source_of, sink = tallies[1:1 + 2 * couples:2], tallies[2:2 + 2 * couples:2]
    margin = jnp.minimum(source_of - 1, bound - sink)
    shifted = jax.random.randint(jax.random.fold_in(own_key, 1), (couples,), 0, 1 << 20) % (margin + 1)
    tallies = tallies.at[1:1 + 2 * couples:2].set(source_of - shifted).at[2:2 + 2 * couples:2].set(sink + shifted)
    return tallies[jax.random.permutation(jax.random.fold_in(own_key, 2), count)]


def shared_out(rng, own, number, rows, number_of, top, most, lean):
    ranking = jax.random.permutation(rng, number_of)
    heavy_load, ordinary = portions_of(number_of, rows * top, most, lean, True), portions_of(number_of, rows * top, most, lean, False)
    places = jnp.arange(number_of)

    def named(lengths, offset_by):
        used = int((lengths > 0).sum())
        fixed = max(1, used // 4)
        shifted = fixed + (places - fixed + offset_by * (used - fixed)) % max(1, number_of - fixed)
        return jnp.zeros((number_of,), jnp.int32).at[ranking[jnp.where(places < fixed, places, shifted)]].set(jnp.asarray(lengths, jnp.int32))

    lengths = jnp.where(number % 4 == 0, named(heavy_load, number // 4), named(ordinary, number - number // 4 - 1))
    mixed = jax.random.permutation(jax.random.fold_in(own, 3), number_of)
    donor, receiver = mixed[0:number_of // 2 * 2:2], mixed[1:number_of // 2 * 2:2]
    margin = jnp.minimum(lengths[donor] - 1, most - lengths[receiver]) // 2
    margin = jnp.where((donor == ranking[0]) | (receiver == ranking[0]) | (lengths[receiver] == 0), 0, jnp.maximum(margin, 0))
    shifted = jax.random.randint(jax.random.fold_in(own, 4), (number_of // 2,), 0, 1 << 20) % (margin + 1)
    lengths = lengths.at[donor].add(-shifted).at[receiver].add(shifted)
    labels = jnp.searchsorted(jnp.cumsum(lengths), jnp.arange(rows * top), side="right").astype(jnp.int32)
    listing = labels.reshape(top, rows).T
    listing = listing[jax.random.permutation(jax.random.fold_in(own, 1), rows)]
    offset_by = jax.random.randint(jax.random.fold_in(own, 2), (rows, 1), 0, top)
    return jnp.take_along_axis(listing, (jnp.arange(top)[None, :] + offset_by) % top, axis=1)


def portions_of(amount, total, most, lean, full):
    loads = [(1 << 20) // math.isqrt(rank ** lean) + 1 for rank in range(1, amount + 1)]
    largest = most if full else min(most, max(-(-total // amount), total * loads[0] // sum(loads)))
    least = 1 if total - largest >= amount - 1 else 0
    given, surplus = [largest] + [least] * (amount - 1), total - largest - least * (amount - 1)
    while surplus > 0:
        free = [i for i in range(1, amount) if given[i] < largest] or [i for i in range(1, amount) if given[i] < most]
        whole, left = sum([loads[i] for i in free]), surplus
        for i in free:
            more = min(most - given[i], max(1, left * loads[i] // whole), surplus)
            given[i] = given[i] + more
            surplus = surplus - more
    return np.array(given)


def noise(own_key, shape, deviation, limit, cuts=(), held_as=jnp.bfloat16):
    drawn = jax.random.normal(own_key, shape, jnp.float32) * deviation
    if len(cuts) > 0:
        drawn = shard_levels(own_key, shape, cuts, -0.22, 0.18) * drawn
    return jnp.clip(drawn, min=-limit, max=limit).astype(held_as)


def setup_inputs(seed: int = 0) -> dict:
    seeds = jax.random.split(jax.random.key(seed), 18)
    hidden_in = noise(seeds[0], (SEQS, SEQ_LEN, D), 1.0, 6.0, ((0, 4), (1, 8)), jnp.float32)
    block_map = jax.random.permutation(seeds[1], BLOCKS).astype(jnp.int32)
    doc_ids = jax.vmap(lambda own: jnp.searchsorted(jnp.cumsum(uneven_parts(own, DOCS, SEQ_LEN, SEQ_LEN // 2, 0)), jnp.arange(SEQ_LEN), side="right"))(jax.random.split(seeds[2], SEQS)).reshape((SEQS, SEQ_LEN)).astype(jnp.int32)
    routes_keys = jax.random.split(jax.random.fold_in(seeds[3], 1), SEQS * SEQ_LEN // TOK_DEV)
    routes_turns = jax.random.permutation(jax.random.fold_in(seeds[3], 3), SEQS * SEQ_LEN // TOK_DEV)
    routes = jax.vmap(lambda own, number: shared_out(jax.random.fold_in(seeds[3], 2), own, number, TOK_DEV, EXPERTS, TOP, CAP, 2))(routes_keys, routes_turns).reshape((SEQS, SEQ_LEN, TOP))
    attn_gain = jnp.clip(1.0 + 0.1 * jax.random.normal(seeds[4], (D,), jnp.float32), 0.5, 1.5)
    query_proj = noise(seeds[5], (D, QD), D ** -0.5, 0.125, ((0, 4),))
    key_proj = noise(seeds[6], (D, KVD), D ** -0.5, 0.125, ((0, 4),))
    value_proj = noise(seeds[7], (D, KVD), D ** -0.5, 0.125, ((0, 4),))
    query_gain = jnp.clip(1.0 + 0.18 * jax.random.normal(seeds[8], (HEAD_DIM,), jnp.float32), 0.1, 1.9)
    key_gain = jnp.clip(1.0 + 0.18 * jax.random.normal(seeds[9], (HEAD_DIM,), jnp.float32), 0.1, 1.9)
    out_proj = noise(seeds[10], (QD, D), (QD // 16) ** -0.5, 0.375, ((0, 4),))
    ffn_gain = jnp.clip(1.0 + 0.1 * jax.random.normal(seeds[11], (D,), jnp.float32), 0.5, 1.5)
    router_proj = noise(seeds[12], (D, EXPERTS), D ** -0.5, 0.125, ((0, 4),))
    expert_gate = noise(seeds[13], (EXPERTS, D, FF), D ** -0.5, 0.125, ((0, 8), (1, 4)))
    expert_up = noise(seeds[14], (EXPERTS, D, FF), D ** -0.5, 0.125, ((0, 8), (1, 4)))
    expert_down = noise(seeds[15], (EXPERTS, FF, D), (FF // 4) ** -0.5, 0.4375, ((0, 8), (1, 4)))
    cotangent = noise(seeds[16], (SEQS, SEQ_LEN, D), 1.0, 6.0, ((0, 4), (1, 8)), jnp.float32)
    return {"hidden_in": hidden_in, "block_map": block_map, "doc_ids": doc_ids, "routes": routes, "attn_gain": attn_gain, "query_proj": query_proj, "key_proj": key_proj, "value_proj": value_proj, "query_gain": query_gain, "key_gain": key_gain, "out_proj": out_proj, "ffn_gain": ffn_gain, "router_proj": router_proj, "expert_gate": expert_gate, "expert_up": expert_up, "expert_down": expert_down, "cotangent": cotangent}


EPSILON = 1e-06
ROPE_BASE = 1000000.0
NEG_FILL = -1e+30

@jax.custom_vjp
def low(v):
    return lax.optimization_barrier(v.astype(jnp.bfloat16)).astype(jnp.float32)

@jax.custom_vjp
def low_back(v):
    return v

def low_keep(v):
    return (low(v), None)

def low_pass(kept, grad):
    return (grad,)

def back_keep(v):
    return (v, None)

def back_low(kept, grad):
    return (low(grad),)
low.defvjp(low_keep, low_pass)
low_back.defvjp(back_keep, back_low)

def rms_scale(field):
    return lax.rsqrt(lax.optimization_barrier(jnp.mean(field * field, axis=-1, keepdims=True)) + EPSILON)

def rotary(positions):
    halfway = HEAD_DIM // 2
    inverse = ROPE_BASE ** (-2.0 * jnp.arange(halfway, dtype=jnp.float32) / HEAD_DIM)
    angle = positions.astype(jnp.float32)[:, None] * inverse[None, :]
    return (jnp.cos(angle), jnp.sin(angle))

def rotate(field, cosine, sine_table):
    halfway = field.shape[-1] // 2
    former = field[..., :halfway]
    latter = field[..., halfway:]
    cos_b = cosine[:, None, :]
    sin_b = sine_table[:, None, :]
    return jnp.concatenate([former * cos_b - latter * sin_b, latter * cos_b + former * sin_b], axis=-1)

def head_norm(field, factor):
    return field * rms_scale(field) * factor

def attention(query, key_rot, values, positions, documents):
    length = query.shape[0]
    block_rows = min(512, length)
    group_size = HEADS // KV_HEADS
    score_scale = HEAD_DIM ** (-0.5)
    highest = lax.Precision.HIGHEST

    def one_block(start):
        q_block = lax.dynamic_slice_in_dim(query, start, block_rows, 0).reshape(block_rows, KV_HEADS, group_size, HEAD_DIM)
        pos_block = lax.dynamic_slice_in_dim(positions, start, block_rows, 0)
        doc_block = lax.dynamic_slice_in_dim(documents, start, block_rows, 0)
        scores = jnp.einsum('qkgd,tkd->kgqt', q_block, key_rot, precision=highest) * score_scale
        scores = low_back(scores)
        allowed = (positions[None, :] <= pos_block[:, None]) & (documents[None, :] == doc_block[:, None])
        scores = jnp.where(allowed[None, None], scores, NEG_FILL)
        probs = low(jax.nn.softmax(scores, axis=-1))
        mixed = jnp.einsum('kgqt,tkd->qkgd', probs, values, precision=highest)
        return mixed.reshape(block_rows, HEADS * HEAD_DIM)
    starts = jnp.arange(length // block_rows, dtype=jnp.int32) * block_rows
    return lax.map(jax.checkpoint(one_block), starts).reshape(length, HEADS * HEAD_DIM)

def block_forward(params, hidden, positions, documents, route_ids):
    attn_gain, w_query, w_key, w_value, query_gain, key_gain, w_out, ffn_gain, w_router, w_gate, w_up, w_down = params
    highest = lax.Precision.HIGHEST
    length = hidden.shape[0]
    first_input = low(hidden * rms_scale(hidden) * attn_gain)
    query = low_back(jnp.dot(first_input, w_query, precision=highest))
    key_raw = low_back(jnp.dot(first_input, w_key, precision=highest))
    values = low_back(low(jnp.dot(first_input, w_value, precision=highest)))
    cosine, sine_table = rotary(positions)
    query = low(rotate(head_norm(query.reshape(length, HEADS, HEAD_DIM), query_gain), cosine, sine_table))
    key_rot = low(rotate(head_norm(key_raw.reshape(length, KV_HEADS, HEAD_DIM), key_gain), cosine, sine_table))
    values = values.reshape(length, KV_HEADS, HEAD_DIM)
    attended = low_back(low(attention(query, key_rot, values, positions, documents)))
    branch = low_back(jnp.dot(attended, w_out, precision=highest))
    middle = hidden + branch
    second_input = low(middle * rms_scale(middle) * ffn_gain)
    logits = low_back(jnp.dot(second_input, w_router, precision=highest))
    chosen = jnp.take_along_axis(logits, route_ids, axis=1)
    route_weights = jax.nn.softmax(chosen, axis=-1)
    experts = w_router.shape[1]
    route_hot = (route_ids[:, :, None] == jnp.arange(experts, dtype=jnp.int32)[None, None, :]).astype(jnp.float32)
    combine = lax.optimization_barrier(jnp.sum(route_weights[:, :, None] * route_hot, axis=1))

    def expert_step(total, inputs):
        gate_e, up_e, down_e, column = inputs
        copied = low_back(second_input)
        gate_val = low_back(jnp.dot(copied, gate_e, precision=highest))
        up_val = low_back(jnp.dot(copied, up_e, precision=highest))
        hid_low = low(jax.nn.silu(gate_val) * up_val)
        result = low_back(low(jnp.dot(hid_low, down_e, precision=highest)))
        return (total + column[:, None] * result, None)
    mixture, unused = lax.scan(expert_step, jnp.zeros_like(hidden), (w_gate, w_up, w_down, combine.T))
    return middle + mixture

def reference(hidden_in, block_map, doc_ids, routes, attn_gain, query_proj, key_proj, value_proj, query_gain, key_gain, out_proj, ffn_gain, router_proj, expert_gate, expert_up, expert_down, cotangent):
    block_len = TOK_DEV // 2
    offsets = jnp.arange(block_len, dtype=jnp.int32)
    positions = (block_map.astype(jnp.int32)[:, None] * block_len + offsets[None, :]).reshape(-1).astype(jnp.int32)
    params = tuple((item.astype(jnp.float32) for item in (attn_gain, query_proj, key_proj, value_proj, query_gain, key_gain, out_proj, ffn_gain, router_proj, expert_gate, expert_up, expert_down)))
    zero_grads = tuple((jnp.zeros_like(item) for item in params))

    def one_sequence(totals, inputs):
        hidden, doc_row, route_ids, cot_row = inputs
        documents = jnp.take(doc_row, positions)

        def apply_layer(*operands):
            return block_forward(operands[:-1], operands[-1], positions, documents, route_ids)
        result, pullback = jax.vjp(apply_layer, *params, hidden)
        grads = pullback(cot_row)
        totals = tuple((acc + piece for acc, piece in zip(totals, grads[:-1])))
        return (totals, (result, grads[-1]))
    totals, (outputs, input_grads) = lax.scan(one_sequence, zero_grads, (hidden_in, doc_ids, routes, cotangent))
    return (outputs, input_grads, totals[0], totals[1], totals[2], totals[3], totals[4], totals[5], totals[6], totals[7], totals[8], totals[9], totals[10], totals[11])
```

```python
import jax
import jax.numpy as jnp
from jax import lax
from jax.sharding import PartitionSpec as P

D = 2048
HEADS = 32
KV_HEADS = 4
HEAD_DIM = 128
TOP = 8


EPSILON = 1e-06
ROPE_BASE = 1000000.0
NEG_FILL = -1e30


def matmul(left, right):
    return jnp.dot(left, right, preferred_element_type=jnp.float32)


def contract(form, left, right):
    return jnp.einsum(form, left, right, preferred_element_type=jnp.float32)


def rms_scale(field):
    return lax.rsqrt(jnp.mean(field * field, axis=-1, keepdims=True) + EPSILON)


def rotary(positions):
    halfway = HEAD_DIM // 2
    inverse = ROPE_BASE ** (-2.0 * jnp.arange(halfway, dtype=jnp.float32) / HEAD_DIM)
    angle = positions.astype(jnp.float32)[:, None] * inverse[None, :]
    return (jnp.cos(angle), jnp.sin(angle))


def rotate(field, cosine, sine_table):
    halfway = field.shape[-1] // 2
    former = field[..., :halfway]
    latter = field[..., halfway:]
    cos_b = cosine[:, None, :]
    sin_b = sine_table[:, None, :]
    return jnp.concatenate(
        [former * cos_b - latter * sin_b, latter * cos_b + former * sin_b], axis=-1
    )


def rotate_back(field, cosine, sine_table):
    halfway = field.shape[-1] // 2
    former = field[..., :halfway]
    latter = field[..., halfway:]
    cos_b = cosine[:, None, :]
    sin_b = sine_table[:, None, :]
    return jnp.concatenate(
        [former * cos_b + latter * sin_b, latter * cos_b - former * sin_b], axis=-1
    )


def norm_back(grad, normed, inv_scale, factor):
    lead_axes = tuple(range(grad.ndim - 1))
    factor_grad = jnp.sum(grad * normed, axis=lead_axes)
    scaled = grad * factor
    return (
        inv_scale * (scaled - normed * jnp.mean(scaled * normed, axis=-1, keepdims=True)),
        factor_grad,
    )


def per_device(
    hidden_in,
    block_map,
    doc_ids,
    routes,
    attn_gain,
    query_proj,
    key_proj,
    value_proj,
    query_gain,
    key_gain,
    out_proj,
    ffn_gain,
    router_proj,
    expert_gate,
    expert_up,
    expert_down,
    cotangent,
):
    tokens = hidden_in.shape[1]
    ctx_size = lax.axis_size("ctx")
    fsdp_size = lax.axis_size("fsdp")
    fsdp_index = lax.axis_index("fsdp")
    local_experts = expert_gate.shape[0]
    experts = local_experts * ctx_size
    capacity = min(tokens, 3 * tokens * TOP // (2 * experts))
    block_len = tokens // 2
    group_size = HEADS // KV_HEADS
    score_scale = HEAD_DIM ** (-0.5)
    heads_dev = HEADS // fsdp_size
    share = max(1, fsdp_size // KV_HEADS)
    kv_dev = max(1, heads_dev // group_size)
    group_dev = heads_dev // kv_dev
    d_part = D // fsdp_size
    seqs = fsdp_size
    group_rows = seqs * tokens

    ctx_index = lax.axis_index("ctx")
    own_blocks = lax.dynamic_slice_in_dim(block_map, 2 * ctx_index, 2, 0)
    offsets = jnp.arange(block_len, dtype=jnp.int32)
    local_pos = (own_blocks[:, None] * block_len + offsets[None, :]).reshape(-1)
    all_pos = (block_map[:, None] * block_len + offsets[None, :]).reshape(-1)
    doc_rows = lax.all_gather(doc_ids[0], "fsdp", axis=0, tiled=False)
    docs_query = jnp.take(doc_rows, local_pos, axis=1)
    docs_key = jnp.take(doc_rows, all_pos, axis=1)
    visible = (all_pos[None, None, :] <= local_pos[None, :, None]) & (
        docs_key[:, None, :] == docs_query[:, :, None]
    )
    cosine, sine_table = rotary(local_pos)
    hidden = hidden_in[0]
    first_scale = rms_scale(hidden)
    first_normed = hidden * first_scale
    first_input = (first_normed * attn_gain).astype(jnp.bfloat16)
    group_input = lax.all_gather(first_input, "fsdp", axis=0, tiled=True)
    w_query_cols = lax.all_to_all(query_proj, "fsdp", 1, 0, tiled=True)
    if share == 1:
        w_key_cols = lax.all_to_all(key_proj, "fsdp", 1, 0, tiled=True)
        w_value_cols = lax.all_to_all(value_proj, "fsdp", 1, 0, tiled=True)
    else:
        kv_start = (fsdp_index // share) * HEAD_DIM
        w_key_cols = lax.dynamic_slice_in_dim(
            lax.all_gather(key_proj, "fsdp", axis=0, tiled=True), kv_start, HEAD_DIM, 1
        )
        w_value_cols = lax.dynamic_slice_in_dim(
            lax.all_gather(value_proj, "fsdp", axis=0, tiled=True), kv_start, HEAD_DIM, 1
        )
    query_raw = matmul(group_input, w_query_cols).reshape(seqs, tokens, heads_dev, HEAD_DIM)
    key_raw = matmul(group_input, w_key_cols).reshape(seqs, tokens, kv_dev, HEAD_DIM)
    value_low = (
        matmul(group_input, w_value_cols)
        .astype(jnp.bfloat16)
        .reshape(seqs, tokens, kv_dev * HEAD_DIM)
    )
    query_scale = rms_scale(query_raw)
    query_normed = query_raw * query_scale
    query_rot = rotate(query_normed * query_gain, cosine, sine_table).astype(jnp.bfloat16)
    key_scale = rms_scale(key_raw)
    key_normed = key_raw * key_scale
    key_rot = (
        rotate(key_normed * key_gain, cosine, sine_table)
        .reshape(seqs, tokens, kv_dev * HEAD_DIM)
        .astype(jnp.bfloat16)
    )
    keys_all = lax.all_gather(key_rot, "ctx", axis=1, tiled=True).reshape(
        seqs, -1, kv_dev, HEAD_DIM
    )
    values_all = lax.all_gather(value_low, "ctx", axis=1, tiled=True).reshape(
        seqs, -1, kv_dev, HEAD_DIM
    )
    query_groups = query_rot.reshape(seqs, tokens, kv_dev, group_dev, HEAD_DIM)

    def masked_scores():
        scores = contract("stkgd,sjkd->skgtj", query_groups, keys_all) * score_scale
        return jnp.where(visible[:, None, None], scores, NEG_FILL)

    scores = masked_scores()
    peak = jnp.max(scores, axis=-1, keepdims=True)
    expo = jnp.exp(scores - peak)
    total = jnp.sum(expo, axis=-1, keepdims=True)
    probs = (expo / total).astype(jnp.bfloat16)
    log_sums = peak + jnp.log(total)
    attended = (
        contract("skgtj,sjkd->stkgd", probs, values_all)
        .astype(jnp.bfloat16)
        .reshape(group_rows, heads_dev * HEAD_DIM)
    )
    branch_parts = matmul(attended, out_proj).reshape(seqs, tokens, D)
    branch = lax.psum_scatter(branch_parts, "fsdp", scatter_dimension=0, tiled=True)[0]
    middle = hidden + branch
    second_scale = rms_scale(middle)
    second_normed = middle * second_scale
    second_input = (second_normed * ffn_gain).astype(jnp.bfloat16)
    w_gate, w_up, w_down, w_router = (
        lax.all_gather(expert_gate, "fsdp", axis=1, tiled=True),
        lax.all_gather(expert_up, "fsdp", axis=1, tiled=True),
        lax.all_gather(expert_down, "fsdp", axis=1, tiled=True),
        lax.all_gather(router_proj, "fsdp", axis=0, tiled=True),
    )
    logits = matmul(second_input, w_router)
    route_ids = routes[0]
    chosen = jnp.take_along_axis(logits, route_ids, axis=1)
    route_weights = jax.nn.softmax(chosen, axis=-1)
    flat_ids = route_ids.reshape(-1)
    expert_range = jnp.arange(experts, dtype=jnp.int32)
    one_hot = (flat_ids[:, None] == expert_range[None, :]).astype(jnp.int32)
    earlier = jnp.cumsum(one_hot, axis=0) - one_hot
    slot_index = jnp.sum(earlier * one_hot, axis=1)
    target = flat_ids * capacity + slot_index

    def dispatch(route_rows):
        buffer = jnp.zeros((experts * capacity, D), jnp.bfloat16).at[target].set(route_rows)
        return buffer.reshape(ctx_size, local_experts, capacity, D)

    def collect(returned):
        return jnp.take(returned.reshape(experts * capacity, D), target, axis=0)

    received = lax.all_to_all(
        dispatch(jnp.repeat(second_input, TOP, axis=0)),
        "ctx",
        split_axis=0,
        concat_axis=2,
        tiled=True,
    )[0]
    gate_val = contract("erd,edf->erf", received, w_gate)
    up_val = contract("erd,edf->erf", received, w_up)
    gate_sig = jax.nn.sigmoid(gate_val)
    hid_low = (gate_val * gate_sig * up_val).astype(jnp.bfloat16)
    expert_out = contract("erf,efd->erd", hid_low, w_down).astype(jnp.bfloat16)
    route_out = (
        collect(lax.all_to_all(expert_out[None], "ctx", split_axis=2, concat_axis=0, tiled=True))
        .reshape(tokens, TOP, D)
        .astype(jnp.float32)
    )
    layer_out = middle + jnp.einsum("tr,trd->td", route_weights, route_out)
    grad_out = cotangent[0]
    grad_weights = jnp.einsum("td,trd->tr", grad_out, route_out)
    grad_routes = (
        (route_weights[:, :, None] * grad_out[:, None, :])
        .astype(jnp.bfloat16)
        .reshape(tokens * TOP, D)
    )
    grad_expert = lax.all_to_all(
        dispatch(grad_routes), "ctx", split_axis=0, concat_axis=2, tiled=True
    )[0]
    grad_hid = contract("erd,efd->erf", grad_expert, w_down)
    down_grad_full = contract("erf,erd->efd", hid_low, grad_expert)
    grad_gate = (grad_hid * up_val * gate_sig * (1.0 + gate_val * (1.0 - gate_sig))).astype(
        jnp.bfloat16
    )
    grad_up = (grad_hid * gate_val * gate_sig).astype(jnp.bfloat16)
    gate_grad_full = contract("erd,erf->edf", received, grad_gate)
    up_grad_full = contract("erd,erf->edf", received, grad_up)
    grad_rows = (
        contract("erf,edf->erd", grad_gate, w_gate) + contract("erf,edf->erd", grad_up, w_up)
    ).astype(jnp.bfloat16)
    grad_copies = collect(
        lax.all_to_all(grad_rows[None], "ctx", split_axis=2, concat_axis=0, tiled=True)
    ).reshape(tokens, TOP, D)
    grad_chosen = route_weights * (
        grad_weights - jnp.sum(route_weights * grad_weights, axis=-1, keepdims=True)
    )
    route_hot = (route_ids[:, :, None] == expert_range[None, None, :]).astype(jnp.float32)
    grad_logits = jnp.einsum("tr,tre->te", grad_chosen, route_hot).astype(jnp.bfloat16)
    router_grad_full = contract("td,te->de", second_input, grad_logits)
    grad_second = jnp.sum(grad_copies.astype(jnp.float32), axis=1) + contract(
        "te,de->td", grad_logits, w_router
    )
    grad_middle, ffn_gain_grad = norm_back(grad_second, second_normed, second_scale, ffn_gain)
    grad_middle = grad_middle + grad_out

    grad_branch = lax.all_gather(grad_middle.astype(jnp.bfloat16), "fsdp", axis=0, tiled=True)
    out_grad_part = contract("tq,td->qd", attended, grad_branch)
    grad_attended = contract("td,qd->tq", grad_branch, out_proj).astype(jnp.bfloat16)
    grad_groups = grad_attended.reshape(seqs, tokens, kv_dev, group_dev, HEAD_DIM)

    probs_back = jnp.exp(masked_scores() - log_sums)
    grad_probs = contract("stkgd,sjkd->skgtj", grad_groups, values_all)
    delta = jnp.sum(probs_back * grad_probs, axis=-1, keepdims=True)
    grad_scores = (probs_back * (grad_probs - delta)).astype(jnp.bfloat16)
    grad_qgroups = contract("skgtj,sjkd->stkgd", grad_scores, keys_all) * score_scale
    grad_kheads = contract("skgtj,stkgd->sjkd", grad_scores, query_groups) * score_scale
    grad_vheads = contract("skgtj,stkgd->sjkd", probs_back.astype(jnp.bfloat16), grad_groups)

    def kv_reduce(grads):
        summed = lax.psum_scatter(
            grads.reshape(seqs, -1, kv_dev * HEAD_DIM).astype(jnp.bfloat16),
            "ctx",
            scatter_dimension=1,
            tiled=True,
        ).astype(jnp.float32)
        total = summed
        for step in range(1, share):
            pairs = [
                (i, (i // share) * share + (i % share + step) % share) for i in range(fsdp_size)
            ]
            total = total + lax.ppermute(summed, "fsdp", pairs)
        return total

    grad_key_rot = kv_reduce(grad_kheads)
    grad_value = kv_reduce(grad_vheads)
    grad_query_rot = grad_qgroups.reshape(seqs, tokens, heads_dev, HEAD_DIM)
    grad_query, query_gain_grad = norm_back(
        rotate_back(grad_query_rot, cosine, sine_table), query_normed, query_scale, query_gain
    )
    grad_key, key_gain_grad = norm_back(
        rotate_back(grad_key_rot.reshape(seqs, tokens, kv_dev, HEAD_DIM), cosine, sine_table),
        key_normed,
        key_scale,
        key_gain,
    )
    if share > 1:
        key_gain_grad = key_gain_grad * (fsdp_index % share == 0).astype(jnp.float32)
    grad_query = grad_query.reshape(group_rows, heads_dev * HEAD_DIM).astype(jnp.bfloat16)
    grad_key = grad_key.reshape(group_rows, kv_dev * HEAD_DIM).astype(jnp.bfloat16)
    grad_value = grad_value.reshape(group_rows, kv_dev * HEAD_DIM).astype(jnp.bfloat16)

    def gather_heads(grads):
        whole = lax.all_gather(grads, "fsdp", axis=1, tiled=True)
        if share > 1:
            whole = whole.reshape(group_rows, KV_HEADS, share, HEAD_DIM)[:, :, 0]
            whole = whole.reshape(group_rows, KV_HEADS * HEAD_DIM)
        return whole

    query_all = lax.all_gather(grad_query, "fsdp", axis=1, tiled=True)
    key_all = gather_heads(grad_key)
    value_all = gather_heads(grad_value)
    input_part = lax.dynamic_slice_in_dim(group_input, fsdp_index * d_part, d_part, 1)
    query_grad_part = contract("td,tq->dq", input_part, query_all)
    key_grad_part = contract("td,tq->dq", input_part, key_all)
    value_grad_part = contract("td,tq->dq", input_part, value_all)
    grad_first_cols = (
        contract("tq,dq->td", query_all, query_proj)
        + contract("tq,dq->td", key_all, key_proj)
        + contract("tq,dq->td", value_all, value_proj)
    )
    grad_first = lax.all_to_all(
        grad_first_cols.reshape(seqs, tokens, d_part), "fsdp", 0, 2, tiled=True
    )[0]
    grad_hidden, attn_gain_grad = norm_back(grad_first, first_normed, first_scale, attn_gain)
    grad_hidden = grad_hidden + grad_middle
    gate_grad, up_grad, down_grad = (
        lax.psum_scatter(
            gate_grad_full.astype(jnp.bfloat16), "fsdp", scatter_dimension=1, tiled=True
        ).astype(jnp.float32),
        lax.psum_scatter(
            up_grad_full.astype(jnp.bfloat16), "fsdp", scatter_dimension=1, tiled=True
        ).astype(jnp.float32),
        lax.psum_scatter(
            down_grad_full.astype(jnp.bfloat16), "fsdp", scatter_dimension=1, tiled=True
        ).astype(jnp.float32),
    )
    router_shard = lax.psum_scatter(
        router_grad_full.astype(jnp.bfloat16), "fsdp", scatter_dimension=0, tiled=True
    ).astype(jnp.float32)
    query_grad, key_grad, value_grad, out_grad, router_grad = (
        lax.psum(query_grad_part.astype(jnp.bfloat16), "ctx").astype(jnp.float32),
        lax.psum(key_grad_part.astype(jnp.bfloat16), "ctx").astype(jnp.float32),
        lax.psum(value_grad_part.astype(jnp.bfloat16), "ctx").astype(jnp.float32),
        lax.psum(out_grad_part.astype(jnp.bfloat16), "ctx").astype(jnp.float32),
        lax.psum(router_shard.astype(jnp.bfloat16), "ctx").astype(jnp.float32),
    )
    attn_gain_total, query_gain_total, key_gain_total, ffn_gain_total = lax.psum(
        (attn_gain_grad, query_gain_grad, key_gain_grad, ffn_gain_grad), ("ctx", "fsdp")
    )
    return (
        layer_out[None],
        grad_hidden[None],
        attn_gain_total,
        query_grad,
        key_grad,
        value_grad,
        query_gain_total,
        key_gain_total,
        out_grad,
        ffn_gain_total,
        router_grad,
        gate_grad,
        up_grad,
        down_grad,
    )


def solution(mesh):
    placed = (
        P("fsdp", "ctx", None),
        P(),
        P("fsdp", None),
        P("fsdp", "ctx", None),
        P(),
        P("fsdp", None),
        P("fsdp", None),
        P("fsdp", None),
        P(),
        P(),
        P("fsdp", None),
        P(),
        P("fsdp", None),
        P("ctx", "fsdp", None),
        P("ctx", "fsdp", None),
        P("ctx", "fsdp", None),
        P("fsdp", "ctx", None),
    )
    return jax.shard_map(
        per_device,
        mesh=mesh,
        in_specs=placed,
        out_specs=(
            P("fsdp", "ctx", None),
            P("fsdp", "ctx", None),
            P(),
            P("fsdp", None),
            P("fsdp", None),
            P("fsdp", None),
            P(),
            P(),
            P("fsdp", None),
            P(),
            P("fsdp", None),
            P("ctx", "fsdp", None),
            P("ctx", "fsdp", None),
            P("ctx", "fsdp", None),
        ),
        check_vma=False,
    )
```

```python
import jax
import jax.numpy as jnp
from jax import lax
from jax.sharding import PartitionSpec as P

D = 2048
HEADS = 32
KV_HEADS = 4
HEAD_DIM = 128
TOP = 8


EPSILON = 1e-06
ROPE_BASE = 1000000.0
NEG_FILL = -1e30


def matmul(left, right):
    return jnp.dot(left, right, preferred_element_type=jnp.float32)


def contract(form, left, right):
    return jnp.einsum(form, left, right, preferred_element_type=jnp.float32)


def rms_scale(field):
    return lax.rsqrt(jnp.mean(field * field, axis=-1, keepdims=True) + EPSILON)


def rotary(positions):
    halfway = HEAD_DIM // 2
    inverse = ROPE_BASE ** (-2.0 * jnp.arange(halfway, dtype=jnp.float32) / HEAD_DIM)
    angle = positions.astype(jnp.float32)[:, None] * inverse[None, :]
    return (jnp.cos(angle), jnp.sin(angle))


def rotate(field, cosine, sine_table):
    halfway = field.shape[-1] // 2
    former = field[..., :halfway]
    latter = field[..., halfway:]
    cos_b = cosine[:, None, :]
    sin_b = sine_table[:, None, :]
    return jnp.concatenate(
        [former * cos_b - latter * sin_b, latter * cos_b + former * sin_b], axis=-1
    )


def rotate_back(field, cosine, sine_table):
    halfway = field.shape[-1] // 2
    former = field[..., :halfway]
    latter = field[..., halfway:]
    cos_b = cosine[:, None, :]
    sin_b = sine_table[:, None, :]
    return jnp.concatenate(
        [former * cos_b + latter * sin_b, latter * cos_b - former * sin_b], axis=-1
    )


def norm_back(grad, normed, inv_scale, factor):
    lead_axes = tuple(range(grad.ndim - 1))
    factor_grad = jnp.sum(grad * normed, axis=lead_axes)
    scaled = grad * factor
    return (
        inv_scale * (scaled - normed * jnp.mean(scaled * normed, axis=-1, keepdims=True)),
        factor_grad,
    )


def gather_a2a(x, axis_name, size, axis):
    rep = jnp.broadcast_to(x[None], (size,) + x.shape)
    got = jnp.moveaxis(lax.all_to_all(rep, axis_name, 0, 0, tiled=True), 0, axis)
    return got.reshape(x.shape[:axis] + (size * x.shape[axis],) + x.shape[axis + 1 :])


def scatter_sum_a2a(x, axis_name, size, axis):
    parts = x.reshape(x.shape[:axis] + (size, x.shape[axis] // size) + x.shape[axis + 1 :])
    got = lax.all_to_all(parts, axis_name, axis, axis, tiled=True)
    return jnp.sum(got.astype(jnp.float32), axis=axis)


def per_device(
    hidden_in,
    block_map,
    doc_ids,
    routes,
    attn_gain,
    query_proj,
    key_proj,
    value_proj,
    query_gain,
    key_gain,
    out_proj,
    ffn_gain,
    router_proj,
    expert_gate,
    expert_up,
    expert_down,
    cotangent,
):
    tokens = hidden_in.shape[1]
    ctx_size = lax.axis_size("ctx")
    fsdp_size = lax.axis_size("fsdp")
    fsdp_index = lax.axis_index("fsdp")
    local_experts = expert_gate.shape[0]
    experts = local_experts * ctx_size
    capacity = min(tokens, 3 * tokens * TOP // (2 * experts))
    block_len = tokens // 2
    group_size = HEADS // KV_HEADS
    score_scale = HEAD_DIM ** (-0.5)
    heads_dev = HEADS // fsdp_size
    share = max(1, fsdp_size // KV_HEADS)
    kv_dev = max(1, heads_dev // group_size)
    group_dev = heads_dev // kv_dev
    d_part = D // fsdp_size
    seqs = fsdp_size
    group_rows = seqs * tokens

    ctx_index = lax.axis_index("ctx")
    own_blocks = lax.dynamic_slice_in_dim(block_map, 2 * ctx_index, 2, 0)
    offsets = jnp.arange(block_len, dtype=jnp.int32)
    local_pos = (own_blocks[:, None] * block_len + offsets[None, :]).reshape(-1)
    all_pos = (block_map[:, None] * block_len + offsets[None, :]).reshape(-1)
    doc_rows = gather_a2a(doc_ids.astype(jnp.float32), "fsdp", fsdp_size, 0)
    docs_query = jnp.take(doc_rows, local_pos, axis=1)
    docs_key = jnp.take(doc_rows, all_pos, axis=1)
    visible = (all_pos[None, None, :] <= local_pos[None, :, None]) & (
        docs_key[:, None, :] == docs_query[:, :, None]
    )
    cosine, sine_table = rotary(local_pos)
    hidden = hidden_in[0]
    first_scale = rms_scale(hidden)
    first_normed = hidden * first_scale
    first_input = (first_normed * attn_gain).astype(jnp.bfloat16)
    group_input = lax.all_gather(first_input, "fsdp", axis=0, tiled=True)
    w_query_cols = lax.all_to_all(query_proj, "fsdp", 1, 0, tiled=True)
    if share == 1:
        w_key_cols = lax.all_to_all(key_proj, "fsdp", 1, 0, tiled=True)
        w_value_cols = lax.all_to_all(value_proj, "fsdp", 1, 0, tiled=True)
    else:
        kv_start = (fsdp_index // share) * HEAD_DIM
        w_key_cols = lax.dynamic_slice_in_dim(
            lax.all_gather(key_proj, "fsdp", axis=0, tiled=True), kv_start, HEAD_DIM, 1
        )
        w_value_cols = lax.dynamic_slice_in_dim(
            lax.all_gather(value_proj, "fsdp", axis=0, tiled=True), kv_start, HEAD_DIM, 1
        )
    query_raw = matmul(group_input, w_query_cols).reshape(seqs, tokens, heads_dev, HEAD_DIM)
    key_raw = matmul(group_input, w_key_cols).reshape(seqs, tokens, kv_dev, HEAD_DIM)
    value_low = (
        matmul(group_input, w_value_cols)
        .astype(jnp.bfloat16)
        .reshape(seqs, tokens, kv_dev * HEAD_DIM)
    )
    query_scale = rms_scale(query_raw)
    query_normed = query_raw * query_scale
    query_rot = rotate(query_normed * query_gain, cosine, sine_table).astype(jnp.bfloat16)
    key_scale = rms_scale(key_raw)
    key_normed = key_raw * key_scale
    key_rot = (
        rotate(key_normed * key_gain, cosine, sine_table)
        .reshape(seqs, tokens, kv_dev * HEAD_DIM)
        .astype(jnp.bfloat16)
    )
    keys_all = gather_a2a(key_rot, "ctx", ctx_size, 1).reshape(seqs, -1, kv_dev, HEAD_DIM)
    values_all = gather_a2a(value_low, "ctx", ctx_size, 1).reshape(seqs, -1, kv_dev, HEAD_DIM)
    query_groups = query_rot.reshape(seqs, tokens, kv_dev, group_dev, HEAD_DIM)

    def masked_scores():
        scores = contract("stkgd,sjkd->skgtj", query_groups, keys_all) * score_scale
        return jnp.where(visible[:, None, None], scores, NEG_FILL)

    scores = masked_scores()
    peak = jnp.max(scores, axis=-1, keepdims=True)
    expo = jnp.exp(scores - peak)
    total = jnp.sum(expo, axis=-1, keepdims=True)
    probs = (expo / total).astype(jnp.bfloat16)
    log_sums = peak + jnp.log(total)
    attended = (
        contract("skgtj,sjkd->stkgd", probs, values_all)
        .astype(jnp.bfloat16)
        .reshape(group_rows, heads_dev * HEAD_DIM)
    )
    branch_parts = matmul(attended, out_proj).reshape(seqs, tokens, D)
    branch = lax.psum_scatter(branch_parts, "fsdp", scatter_dimension=0, tiled=True)[0]
    middle = hidden + branch
    second_scale = rms_scale(middle)
    second_normed = middle * second_scale
    second_input = (second_normed * ffn_gain).astype(jnp.bfloat16)
    w_gate, w_up, w_down, w_router = (
        lax.all_gather(expert_gate, "fsdp", axis=1, tiled=True),
        lax.all_gather(expert_up, "fsdp", axis=1, tiled=True),
        lax.all_gather(expert_down, "fsdp", axis=1, tiled=True),
        gather_a2a(router_proj, "fsdp", fsdp_size, 0),
    )
    logits = matmul(second_input, w_router)
    route_ids = routes[0]
    chosen = jnp.take_along_axis(logits, route_ids, axis=1)
    route_weights = jax.nn.softmax(chosen, axis=-1)
    flat_ids = route_ids.reshape(-1)
    expert_range = jnp.arange(experts, dtype=jnp.int32)
    one_hot = (flat_ids[:, None] == expert_range[None, :]).astype(jnp.int32)
    earlier = jnp.cumsum(one_hot, axis=0) - one_hot
    slot_index = jnp.sum(earlier * one_hot, axis=1)
    target = flat_ids * capacity + slot_index

    def dispatch(route_rows):
        buffer = jnp.zeros((experts * capacity, D), jnp.bfloat16).at[target].set(route_rows)
        return buffer.reshape(ctx_size, local_experts, capacity, D)

    def collect(returned):
        return jnp.take(returned.reshape(experts * capacity, D), target, axis=0)

    received = lax.all_to_all(
        dispatch(jnp.repeat(second_input, TOP, axis=0)),
        "ctx",
        split_axis=0,
        concat_axis=2,
        tiled=True,
    )[0]
    gate_val = contract("erd,edf->erf", received, w_gate)
    up_val = contract("erd,edf->erf", received, w_up)
    gate_sig = jax.nn.sigmoid(gate_val)
    hid_low = (gate_val * gate_sig * up_val).astype(jnp.bfloat16)
    expert_out = contract("erf,efd->erd", hid_low, w_down).astype(jnp.bfloat16)
    route_out = (
        collect(lax.all_to_all(expert_out[None], "ctx", split_axis=2, concat_axis=0, tiled=True))
        .reshape(tokens, TOP, D)
        .astype(jnp.float32)
    )
    layer_out = middle + jnp.einsum("tr,trd->td", route_weights, route_out)
    grad_out = cotangent[0]
    grad_weights = jnp.einsum("td,trd->tr", grad_out, route_out)
    grad_routes = (
        (route_weights[:, :, None] * grad_out[:, None, :])
        .astype(jnp.bfloat16)
        .reshape(tokens * TOP, D)
    )
    grad_expert = lax.all_to_all(
        dispatch(grad_routes), "ctx", split_axis=0, concat_axis=2, tiled=True
    )[0]
    grad_hid = contract("erd,efd->erf", grad_expert, w_down)
    down_grad_full = contract("erf,erd->efd", hid_low, grad_expert)
    grad_gate = (grad_hid * up_val * gate_sig * (1.0 + gate_val * (1.0 - gate_sig))).astype(
        jnp.bfloat16
    )
    grad_up = (grad_hid * gate_val * gate_sig).astype(jnp.bfloat16)
    gate_grad_full = contract("erd,erf->edf", received, grad_gate)
    up_grad_full = contract("erd,erf->edf", received, grad_up)
    grad_rows = (
        contract("erf,edf->erd", grad_gate, w_gate) + contract("erf,edf->erd", grad_up, w_up)
    ).astype(jnp.bfloat16)
    grad_copies = collect(
        lax.all_to_all(grad_rows[None], "ctx", split_axis=2, concat_axis=0, tiled=True)
    ).reshape(tokens, TOP, D)
    grad_chosen = route_weights * (
        grad_weights - jnp.sum(route_weights * grad_weights, axis=-1, keepdims=True)
    )
    route_hot = (route_ids[:, :, None] == expert_range[None, None, :]).astype(jnp.float32)
    grad_logits = jnp.einsum("tr,tre->te", grad_chosen, route_hot).astype(jnp.bfloat16)
    router_grad_full = contract("td,te->de", second_input, grad_logits)
    grad_second = jnp.sum(grad_copies.astype(jnp.float32), axis=1) + contract(
        "te,de->td", grad_logits, w_router
    )
    grad_middle, ffn_gain_grad = norm_back(grad_second, second_normed, second_scale, ffn_gain)
    grad_middle = grad_middle + grad_out

    grad_branch = lax.all_gather(grad_middle.astype(jnp.bfloat16), "fsdp", axis=0, tiled=True)
    out_grad_part = contract("tq,td->qd", attended, grad_branch)
    grad_attended = contract("td,qd->tq", grad_branch, out_proj).astype(jnp.bfloat16)
    grad_groups = grad_attended.reshape(seqs, tokens, kv_dev, group_dev, HEAD_DIM)

    probs_back = jnp.exp(masked_scores() - log_sums)
    grad_probs = contract("stkgd,sjkd->skgtj", grad_groups, values_all)
    delta = jnp.sum(probs_back * grad_probs, axis=-1, keepdims=True)
    grad_scores = (probs_back * (grad_probs - delta)).astype(jnp.bfloat16)
    grad_qgroups = contract("skgtj,sjkd->stkgd", grad_scores, keys_all) * score_scale
    grad_kheads = contract("skgtj,stkgd->sjkd", grad_scores, query_groups) * score_scale
    grad_vheads = contract("skgtj,stkgd->sjkd", probs_back.astype(jnp.bfloat16), grad_groups)

    def kv_reduce(grads):
        summed = scatter_sum_a2a(
            grads.reshape(seqs, -1, kv_dev * HEAD_DIM).astype(jnp.bfloat16), "ctx", ctx_size, 1
        )
        total = summed
        for step in range(1, share):
            pairs = [
                (i, (i // share) * share + (i % share + step) % share) for i in range(fsdp_size)
            ]
            total = total + lax.ppermute(summed, "fsdp", pairs)
        return total

    grad_key_rot = kv_reduce(grad_kheads)
    grad_value = kv_reduce(grad_vheads)
    grad_query_rot = grad_qgroups.reshape(seqs, tokens, heads_dev, HEAD_DIM)
    grad_query, query_gain_grad = norm_back(
        rotate_back(grad_query_rot, cosine, sine_table), query_normed, query_scale, query_gain
    )
    grad_key, key_gain_grad = norm_back(
        rotate_back(grad_key_rot.reshape(seqs, tokens, kv_dev, HEAD_DIM), cosine, sine_table),
        key_normed,
        key_scale,
        key_gain,
    )
    if share > 1:
        key_gain_grad = key_gain_grad * (fsdp_index % share == 0).astype(jnp.float32)
    grad_query = grad_query.reshape(group_rows, heads_dev * HEAD_DIM).astype(jnp.bfloat16)
    grad_key = grad_key.reshape(group_rows, kv_dev * HEAD_DIM).astype(jnp.bfloat16)
    grad_value = grad_value.reshape(group_rows, kv_dev * HEAD_DIM).astype(jnp.bfloat16)

    def gather_heads(parts):
        whole = parts.reshape(group_rows, -1)
        if share > 1:
            whole = whole.reshape(group_rows, KV_HEADS, share, HEAD_DIM)[:, :, 0]
            whole = whole.reshape(group_rows, KV_HEADS * HEAD_DIM)
        return whole

    q_width, kv_width = heads_dev * HEAD_DIM, kv_dev * HEAD_DIM
    joined = lax.all_gather(
        jnp.concatenate([grad_query, grad_key, grad_value], axis=1), "fsdp", axis=1, tiled=False
    )
    query_all = joined[:, :, :q_width].reshape(group_rows, -1)
    key_all = gather_heads(joined[:, :, q_width : q_width + kv_width])
    value_all = gather_heads(joined[:, :, q_width + kv_width :])
    input_part = lax.dynamic_slice_in_dim(group_input, fsdp_index * d_part, d_part, 1)
    query_grad_part = contract("td,tq->dq", input_part, query_all)
    key_grad_part = contract("td,tq->dq", input_part, key_all)
    value_grad_part = contract("td,tq->dq", input_part, value_all)
    grad_first_cols = (
        contract("tq,dq->td", query_all, query_proj)
        + contract("tq,dq->td", key_all, key_proj)
        + contract("tq,dq->td", value_all, value_proj)
    )
    grad_first = lax.all_to_all(
        grad_first_cols.reshape(seqs, tokens, d_part), "fsdp", 0, 2, tiled=True
    )[0]
    grad_hidden, attn_gain_grad = norm_back(grad_first, first_normed, first_scale, attn_gain)
    grad_hidden = grad_hidden + grad_middle
    gate_grad, up_grad, down_grad = (
        lax.psum_scatter(
            gate_grad_full.astype(jnp.bfloat16), "fsdp", scatter_dimension=1, tiled=True
        ).astype(jnp.float32),
        lax.psum_scatter(
            up_grad_full.astype(jnp.bfloat16), "fsdp", scatter_dimension=1, tiled=True
        ).astype(jnp.float32),
        lax.psum_scatter(
            down_grad_full.astype(jnp.bfloat16), "fsdp", scatter_dimension=1, tiled=True
        ).astype(jnp.float32),
    )
    query_grad, key_grad, value_grad, out_grad = (
        lax.psum(query_grad_part.astype(jnp.bfloat16), "ctx").astype(jnp.float32),
        lax.psum(key_grad_part.astype(jnp.bfloat16), "ctx").astype(jnp.float32),
        lax.psum(value_grad_part.astype(jnp.bfloat16), "ctx").astype(jnp.float32),
        lax.psum(out_grad_part.astype(jnp.bfloat16), "ctx").astype(jnp.float32),
    )
    attn_gain_total, query_gain_total, key_gain_total, ffn_gain_total, router_total = lax.psum(
        (attn_gain_grad, query_gain_grad, key_gain_grad, ffn_gain_grad, router_grad_full),
        ("ctx", "fsdp"),
    )
    router_grad = lax.dynamic_slice_in_dim(router_total, fsdp_index * d_part, d_part, 0)
    return (
        layer_out[None],
        grad_hidden[None],
        attn_gain_total,
        query_grad,
        key_grad,
        value_grad,
        query_gain_total,
        key_gain_total,
        out_grad,
        ffn_gain_total,
        router_grad,
        gate_grad,
        up_grad,
        down_grad,
    )


def solution(mesh):
    placed = (
        P("fsdp", "ctx", None),
        P(),
        P("fsdp", None),
        P("fsdp", "ctx", None),
        P(),
        P("fsdp", None),
        P("fsdp", None),
        P("fsdp", None),
        P(),
        P(),
        P("fsdp", None),
        P(),
        P("fsdp", None),
        P("ctx", "fsdp", None),
        P("ctx", "fsdp", None),
        P("ctx", "fsdp", None),
        P("fsdp", "ctx", None),
    )
    return jax.shard_map(
        per_device,
        mesh=mesh,
        in_specs=placed,
        out_specs=(
            P("fsdp", "ctx", None),
            P("fsdp", "ctx", None),
            P(),
            P("fsdp", None),
            P("fsdp", None),
            P("fsdp", None),
            P(),
            P(),
            P("fsdp", None),
            P(),
            P("fsdp", None),
            P("ctx", "fsdp", None),
            P("ctx", "fsdp", None),
            P("ctx", "fsdp", None),
        ),
        check_vma=False,
    )
```

```python
import jax
import jax.numpy as jnp
from jax import lax
from jax.sharding import PartitionSpec as P

D = 2048
HEADS = 32
KV_HEADS = 4
HEAD_DIM = 128
TOP = 8


EPSILON = 1e-06
ROPE_BASE = 1000000.0
NEG_FILL = -1e30


def matmul(left, right):
    return jnp.dot(left, right, preferred_element_type=jnp.float32)


def contract(form, left, right):
    return jnp.einsum(form, left, right, preferred_element_type=jnp.float32)


def rms_scale(field):
    return lax.rsqrt(jnp.mean(field * field, axis=-1, keepdims=True) + EPSILON)


def rotary(positions):
    halfway = HEAD_DIM // 2
    inverse = ROPE_BASE ** (-2.0 * jnp.arange(halfway, dtype=jnp.float32) / HEAD_DIM)
    angle = positions.astype(jnp.float32)[:, None] * inverse[None, :]
    return (jnp.cos(angle), jnp.sin(angle))


def rotate(field, cosine, sine_table):
    halfway = field.shape[-1] // 2
    former = field[..., :halfway]
    latter = field[..., halfway:]
    cos_b = cosine[:, None, :]
    sin_b = sine_table[:, None, :]
    return jnp.concatenate(
        [former * cos_b - latter * sin_b, latter * cos_b + former * sin_b], axis=-1
    )


def rotate_back(field, cosine, sine_table):
    halfway = field.shape[-1] // 2
    former = field[..., :halfway]
    latter = field[..., halfway:]
    cos_b = cosine[:, None, :]
    sin_b = sine_table[:, None, :]
    return jnp.concatenate(
        [former * cos_b + latter * sin_b, latter * cos_b - former * sin_b], axis=-1
    )


def norm_back(grad, normed, inv_scale, factor):
    lead_axes = tuple(range(grad.ndim - 1))
    factor_grad = jnp.sum(grad * normed, axis=lead_axes)
    scaled = grad * factor
    return (
        inv_scale * (scaled - normed * jnp.mean(scaled * normed, axis=-1, keepdims=True)),
        factor_grad,
    )


def gather_a2a(x, axis_name, size, axis):
    rep = jnp.broadcast_to(x[None], (size,) + x.shape)
    got = jnp.moveaxis(lax.all_to_all(rep, axis_name, 0, 0, tiled=True), 0, axis)
    return got.reshape(x.shape[:axis] + (size * x.shape[axis],) + x.shape[axis + 1 :])


def scatter_sum_a2a(x, axis_name, size, axis):
    parts = x.reshape(x.shape[:axis] + (size, x.shape[axis] // size) + x.shape[axis + 1 :])
    got = lax.all_to_all(parts, axis_name, axis, axis, tiled=True)
    return jnp.sum(got.astype(jnp.float32), axis=axis)


def per_device(
    hidden_in,
    block_map,
    doc_ids,
    routes,
    attn_gain,
    query_proj,
    key_proj,
    value_proj,
    query_gain,
    key_gain,
    out_proj,
    ffn_gain,
    router_proj,
    expert_gate,
    expert_up,
    expert_down,
    cotangent,
):
    tokens = hidden_in.shape[1]
    ctx_size = lax.axis_size("ctx")
    fsdp_size = lax.axis_size("fsdp")
    fsdp_index = lax.axis_index("fsdp")
    local_experts = expert_gate.shape[0]
    experts = local_experts * ctx_size
    capacity = min(tokens, 3 * tokens * TOP // (2 * experts))
    block_len = tokens // 2
    group_size = HEADS // KV_HEADS
    score_scale = HEAD_DIM ** (-0.5)
    heads_dev = HEADS // fsdp_size
    share = max(1, fsdp_size // KV_HEADS)
    kv_dev = max(1, heads_dev // group_size)
    group_dev = heads_dev // kv_dev
    d_part = D // fsdp_size
    seqs = fsdp_size
    group_rows = seqs * tokens

    ctx_index = lax.axis_index("ctx")
    own_blocks = lax.dynamic_slice_in_dim(block_map, 2 * ctx_index, 2, 0)
    offsets = jnp.arange(block_len, dtype=jnp.int32)
    local_pos = (own_blocks[:, None] * block_len + offsets[None, :]).reshape(-1)
    all_pos = (block_map[:, None] * block_len + offsets[None, :]).reshape(-1)
    doc_rows = gather_a2a(doc_ids.astype(jnp.float32), "fsdp", fsdp_size, 0)
    docs_query = jnp.take(doc_rows, local_pos, axis=1)
    docs_key = jnp.take(doc_rows, all_pos, axis=1)
    visible = (all_pos[None, None, :] <= local_pos[None, :, None]) & (
        docs_key[:, None, :] == docs_query[:, :, None]
    )
    cosine, sine_table = rotary(local_pos)
    hidden = hidden_in[0]
    first_scale = rms_scale(hidden)
    first_normed = hidden * first_scale
    first_input = (first_normed * attn_gain).astype(jnp.bfloat16)
    group_input = gather_a2a(first_input, "fsdp", fsdp_size, 0)
    w_query_cols = lax.all_to_all(query_proj, "fsdp", 1, 0, tiled=True)
    if share == 1:
        w_key_cols = lax.all_to_all(key_proj, "fsdp", 1, 0, tiled=True)
        w_value_cols = lax.all_to_all(value_proj, "fsdp", 1, 0, tiled=True)
    else:
        kv_start = (fsdp_index // share) * HEAD_DIM
        w_key_cols = lax.dynamic_slice_in_dim(
            lax.all_gather(key_proj, "fsdp", axis=0, tiled=True), kv_start, HEAD_DIM, 1
        )
        w_value_cols = lax.dynamic_slice_in_dim(
            lax.all_gather(value_proj, "fsdp", axis=0, tiled=True), kv_start, HEAD_DIM, 1
        )
    query_raw = matmul(group_input, w_query_cols).reshape(seqs, tokens, heads_dev, HEAD_DIM)
    key_raw = matmul(group_input, w_key_cols).reshape(seqs, tokens, kv_dev, HEAD_DIM)
    value_low = (
        matmul(group_input, w_value_cols)
        .astype(jnp.bfloat16)
        .reshape(seqs, tokens, kv_dev * HEAD_DIM)
    )
    query_scale = rms_scale(query_raw)
    query_normed = query_raw * query_scale
    query_rot = rotate(query_normed * query_gain, cosine, sine_table).astype(jnp.bfloat16)
    key_scale = rms_scale(key_raw)
    key_normed = key_raw * key_scale
    key_rot = (
        rotate(key_normed * key_gain, cosine, sine_table)
        .reshape(seqs, tokens, kv_dev * HEAD_DIM)
        .astype(jnp.bfloat16)
    )
    keys_all = gather_a2a(key_rot, "ctx", ctx_size, 1).reshape(seqs, -1, kv_dev, HEAD_DIM)
    values_all = gather_a2a(value_low, "ctx", ctx_size, 1).reshape(seqs, -1, kv_dev, HEAD_DIM)
    query_groups = query_rot.reshape(seqs, tokens, kv_dev, group_dev, HEAD_DIM)

    def masked_scores():
        scores = contract("stkgd,sjkd->skgtj", query_groups, keys_all) * score_scale
        return jnp.where(visible[:, None, None], scores, NEG_FILL)

    scores = masked_scores()
    peak = jnp.max(scores, axis=-1, keepdims=True)
    expo = jnp.exp(scores - peak)
    total = jnp.sum(expo, axis=-1, keepdims=True)
    probs = (expo / total).astype(jnp.bfloat16)
    log_sums = peak + jnp.log(total)
    attended = (
        contract("skgtj,sjkd->stkgd", probs, values_all)
        .astype(jnp.bfloat16)
        .reshape(group_rows, heads_dev * HEAD_DIM)
    )
    branch_parts = matmul(attended, out_proj).reshape(seqs, tokens, D)
    branch = scatter_sum_a2a(branch_parts, "fsdp", fsdp_size, 0)[0]
    middle = hidden + branch
    second_scale = rms_scale(middle)
    second_normed = middle * second_scale
    second_input = (second_normed * ffn_gain).astype(jnp.bfloat16)
    w_gate, w_up, w_down, w_router = (
        lax.all_gather(expert_gate, "fsdp", axis=1, tiled=True),
        lax.all_gather(expert_up, "fsdp", axis=1, tiled=True),
        lax.all_gather(expert_down, "fsdp", axis=1, tiled=True),
        gather_a2a(router_proj, "fsdp", fsdp_size, 0),
    )
    logits = matmul(second_input, w_router)
    route_ids = routes[0]
    chosen = jnp.take_along_axis(logits, route_ids, axis=1)
    route_weights = jax.nn.softmax(chosen, axis=-1)
    flat_ids = route_ids.reshape(-1)
    expert_range = jnp.arange(experts, dtype=jnp.int32)
    one_hot = (flat_ids[:, None] == expert_range[None, :]).astype(jnp.int32)
    earlier = jnp.cumsum(one_hot, axis=0) - one_hot
    slot_index = jnp.sum(earlier * one_hot, axis=1)
    target = flat_ids * capacity + slot_index

    def dispatch(route_rows):
        buffer = jnp.zeros((experts * capacity, D), jnp.bfloat16).at[target].set(route_rows)
        return buffer.reshape(ctx_size, local_experts, capacity, D)

    def collect(returned):
        return jnp.take(returned.reshape(experts * capacity, D), target, axis=0)

    received = lax.all_to_all(
        dispatch(jnp.repeat(second_input, TOP, axis=0)),
        "ctx",
        split_axis=0,
        concat_axis=2,
        tiled=True,
    )[0]
    gate_val = contract("erd,edf->erf", received, w_gate)
    up_val = contract("erd,edf->erf", received, w_up)
    gate_sig = jax.nn.sigmoid(gate_val)
    hid_low = (gate_val * gate_sig * up_val).astype(jnp.bfloat16)
    expert_out = contract("erf,efd->erd", hid_low, w_down).astype(jnp.bfloat16)
    route_out = (
        collect(lax.all_to_all(expert_out[None], "ctx", split_axis=2, concat_axis=0, tiled=True))
        .reshape(tokens, TOP, D)
        .astype(jnp.float32)
    )
    layer_out = middle + jnp.einsum("tr,trd->td", route_weights, route_out)
    grad_out = cotangent[0]
    grad_weights = jnp.einsum("td,trd->tr", grad_out, route_out)
    grad_routes = (
        (route_weights[:, :, None] * grad_out[:, None, :])
        .astype(jnp.bfloat16)
        .reshape(tokens * TOP, D)
    )
    grad_expert = lax.all_to_all(
        dispatch(grad_routes), "ctx", split_axis=0, concat_axis=2, tiled=True
    )[0]
    grad_hid = contract("erd,efd->erf", grad_expert, w_down)
    down_grad_full = contract("erf,erd->efd", hid_low, grad_expert)
    grad_gate = (grad_hid * up_val * gate_sig * (1.0 + gate_val * (1.0 - gate_sig))).astype(
        jnp.bfloat16
    )
    grad_up = (grad_hid * gate_val * gate_sig).astype(jnp.bfloat16)
    gate_grad_full = contract("erd,erf->edf", received, grad_gate)
    up_grad_full = contract("erd,erf->edf", received, grad_up)
    grad_rows = (
        contract("erf,edf->erd", grad_gate, w_gate) + contract("erf,edf->erd", grad_up, w_up)
    ).astype(jnp.bfloat16)
    grad_copies = collect(
        lax.all_to_all(grad_rows[None], "ctx", split_axis=2, concat_axis=0, tiled=True)
    ).reshape(tokens, TOP, D)
    grad_chosen = route_weights * (
        grad_weights - jnp.sum(route_weights * grad_weights, axis=-1, keepdims=True)
    )
    route_hot = (route_ids[:, :, None] == expert_range[None, None, :]).astype(jnp.float32)
    grad_logits = jnp.einsum("tr,tre->te", grad_chosen, route_hot).astype(jnp.bfloat16)
    router_grad_full = contract("td,te->de", second_input, grad_logits)
    grad_second = jnp.sum(grad_copies.astype(jnp.float32), axis=1) + contract(
        "te,de->td", grad_logits, w_router
    )
    grad_middle, ffn_gain_grad = norm_back(grad_second, second_normed, second_scale, ffn_gain)
    grad_middle = grad_middle + grad_out

    grad_branch = gather_a2a(grad_middle.astype(jnp.bfloat16), "fsdp", fsdp_size, 0)
    out_grad_part = contract("tq,td->qd", attended, grad_branch)
    grad_attended = contract("td,qd->tq", grad_branch, out_proj).astype(jnp.bfloat16)
    grad_groups = grad_attended.reshape(seqs, tokens, kv_dev, group_dev, HEAD_DIM)

    probs_back = jnp.exp(masked_scores() - log_sums)
    grad_probs = contract("stkgd,sjkd->skgtj", grad_groups, values_all)
    delta = jnp.sum(probs_back * grad_probs, axis=-1, keepdims=True)
    grad_scores = (probs_back * (grad_probs - delta)).astype(jnp.bfloat16)
    grad_qgroups = contract("skgtj,sjkd->stkgd", grad_scores, keys_all) * score_scale
    grad_kheads = contract("skgtj,stkgd->sjkd", grad_scores, query_groups) * score_scale
    grad_vheads = contract("skgtj,stkgd->sjkd", probs_back.astype(jnp.bfloat16), grad_groups)

    def kv_reduce(grads):
        summed = scatter_sum_a2a(
            grads.reshape(seqs, -1, kv_dev * HEAD_DIM).astype(jnp.bfloat16), "ctx", ctx_size, 1
        )
        total = summed
        for step in range(1, share):
            pairs = [
                (i, (i // share) * share + (i % share + step) % share) for i in range(fsdp_size)
            ]
            total = total + lax.ppermute(summed, "fsdp", pairs)
        return total

    grad_key_rot = kv_reduce(grad_kheads)
    grad_value = kv_reduce(grad_vheads)
    grad_query_rot = grad_qgroups.reshape(seqs, tokens, heads_dev, HEAD_DIM)
    grad_query, query_gain_grad = norm_back(
        rotate_back(grad_query_rot, cosine, sine_table), query_normed, query_scale, query_gain
    )
    grad_key, key_gain_grad = norm_back(
        rotate_back(grad_key_rot.reshape(seqs, tokens, kv_dev, HEAD_DIM), cosine, sine_table),
        key_normed,
        key_scale,
        key_gain,
    )
    if share > 1:
        key_gain_grad = key_gain_grad * (fsdp_index % share == 0).astype(jnp.float32)
    grad_query = grad_query.reshape(group_rows, heads_dev * HEAD_DIM).astype(jnp.bfloat16)
    grad_key = grad_key.reshape(group_rows, kv_dev * HEAD_DIM).astype(jnp.bfloat16)
    grad_value = grad_value.reshape(group_rows, kv_dev * HEAD_DIM).astype(jnp.bfloat16)

    def gather_heads(parts):
        whole = parts.reshape(group_rows, -1)
        if share > 1:
            whole = whole.reshape(group_rows, KV_HEADS, share, HEAD_DIM)[:, :, 0]
            whole = whole.reshape(group_rows, KV_HEADS * HEAD_DIM)
        return whole

    q_width, kv_width = heads_dev * HEAD_DIM, kv_dev * HEAD_DIM
    joined = gather_a2a(
        jnp.concatenate([grad_query, grad_key, grad_value], axis=1)[:, None], "fsdp", fsdp_size, 1
    )
    query_all = joined[:, :, :q_width].reshape(group_rows, -1)
    key_all = gather_heads(joined[:, :, q_width : q_width + kv_width])
    value_all = gather_heads(joined[:, :, q_width + kv_width :])
    input_part = lax.dynamic_slice_in_dim(group_input, fsdp_index * d_part, d_part, 1)
    query_grad_part = contract("td,tq->dq", input_part, query_all)
    key_grad_part = contract("td,tq->dq", input_part, key_all)
    value_grad_part = contract("td,tq->dq", input_part, value_all)
    grad_first_cols = (
        contract("tq,dq->td", query_all, query_proj)
        + contract("tq,dq->td", key_all, key_proj)
        + contract("tq,dq->td", value_all, value_proj)
    )
    grad_first = lax.all_to_all(
        grad_first_cols.reshape(seqs, tokens, d_part), "fsdp", 0, 2, tiled=True
    )[0]
    grad_hidden, attn_gain_grad = norm_back(grad_first, first_normed, first_scale, attn_gain)
    grad_hidden = grad_hidden + grad_middle
    gate_grad, up_grad, down_grad = (
        lax.psum_scatter(
            gate_grad_full.astype(jnp.bfloat16), "fsdp", scatter_dimension=1, tiled=True
        ).astype(jnp.float32),
        lax.psum_scatter(
            up_grad_full.astype(jnp.bfloat16), "fsdp", scatter_dimension=1, tiled=True
        ).astype(jnp.float32),
        lax.psum_scatter(
            down_grad_full.astype(jnp.bfloat16), "fsdp", scatter_dimension=1, tiled=True
        ).astype(jnp.float32),
    )
    router_shard = scatter_sum_a2a(router_grad_full, "fsdp", fsdp_size, 0)
    query_grad, key_grad, value_grad, out_grad, router_grad = (
        lax.psum(query_grad_part.astype(jnp.bfloat16), "ctx").astype(jnp.float32),
        lax.psum(key_grad_part.astype(jnp.bfloat16), "ctx").astype(jnp.float32),
        lax.psum(value_grad_part.astype(jnp.bfloat16), "ctx").astype(jnp.float32),
        lax.psum(out_grad_part.astype(jnp.bfloat16), "ctx").astype(jnp.float32),
        jnp.sum(gather_a2a(router_shard[None], "ctx", ctx_size, 0), axis=0),
    )
    attn_gain_total, query_gain_total, key_gain_total, ffn_gain_total = lax.psum(
        (attn_gain_grad, query_gain_grad, key_gain_grad, ffn_gain_grad), ("ctx", "fsdp")
    )
    return (
        layer_out[None],
        grad_hidden[None],
        attn_gain_total,
        query_grad,
        key_grad,
        value_grad,
        query_gain_total,
        key_gain_total,
        out_grad,
        ffn_gain_total,
        router_grad,
        gate_grad,
        up_grad,
        down_grad,
    )


def solution(mesh):
    placed = (
        P("fsdp", "ctx", None),
        P(),
        P("fsdp", None),
        P("fsdp", "ctx", None),
        P(),
        P("fsdp", None),
        P("fsdp", None),
        P("fsdp", None),
        P(),
        P(),
        P("fsdp", None),
        P(),
        P("fsdp", None),
        P("ctx", "fsdp", None),
        P("ctx", "fsdp", None),
        P("ctx", "fsdp", None),
        P("fsdp", "ctx", None),
    )
    return jax.shard_map(
        per_device,
        mesh=mesh,
        in_specs=placed,
        out_specs=(
            P("fsdp", "ctx", None),
            P("fsdp", "ctx", None),
            P(),
            P("fsdp", None),
            P("fsdp", None),
            P("fsdp", None),
            P(),
            P(),
            P("fsdp", None),
            P(),
            P("fsdp", None),
            P("ctx", "fsdp", None),
            P("ctx", "fsdp", None),
            P("ctx", "fsdp", None),
        ),
        check_vma=False,
    )
```

```python
import jax
import jax.numpy as jnp
from jax import lax
from jax.sharding import PartitionSpec as P

D = 2048
HEADS = 32
KV_HEADS = 4
HEAD_DIM = 128
TOP = 8


EPSILON = 1e-06
ROPE_BASE = 1000000.0
NEG_FILL = -1e30


def matmul(left, right):
    return jnp.dot(left, right, preferred_element_type=jnp.float32)


def contract(form, left, right):
    return jnp.einsum(form, left, right, preferred_element_type=jnp.float32)


def rms_scale(field):
    return lax.rsqrt(jnp.mean(field * field, axis=-1, keepdims=True) + EPSILON)


def rotary(positions):
    halfway = HEAD_DIM // 2
    inverse = ROPE_BASE ** (-2.0 * jnp.arange(halfway, dtype=jnp.float32) / HEAD_DIM)
    angle = positions.astype(jnp.float32)[:, None] * inverse[None, :]
    return (jnp.cos(angle), jnp.sin(angle))


def rotate(field, cosine, sine_table):
    halfway = field.shape[-1] // 2
    former = field[..., :halfway]
    latter = field[..., halfway:]
    cos_b = cosine[:, None, :]
    sin_b = sine_table[:, None, :]
    return jnp.concatenate(
        [former * cos_b - latter * sin_b, latter * cos_b + former * sin_b], axis=-1
    )


def rotate_back(field, cosine, sine_table):
    halfway = field.shape[-1] // 2
    former = field[..., :halfway]
    latter = field[..., halfway:]
    cos_b = cosine[:, None, :]
    sin_b = sine_table[:, None, :]
    return jnp.concatenate(
        [former * cos_b + latter * sin_b, latter * cos_b - former * sin_b], axis=-1
    )


def norm_back(grad, normed, inv_scale, factor):
    lead_axes = tuple(range(grad.ndim - 1))
    factor_grad = jnp.sum(grad * normed, axis=lead_axes)
    scaled = grad * factor
    return (
        inv_scale * (scaled - normed * jnp.mean(scaled * normed, axis=-1, keepdims=True)),
        factor_grad,
    )


def gather_a2a(x, axis_name, size, axis):
    rep = jnp.broadcast_to(x[None], (size,) + x.shape)
    got = jnp.moveaxis(lax.all_to_all(rep, axis_name, 0, 0, tiled=True), 0, axis)
    return got.reshape(x.shape[:axis] + (size * x.shape[axis],) + x.shape[axis + 1 :])


def scatter_sum_a2a(x, axis_name, size, axis):
    parts = x.reshape(x.shape[:axis] + (size, x.shape[axis] // size) + x.shape[axis + 1 :])
    got = lax.all_to_all(parts, axis_name, axis, axis, tiled=True)
    return jnp.sum(got.astype(jnp.float32), axis=axis)


def per_device(
    hidden_in,
    block_map,
    doc_ids,
    routes,
    attn_gain,
    query_proj,
    key_proj,
    value_proj,
    query_gain,
    key_gain,
    out_proj,
    ffn_gain,
    router_proj,
    expert_gate,
    expert_up,
    expert_down,
    cotangent,
):
    tokens = hidden_in.shape[1]
    ctx_size = lax.axis_size("ctx")
    fsdp_size = lax.axis_size("fsdp")
    fsdp_index = lax.axis_index("fsdp")
    local_experts = expert_gate.shape[0]
    experts = local_experts * ctx_size
    capacity = min(tokens, 3 * tokens * TOP // (2 * experts))
    block_len = tokens // 2
    group_size = HEADS // KV_HEADS
    score_scale = HEAD_DIM ** (-0.5)
    heads_dev = HEADS // fsdp_size
    share = max(1, fsdp_size // KV_HEADS)
    kv_dev = max(1, heads_dev // group_size)
    group_dev = heads_dev // kv_dev
    d_part = D // fsdp_size
    seqs = fsdp_size
    group_rows = seqs * tokens

    ctx_index = lax.axis_index("ctx")
    own_blocks = lax.dynamic_slice_in_dim(block_map, 2 * ctx_index, 2, 0)
    offsets = jnp.arange(block_len, dtype=jnp.int32)
    local_pos = (own_blocks[:, None] * block_len + offsets[None, :]).reshape(-1)
    all_pos = (block_map[:, None] * block_len + offsets[None, :]).reshape(-1)
    doc_rows = gather_a2a(doc_ids.astype(jnp.float32), "fsdp", fsdp_size, 0)
    docs_query = jnp.take(doc_rows, local_pos, axis=1)
    docs_key = jnp.take(doc_rows, all_pos, axis=1)
    visible = (all_pos[None, None, :] <= local_pos[None, :, None]) & (
        docs_key[:, None, :] == docs_query[:, :, None]
    )
    cosine, sine_table = rotary(local_pos)
    hidden = hidden_in[0]
    first_scale = rms_scale(hidden)
    first_normed = hidden * first_scale
    first_input = (first_normed * attn_gain).astype(jnp.bfloat16)
    group_input = gather_a2a(first_input, "fsdp", fsdp_size, 0)
    q_width, kv_width = heads_dev * HEAD_DIM, kv_dev * HEAD_DIM
    if share == 1:
        blocks = jnp.concatenate(
            [
                query_proj.reshape(d_part, fsdp_size, q_width),
                key_proj.reshape(d_part, fsdp_size, kv_width),
                value_proj.reshape(d_part, fsdp_size, kv_width),
            ],
            axis=2,
        )
        half = d_part // 2
        core = ctx_index % 2
        mine = lax.all_to_all(
            lax.dynamic_slice_in_dim(blocks, core * half, half, 0), "fsdp", 1, 0, tiled=True
        ).reshape(fsdp_size, half, -1)
        other = lax.ppermute(mine, "ctx", [(i, i ^ 1) for i in range(ctx_size)])
        w_cols = jnp.where(
            core == 0, jnp.stack([mine, other], axis=1), jnp.stack([other, mine], axis=1)
        ).reshape(D, -1)
    else:
        kv_start = (fsdp_index // share) * HEAD_DIM
        w_cols = jnp.concatenate(
            [
                lax.all_to_all(query_proj, "fsdp", 1, 0, tiled=True),
                lax.dynamic_slice_in_dim(
                    lax.all_gather(key_proj, "fsdp", axis=0, tiled=True), kv_start, HEAD_DIM, 1
                ),
                lax.dynamic_slice_in_dim(
                    lax.all_gather(value_proj, "fsdp", axis=0, tiled=True), kv_start, HEAD_DIM, 1
                ),
            ],
            axis=1,
        )
    w_cols, expert_gate, expert_up = lax.optimization_barrier((w_cols, expert_gate, expert_up))
    projected = matmul(group_input, w_cols)
    query_raw = projected[:, :q_width].reshape(seqs, tokens, heads_dev, HEAD_DIM)
    key_raw = projected[:, q_width : q_width + kv_width].reshape(seqs, tokens, kv_dev, HEAD_DIM)
    value_low = (
        projected[:, q_width + kv_width :]
        .astype(jnp.bfloat16)
        .reshape(seqs, tokens, kv_dev * HEAD_DIM)
    )
    query_scale = rms_scale(query_raw)
    query_normed = query_raw * query_scale
    query_rot = rotate(query_normed * query_gain, cosine, sine_table).astype(jnp.bfloat16)
    key_scale = rms_scale(key_raw)
    key_normed = key_raw * key_scale
    key_rot = (
        rotate(key_normed * key_gain, cosine, sine_table)
        .reshape(seqs, tokens, kv_dev * HEAD_DIM)
        .astype(jnp.bfloat16)
    )
    keys_all = gather_a2a(key_rot, "ctx", ctx_size, 1).reshape(seqs, -1, kv_dev, HEAD_DIM)
    values_all = gather_a2a(value_low, "ctx", ctx_size, 1).reshape(seqs, -1, kv_dev, HEAD_DIM)
    query_groups = query_rot.reshape(seqs, tokens, kv_dev, group_dev, HEAD_DIM)

    def masked_scores():
        scores = contract("stkgd,sjkd->skgtj", query_groups, keys_all) * score_scale
        return jnp.where(visible[:, None, None], scores, NEG_FILL)

    scores = masked_scores()
    peak = jnp.max(scores, axis=-1, keepdims=True)
    expo = jnp.exp(scores - peak)
    total = jnp.sum(expo, axis=-1, keepdims=True)
    probs = (expo / total).astype(jnp.bfloat16)
    log_sums = peak + jnp.log(total)
    attended = (
        contract("skgtj,sjkd->stkgd", probs, values_all)
        .astype(jnp.bfloat16)
        .reshape(group_rows, heads_dev * HEAD_DIM)
    )
    branch_parts = matmul(attended, out_proj).reshape(seqs, tokens, D)
    branch = scatter_sum_a2a(branch_parts.astype(jnp.bfloat16), "fsdp", fsdp_size, 0)[0]
    branch, expert_down = lax.optimization_barrier((branch, expert_down))
    middle = hidden + branch
    second_scale = rms_scale(middle)
    second_normed = middle * second_scale
    second_input = (second_normed * ffn_gain).astype(jnp.bfloat16)
    w_gate, w_up, w_down, w_router = (
        lax.all_gather(expert_gate, "fsdp", axis=1, tiled=True),
        lax.all_gather(expert_up, "fsdp", axis=1, tiled=True),
        lax.all_gather(expert_down, "fsdp", axis=1, tiled=True),
        gather_a2a(router_proj, "fsdp", fsdp_size, 0),
    )
    logits = matmul(second_input, w_router)
    route_ids = routes[0]
    chosen = jnp.take_along_axis(logits, route_ids, axis=1)
    route_weights = jax.nn.softmax(chosen, axis=-1)
    flat_ids = route_ids.reshape(-1)
    expert_range = jnp.arange(experts, dtype=jnp.int32)
    one_hot = (flat_ids[:, None] == expert_range[None, :]).astype(jnp.int32)
    earlier = jnp.cumsum(one_hot, axis=0) - one_hot
    slot_index = jnp.sum(earlier * one_hot, axis=1)
    target = flat_ids * capacity + slot_index

    def dispatch(route_rows):
        buffer = jnp.zeros((experts * capacity, D), jnp.bfloat16).at[target].set(route_rows)
        return buffer.reshape(ctx_size, local_experts, capacity, D)

    def collect(returned):
        return jnp.take(returned.reshape(experts * capacity, D), target, axis=0)

    received = lax.all_to_all(
        dispatch(jnp.repeat(second_input, TOP, axis=0)),
        "ctx",
        split_axis=0,
        concat_axis=2,
        tiled=True,
    )[0]
    gate_val = contract("erd,edf->erf", received, w_gate)
    up_val = contract("erd,edf->erf", received, w_up)
    gate_sig = jax.nn.sigmoid(gate_val)
    hid_low = (gate_val * gate_sig * up_val).astype(jnp.bfloat16)
    expert_out = contract("erf,efd->erd", hid_low, w_down).astype(jnp.bfloat16)
    route_out = (
        collect(lax.all_to_all(expert_out[None], "ctx", split_axis=2, concat_axis=0, tiled=True))
        .reshape(tokens, TOP, D)
        .astype(jnp.float32)
    )
    layer_out = middle + jnp.einsum("tr,trd->td", route_weights, route_out)
    grad_out = cotangent[0]
    grad_weights = jnp.einsum("td,trd->tr", grad_out, route_out)
    grad_routes = (
        (route_weights[:, :, None] * grad_out[:, None, :])
        .astype(jnp.bfloat16)
        .reshape(tokens * TOP, D)
    )
    grad_expert = lax.all_to_all(
        dispatch(grad_routes), "ctx", split_axis=0, concat_axis=2, tiled=True
    )[0]
    grad_hid = contract("erd,efd->erf", grad_expert, w_down)
    down_grad_full = contract("erf,erd->efd", hid_low, grad_expert)
    grad_gate = (grad_hid * up_val * gate_sig * (1.0 + gate_val * (1.0 - gate_sig))).astype(
        jnp.bfloat16
    )
    grad_up = (grad_hid * gate_val * gate_sig).astype(jnp.bfloat16)
    gate_grad_full = contract("erd,erf->edf", received, grad_gate)
    up_grad_full = contract("erd,erf->edf", received, grad_up)
    grad_rows = (
        contract("erf,edf->erd", grad_gate, w_gate) + contract("erf,edf->erd", grad_up, w_up)
    ).astype(jnp.bfloat16)
    grad_copies = collect(
        lax.all_to_all(grad_rows[None], "ctx", split_axis=2, concat_axis=0, tiled=True)
    ).reshape(tokens, TOP, D)
    grad_chosen = route_weights * (
        grad_weights - jnp.sum(route_weights * grad_weights, axis=-1, keepdims=True)
    )
    route_hot = (route_ids[:, :, None] == expert_range[None, None, :]).astype(jnp.float32)
    grad_logits = jnp.einsum("tr,tre->te", grad_chosen, route_hot).astype(jnp.bfloat16)
    router_grad_full = contract("td,te->de", second_input, grad_logits)
    grad_second = jnp.sum(grad_copies.astype(jnp.float32), axis=1) + contract(
        "te,de->td", grad_logits, w_router
    )
    grad_middle, ffn_gain_grad = norm_back(grad_second, second_normed, second_scale, ffn_gain)
    grad_middle = grad_middle + grad_out

    grad_branch = gather_a2a(grad_middle.astype(jnp.bfloat16), "fsdp", fsdp_size, 0)
    out_grad_part = contract("tq,td->qd", attended, grad_branch)
    grad_attended = contract("td,qd->tq", grad_branch, out_proj).astype(jnp.bfloat16)
    grad_groups = grad_attended.reshape(seqs, tokens, kv_dev, group_dev, HEAD_DIM)

    probs_back = jnp.exp(masked_scores() - log_sums)
    grad_probs = contract("stkgd,sjkd->skgtj", grad_groups, values_all)
    delta = jnp.sum(probs_back * grad_probs, axis=-1, keepdims=True)
    grad_scores = (probs_back * (grad_probs - delta)).astype(jnp.bfloat16)
    grad_qgroups = contract("skgtj,sjkd->stkgd", grad_scores, keys_all) * score_scale
    grad_kheads = contract("skgtj,stkgd->sjkd", grad_scores, query_groups) * score_scale
    grad_vheads = contract("skgtj,stkgd->sjkd", probs_back.astype(jnp.bfloat16), grad_groups)

    def kv_reduce(grads):
        summed = scatter_sum_a2a(
            grads.reshape(seqs, -1, kv_dev * HEAD_DIM).astype(jnp.bfloat16), "ctx", ctx_size, 1
        )
        total = summed
        for step in range(1, share):
            pairs = [
                (i, (i // share) * share + (i % share + step) % share) for i in range(fsdp_size)
            ]
            total = total + lax.ppermute(summed, "fsdp", pairs)
        return total

    grad_key_rot = kv_reduce(grad_kheads)
    grad_value = kv_reduce(grad_vheads)
    grad_query_rot = grad_qgroups.reshape(seqs, tokens, heads_dev, HEAD_DIM)
    grad_query, query_gain_grad = norm_back(
        rotate_back(grad_query_rot, cosine, sine_table), query_normed, query_scale, query_gain
    )
    grad_key, key_gain_grad = norm_back(
        rotate_back(grad_key_rot.reshape(seqs, tokens, kv_dev, HEAD_DIM), cosine, sine_table),
        key_normed,
        key_scale,
        key_gain,
    )
    if share > 1:
        key_gain_grad = key_gain_grad * (fsdp_index % share == 0).astype(jnp.float32)
    grad_query = grad_query.reshape(group_rows, heads_dev * HEAD_DIM).astype(jnp.bfloat16)
    grad_key = grad_key.reshape(group_rows, kv_dev * HEAD_DIM).astype(jnp.bfloat16)
    grad_value = grad_value.reshape(group_rows, kv_dev * HEAD_DIM).astype(jnp.bfloat16)

    def gather_heads(parts):
        whole = parts.reshape(group_rows, -1)
        if share > 1:
            whole = whole.reshape(group_rows, KV_HEADS, share, HEAD_DIM)[:, :, 0]
            whole = whole.reshape(group_rows, KV_HEADS * HEAD_DIM)
        return whole

    joined = gather_a2a(
        jnp.concatenate([grad_query, grad_key, grad_value], axis=1)[:, None], "fsdp", fsdp_size, 1
    )
    query_all = joined[:, :, :q_width].reshape(group_rows, -1)
    key_all = gather_heads(joined[:, :, q_width : q_width + kv_width])
    value_all = gather_heads(joined[:, :, q_width + kv_width :])
    input_part = lax.dynamic_slice_in_dim(group_input, fsdp_index * d_part, d_part, 1)
    query_grad_part = contract("td,tq->dq", input_part, query_all)
    key_grad_part = contract("td,tq->dq", input_part, key_all)
    value_grad_part = contract("td,tq->dq", input_part, value_all)
    grad_first_cols = (
        contract("tq,dq->td", query_all, query_proj)
        + contract("tq,dq->td", key_all, key_proj)
        + contract("tq,dq->td", value_all, value_proj)
    )
    grad_first = lax.all_to_all(
        grad_first_cols.reshape(seqs, tokens, d_part), "fsdp", 0, 2, tiled=True
    )[0]
    grad_hidden, attn_gain_grad = norm_back(grad_first, first_normed, first_scale, attn_gain)
    grad_hidden = grad_hidden + grad_middle
    gate_grad, up_grad, down_grad = (
        lax.psum_scatter(
            gate_grad_full.astype(jnp.bfloat16), "fsdp", scatter_dimension=1, tiled=True
        ).astype(jnp.float32),
        lax.psum_scatter(
            up_grad_full.astype(jnp.bfloat16), "fsdp", scatter_dimension=1, tiled=True
        ).astype(jnp.float32),
        lax.psum_scatter(
            down_grad_full.astype(jnp.bfloat16), "fsdp", scatter_dimension=1, tiled=True
        ).astype(jnp.float32),
    )
    router_shard = scatter_sum_a2a(router_grad_full, "fsdp", fsdp_size, 0)
    query_grad, key_grad, value_grad, out_grad, router_grad = (
        lax.psum(query_grad_part.astype(jnp.bfloat16), "ctx").astype(jnp.float32),
        lax.psum(key_grad_part.astype(jnp.bfloat16), "ctx").astype(jnp.float32),
        lax.psum(value_grad_part.astype(jnp.bfloat16), "ctx").astype(jnp.float32),
        lax.psum(out_grad_part.astype(jnp.bfloat16), "ctx").astype(jnp.float32),
        jnp.sum(gather_a2a(router_shard[None], "ctx", ctx_size, 0), axis=0),
    )
    attn_gain_total, query_gain_total, key_gain_total, ffn_gain_total = lax.psum(
        (attn_gain_grad, query_gain_grad, key_gain_grad, ffn_gain_grad), ("ctx", "fsdp")
    )
    return (
        layer_out[None],
        grad_hidden[None],
        attn_gain_total,
        query_grad,
        key_grad,
        value_grad,
        query_gain_total,
        key_gain_total,
        out_grad,
        ffn_gain_total,
        router_grad,
        gate_grad,
        up_grad,
        down_grad,
    )


def solution(mesh):
    placed = (
        P("fsdp", "ctx", None),
        P(),
        P("fsdp", None),
        P("fsdp", "ctx", None),
        P(),
        P("fsdp", None),
        P("fsdp", None),
        P("fsdp", None),
        P(),
        P(),
        P("fsdp", None),
        P(),
        P("fsdp", None),
        P("ctx", "fsdp", None),
        P("ctx", "fsdp", None),
        P("ctx", "fsdp", None),
        P("fsdp", "ctx", None),
    )
    return jax.shard_map(
        per_device,
        mesh=mesh,
        in_specs=placed,
        out_specs=(
            P("fsdp", "ctx", None),
            P("fsdp", "ctx", None),
            P(),
            P("fsdp", None),
            P("fsdp", None),
            P("fsdp", None),
            P(),
            P(),
            P("fsdp", None),
            P(),
            P("fsdp", None),
            P("ctx", "fsdp", None),
            P("ctx", "fsdp", None),
            P("ctx", "fsdp", None),
        ),
        check_vma=False,
    )
```

```python
import jax
import jax.numpy as jnp
from jax import lax
from jax.sharding import PartitionSpec as P

D = 2048
HEADS = 32
KV_HEADS = 4
HEAD_DIM = 128
TOP = 8


EPSILON = 1e-06
ROPE_BASE = 1000000.0
NEG_FILL = -1e30


def matmul(left, right):
    return jnp.dot(left, right, preferred_element_type=jnp.float32)


def contract(form, left, right):
    return jnp.einsum(form, left, right, preferred_element_type=jnp.float32)


def rms_scale(field):
    return lax.rsqrt(jnp.mean(field * field, axis=-1, keepdims=True) + EPSILON)


def rotary(positions):
    halfway = HEAD_DIM // 2
    inverse = ROPE_BASE ** (-2.0 * jnp.arange(halfway, dtype=jnp.float32) / HEAD_DIM)
    angle = positions.astype(jnp.float32)[:, None] * inverse[None, :]
    return (jnp.cos(angle), jnp.sin(angle))


def rotate(field, cosine, sine_table):
    halfway = field.shape[-1] // 2
    former = field[..., :halfway]
    latter = field[..., halfway:]
    cos_b = cosine[:, None, :]
    sin_b = sine_table[:, None, :]
    return jnp.concatenate(
        [former * cos_b - latter * sin_b, latter * cos_b + former * sin_b], axis=-1
    )


def rotate_back(field, cosine, sine_table):
    halfway = field.shape[-1] // 2
    former = field[..., :halfway]
    latter = field[..., halfway:]
    cos_b = cosine[:, None, :]
    sin_b = sine_table[:, None, :]
    return jnp.concatenate(
        [former * cos_b + latter * sin_b, latter * cos_b - former * sin_b], axis=-1
    )


def norm_back(grad, normed, inv_scale, factor):
    lead_axes = tuple(range(grad.ndim - 1))
    factor_grad = jnp.sum(grad * normed, axis=lead_axes)
    scaled = grad * factor
    return (
        inv_scale * (scaled - normed * jnp.mean(scaled * normed, axis=-1, keepdims=True)),
        factor_grad,
    )


def gather_a2a(x, axis_name, size, axis):
    rep = jnp.broadcast_to(x[None], (size,) + x.shape)
    got = jnp.moveaxis(lax.all_to_all(rep, axis_name, 0, 0, tiled=True), 0, axis)
    return got.reshape(x.shape[:axis] + (size * x.shape[axis],) + x.shape[axis + 1 :])


def scatter_sum_a2a(x, axis_name, size, axis):
    parts = x.reshape(x.shape[:axis] + (size, x.shape[axis] // size) + x.shape[axis + 1 :])
    got = lax.all_to_all(parts, axis_name, axis, axis, tiled=True)
    return jnp.sum(got.astype(jnp.float32), axis=axis)


def per_device(
    hidden_in,
    block_map,
    doc_ids,
    routes,
    attn_gain,
    query_proj,
    key_proj,
    value_proj,
    query_gain,
    key_gain,
    out_proj,
    ffn_gain,
    router_proj,
    expert_gate,
    expert_up,
    expert_down,
    cotangent,
):
    tokens = hidden_in.shape[1]
    ctx_size = lax.axis_size("ctx")
    fsdp_size = lax.axis_size("fsdp")
    fsdp_index = lax.axis_index("fsdp")
    local_experts = expert_gate.shape[0]
    experts = local_experts * ctx_size
    capacity = min(tokens, 3 * tokens * TOP // (2 * experts))
    block_len = tokens // 2
    group_size = HEADS // KV_HEADS
    score_scale = HEAD_DIM ** (-0.5)
    heads_dev = HEADS // fsdp_size
    share = max(1, fsdp_size // KV_HEADS)
    kv_dev = max(1, heads_dev // group_size)
    group_dev = heads_dev // kv_dev
    d_part = D // fsdp_size
    seqs = fsdp_size
    group_rows = seqs * tokens

    ctx_index = lax.axis_index("ctx")
    own_blocks = lax.dynamic_slice_in_dim(block_map, 2 * ctx_index, 2, 0)
    offsets = jnp.arange(block_len, dtype=jnp.int32)
    local_pos = (own_blocks[:, None] * block_len + offsets[None, :]).reshape(-1)
    all_pos = (block_map[:, None] * block_len + offsets[None, :]).reshape(-1)
    cosine, sine_table = rotary(local_pos)
    hidden = hidden_in[0]
    first_scale = rms_scale(hidden)
    first_normed = hidden * first_scale
    first_input = (first_normed * attn_gain).astype(jnp.bfloat16)
    q_width, kv_width = heads_dev * HEAD_DIM, kv_dev * HEAD_DIM
    if share == 1:
        blocks = jnp.concatenate(
            [
                query_proj.reshape(d_part, fsdp_size, q_width),
                key_proj.reshape(d_part, fsdp_size, kv_width),
                value_proj.reshape(d_part, fsdp_size, kv_width),
            ],
            axis=2,
        )
        half = d_part // 2
        core = ctx_index % 2
        lanes = 128
        sent_rows = jnp.moveaxis(
            lax.dynamic_slice_in_dim(blocks, core * half, half, 0), 1, 0
        ).reshape(fsdp_size, -1, lanes)
        common = jnp.concatenate(
            [first_input.reshape(-1, lanes), doc_ids.astype(jnp.bfloat16).reshape(-1, lanes)],
            axis=0,
        )
        payload = jnp.concatenate(
            [sent_rows, jnp.broadcast_to(common[None], (fsdp_size,) + common.shape)], axis=1
        )
        got = lax.all_to_all(payload, "fsdp", 0, 0, tiled=True)
        w_rows = sent_rows.shape[1]
        h_rows = tokens * D // lanes
        mine = got[:, :w_rows].reshape(fsdp_size, half, -1)
        group_input = got[:, w_rows : w_rows + h_rows].reshape(group_rows, D)
        doc_rows = got[:, w_rows + h_rows :].reshape(fsdp_size, -1).astype(jnp.float32)
        other = lax.ppermute(mine, "ctx", [(i, i ^ 1) for i in range(ctx_size)])
        w_cols = jnp.where(
            core == 0, jnp.stack([mine, other], axis=1), jnp.stack([other, mine], axis=1)
        ).reshape(D, -1)
    else:
        group_input = gather_a2a(first_input, "fsdp", fsdp_size, 0)
        doc_rows = gather_a2a(doc_ids.astype(jnp.float32), "fsdp", fsdp_size, 0)
        kv_start = (fsdp_index // share) * HEAD_DIM
        w_cols = jnp.concatenate(
            [
                lax.all_to_all(query_proj, "fsdp", 1, 0, tiled=True),
                lax.dynamic_slice_in_dim(
                    lax.all_gather(key_proj, "fsdp", axis=0, tiled=True), kv_start, HEAD_DIM, 1
                ),
                lax.dynamic_slice_in_dim(
                    lax.all_gather(value_proj, "fsdp", axis=0, tiled=True), kv_start, HEAD_DIM, 1
                ),
            ],
            axis=1,
        )
    w_cols, expert_gate, expert_up, expert_down = lax.optimization_barrier(
        (w_cols, expert_gate, expert_up, expert_down)
    )
    docs_query = jnp.take(doc_rows, local_pos, axis=1)
    docs_key = jnp.take(doc_rows, all_pos, axis=1)
    visible = (all_pos[None, None, :] <= local_pos[None, :, None]) & (
        docs_key[:, None, :] == docs_query[:, :, None]
    )
    projected = matmul(group_input, w_cols)
    query_raw = projected[:, :q_width].reshape(seqs, tokens, heads_dev, HEAD_DIM)
    key_raw = projected[:, q_width : q_width + kv_width].reshape(seqs, tokens, kv_dev, HEAD_DIM)
    value_low = (
        projected[:, q_width + kv_width :]
        .astype(jnp.bfloat16)
        .reshape(seqs, tokens, kv_dev * HEAD_DIM)
    )
    query_scale = rms_scale(query_raw)
    query_normed = query_raw * query_scale
    query_rot = rotate(query_normed * query_gain, cosine, sine_table).astype(jnp.bfloat16)
    key_scale = rms_scale(key_raw)
    key_normed = key_raw * key_scale
    key_rot = (
        rotate(key_normed * key_gain, cosine, sine_table)
        .reshape(seqs, tokens, kv_dev * HEAD_DIM)
        .astype(jnp.bfloat16)
    )
    keys_all = gather_a2a(key_rot, "ctx", ctx_size, 1).reshape(seqs, -1, kv_dev, HEAD_DIM)
    values_all = gather_a2a(value_low, "ctx", ctx_size, 1).reshape(seqs, -1, kv_dev, HEAD_DIM)
    query_groups = query_rot.reshape(seqs, tokens, kv_dev, group_dev, HEAD_DIM)

    def masked_scores():
        scores = contract("stkgd,sjkd->skgtj", query_groups, keys_all) * score_scale
        return jnp.where(visible[:, None, None], scores, NEG_FILL)

    scores = masked_scores()
    peak = jnp.max(scores, axis=-1, keepdims=True)
    expo = jnp.exp(scores - peak)
    total = jnp.sum(expo, axis=-1, keepdims=True)
    probs = (expo / total).astype(jnp.bfloat16)
    log_sums = peak + jnp.log(total)
    attended = (
        contract("skgtj,sjkd->stkgd", probs, values_all)
        .astype(jnp.bfloat16)
        .reshape(group_rows, heads_dev * HEAD_DIM)
    )
    branch_parts = matmul(attended, out_proj).reshape(seqs, tokens, D)
    branch = scatter_sum_a2a(branch_parts.astype(jnp.bfloat16), "fsdp", fsdp_size, 0)[0]
    middle = hidden + branch
    second_scale = rms_scale(middle)
    second_normed = middle * second_scale
    second_input = (second_normed * ffn_gain).astype(jnp.bfloat16)
    w_gate, w_up, w_down, w_router = (
        lax.all_gather(expert_gate, "fsdp", axis=1, tiled=True),
        lax.all_gather(expert_up, "fsdp", axis=1, tiled=True),
        lax.all_gather(expert_down, "fsdp", axis=1, tiled=True),
        gather_a2a(router_proj, "fsdp", fsdp_size, 0),
    )
    logits = matmul(second_input, w_router)
    route_ids = routes[0]
    chosen = jnp.take_along_axis(logits, route_ids, axis=1)
    route_weights = jax.nn.softmax(chosen, axis=-1)
    flat_ids = route_ids.reshape(-1)
    expert_range = jnp.arange(experts, dtype=jnp.int32)
    one_hot = (flat_ids[:, None] == expert_range[None, :]).astype(jnp.int32)
    earlier = jnp.cumsum(one_hot, axis=0) - one_hot
    slot_index = jnp.sum(earlier * one_hot, axis=1)
    target = flat_ids * capacity + slot_index

    def dispatch(route_rows):
        buffer = jnp.zeros((experts * capacity, D), jnp.bfloat16).at[target].set(route_rows)
        return buffer.reshape(ctx_size, local_experts, capacity, D)

    def collect(returned):
        return jnp.take(returned.reshape(experts * capacity, D), target, axis=0)

    received = lax.all_to_all(
        dispatch(jnp.repeat(second_input, TOP, axis=0)),
        "ctx",
        split_axis=0,
        concat_axis=2,
        tiled=True,
    )[0]
    gate_val = contract("erd,edf->erf", received, w_gate)
    up_val = contract("erd,edf->erf", received, w_up)
    gate_sig = jax.nn.sigmoid(gate_val)
    hid_low = (gate_val * gate_sig * up_val).astype(jnp.bfloat16)
    expert_out = contract("erf,efd->erd", hid_low, w_down).astype(jnp.bfloat16)
    route_out = (
        collect(lax.all_to_all(expert_out[None], "ctx", split_axis=2, concat_axis=0, tiled=True))
        .reshape(tokens, TOP, D)
        .astype(jnp.float32)
    )
    layer_out = middle + jnp.einsum("tr,trd->td", route_weights, route_out)
    grad_out = cotangent[0]
    grad_weights = jnp.einsum("td,trd->tr", grad_out, route_out)
    grad_routes = (
        (route_weights[:, :, None] * grad_out[:, None, :])
        .astype(jnp.bfloat16)
        .reshape(tokens * TOP, D)
    )
    grad_expert = lax.all_to_all(
        dispatch(grad_routes), "ctx", split_axis=0, concat_axis=2, tiled=True
    )[0]
    grad_hid = contract("erd,efd->erf", grad_expert, w_down)
    down_grad_full = contract("erf,erd->efd", hid_low, grad_expert)
    grad_gate = (grad_hid * up_val * gate_sig * (1.0 + gate_val * (1.0 - gate_sig))).astype(
        jnp.bfloat16
    )
    grad_up = (grad_hid * gate_val * gate_sig).astype(jnp.bfloat16)
    gate_grad_full = contract("erd,erf->edf", received, grad_gate)
    up_grad_full = contract("erd,erf->edf", received, grad_up)
    grad_rows = (
        contract("erf,edf->erd", grad_gate, w_gate) + contract("erf,edf->erd", grad_up, w_up)
    ).astype(jnp.bfloat16)
    grad_copies = collect(
        lax.all_to_all(grad_rows[None], "ctx", split_axis=2, concat_axis=0, tiled=True)
    ).reshape(tokens, TOP, D)
    grad_chosen = route_weights * (
        grad_weights - jnp.sum(route_weights * grad_weights, axis=-1, keepdims=True)
    )
    route_hot = (route_ids[:, :, None] == expert_range[None, None, :]).astype(jnp.float32)
    grad_logits = jnp.einsum("tr,tre->te", grad_chosen, route_hot).astype(jnp.bfloat16)
    router_grad_full = contract("td,te->de", second_input, grad_logits)
    grad_second = jnp.sum(grad_copies.astype(jnp.float32), axis=1) + contract(
        "te,de->td", grad_logits, w_router
    )
    grad_middle, ffn_gain_grad = norm_back(grad_second, second_normed, second_scale, ffn_gain)
    grad_middle = grad_middle + grad_out

    grad_branch = gather_a2a(grad_middle.astype(jnp.bfloat16), "fsdp", fsdp_size, 0)
    out_grad_part = contract("tq,td->qd", attended, grad_branch)
    grad_attended = contract("td,qd->tq", grad_branch, out_proj).astype(jnp.bfloat16)
    grad_groups = grad_attended.reshape(seqs, tokens, kv_dev, group_dev, HEAD_DIM)

    probs_back = jnp.exp(masked_scores() - log_sums)
    grad_probs = contract("stkgd,sjkd->skgtj", grad_groups, values_all)
    delta = jnp.sum(probs_back * grad_probs, axis=-1, keepdims=True)
    grad_scores = (probs_back * (grad_probs - delta)).astype(jnp.bfloat16)
    grad_qgroups = contract("skgtj,sjkd->stkgd", grad_scores, keys_all) * score_scale
    grad_kheads = contract("skgtj,stkgd->sjkd", grad_scores, query_groups) * score_scale
    grad_vheads = contract("skgtj,stkgd->sjkd", probs_back.astype(jnp.bfloat16), grad_groups)

    def kv_reduce(grads):
        summed = scatter_sum_a2a(
            grads.reshape(seqs, -1, kv_dev * HEAD_DIM).astype(jnp.bfloat16), "ctx", ctx_size, 1
        )
        total = summed
        for step in range(1, share):
            pairs = [
                (i, (i // share) * share + (i % share + step) % share) for i in range(fsdp_size)
            ]
            total = total + lax.ppermute(summed, "fsdp", pairs)
        return total

    grad_key_rot = kv_reduce(grad_kheads)
    grad_value = kv_reduce(grad_vheads)
    grad_query_rot = grad_qgroups.reshape(seqs, tokens, heads_dev, HEAD_DIM)
    grad_query, query_gain_grad = norm_back(
        rotate_back(grad_query_rot, cosine, sine_table), query_normed, query_scale, query_gain
    )
    grad_key, key_gain_grad = norm_back(
        rotate_back(grad_key_rot.reshape(seqs, tokens, kv_dev, HEAD_DIM), cosine, sine_table),
        key_normed,
        key_scale,
        key_gain,
    )
    if share > 1:
        key_gain_grad = key_gain_grad * (fsdp_index % share == 0).astype(jnp.float32)
    grad_query = grad_query.reshape(group_rows, heads_dev * HEAD_DIM).astype(jnp.bfloat16)
    grad_key = grad_key.reshape(group_rows, kv_dev * HEAD_DIM).astype(jnp.bfloat16)
    grad_value = grad_value.reshape(group_rows, kv_dev * HEAD_DIM).astype(jnp.bfloat16)

    def gather_heads(parts):
        whole = parts.reshape(group_rows, -1)
        if share > 1:
            whole = whole.reshape(group_rows, KV_HEADS, share, HEAD_DIM)[:, :, 0]
            whole = whole.reshape(group_rows, KV_HEADS * HEAD_DIM)
        return whole

    joined = gather_a2a(
        jnp.concatenate([grad_query, grad_key, grad_value], axis=1)[:, None], "fsdp", fsdp_size, 1
    )
    query_all = joined[:, :, :q_width].reshape(group_rows, -1)
    key_all = gather_heads(joined[:, :, q_width : q_width + kv_width])
    value_all = gather_heads(joined[:, :, q_width + kv_width :])
    input_part = lax.dynamic_slice_in_dim(group_input, fsdp_index * d_part, d_part, 1)
    query_grad_part = contract("td,tq->dq", input_part, query_all)
    key_grad_part = contract("td,tq->dq", input_part, key_all)
    value_grad_part = contract("td,tq->dq", input_part, value_all)
    grad_first_cols = (
        contract("tq,dq->td", query_all, query_proj)
        + contract("tq,dq->td", key_all, key_proj)
        + contract("tq,dq->td", value_all, value_proj)
    )
    grad_first = lax.all_to_all(
        grad_first_cols.reshape(seqs, tokens, d_part), "fsdp", 0, 2, tiled=True
    )[0]
    grad_hidden, attn_gain_grad = norm_back(grad_first, first_normed, first_scale, attn_gain)
    grad_hidden = grad_hidden + grad_middle
    gate_grad, up_grad, down_grad = (
        lax.psum_scatter(
            gate_grad_full.astype(jnp.bfloat16), "fsdp", scatter_dimension=1, tiled=True
        ).astype(jnp.float32),
        lax.psum_scatter(
            up_grad_full.astype(jnp.bfloat16), "fsdp", scatter_dimension=1, tiled=True
        ).astype(jnp.float32),
        lax.psum_scatter(
            down_grad_full.astype(jnp.bfloat16), "fsdp", scatter_dimension=1, tiled=True
        ).astype(jnp.float32),
    )
    router_shard = scatter_sum_a2a(router_grad_full, "fsdp", fsdp_size, 0)
    query_grad, key_grad, value_grad, out_grad, router_grad = (
        lax.psum(query_grad_part.astype(jnp.bfloat16), "ctx").astype(jnp.float32),
        lax.psum(key_grad_part.astype(jnp.bfloat16), "ctx").astype(jnp.float32),
        lax.psum(value_grad_part.astype(jnp.bfloat16), "ctx").astype(jnp.float32),
        lax.psum(out_grad_part.astype(jnp.bfloat16), "ctx").astype(jnp.float32),
        jnp.sum(gather_a2a(router_shard[None], "ctx", ctx_size, 0), axis=0),
    )
    attn_gain_total, query_gain_total, key_gain_total, ffn_gain_total = lax.psum(
        (attn_gain_grad, query_gain_grad, key_gain_grad, ffn_gain_grad), ("ctx", "fsdp")
    )
    return (
        layer_out[None],
        grad_hidden[None],
        attn_gain_total,
        query_grad,
        key_grad,
        value_grad,
        query_gain_total,
        key_gain_total,
        out_grad,
        ffn_gain_total,
        router_grad,
        gate_grad,
        up_grad,
        down_grad,
    )


def solution(mesh):
    placed = (
        P("fsdp", "ctx", None),
        P(),
        P("fsdp", None),
        P("fsdp", "ctx", None),
        P(),
        P("fsdp", None),
        P("fsdp", None),
        P("fsdp", None),
        P(),
        P(),
        P("fsdp", None),
        P(),
        P("fsdp", None),
        P("ctx", "fsdp", None),
        P("ctx", "fsdp", None),
        P("ctx", "fsdp", None),
        P("fsdp", "ctx", None),
    )
    return jax.shard_map(
        per_device,
        mesh=mesh,
        in_specs=placed,
        out_specs=(
            P("fsdp", "ctx", None),
            P("fsdp", "ctx", None),
            P(),
            P("fsdp", None),
            P("fsdp", None),
            P("fsdp", None),
            P(),
            P(),
            P("fsdp", None),
            P(),
            P("fsdp", None),
            P("ctx", "fsdp", None),
            P("ctx", "fsdp", None),
            P("ctx", "fsdp", None),
        ),
        check_vma=False,
    )
```

```python
import jax
import jax.numpy as jnp
from jax import lax
from jax.sharding import PartitionSpec as P


D = 2048
HEADS = 32
KV_HEADS = 4
HEAD_DIM = 128
TOP = 8


EPSILON = 1e-06
ROPE_BASE = 1000000.0
NEG_FILL = -1e30


def matmul(left, right):
    return jnp.dot(left, right, preferred_element_type=jnp.float32)


def contract(form, left, right):
    return jnp.einsum(form, left, right, preferred_element_type=jnp.float32)


def rms_scale(field):
    return lax.rsqrt(jnp.mean(field * field, axis=-1, keepdims=True) + EPSILON)


def rotary(positions):
    halfway = HEAD_DIM // 2
    inverse = ROPE_BASE ** (-2.0 * jnp.arange(halfway, dtype=jnp.float32) / HEAD_DIM)
    angle = positions.astype(jnp.float32)[:, None] * inverse[None, :]
    return (jnp.cos(angle), jnp.sin(angle))


def rotate(field, cosine, sine_table):
    halfway = field.shape[-1] // 2
    former = field[..., :halfway]
    latter = field[..., halfway:]
    cos_b = cosine[:, None, :]
    sin_b = sine_table[:, None, :]
    return jnp.concatenate(
        [former * cos_b - latter * sin_b, latter * cos_b + former * sin_b], axis=-1
    )


def rotate_back(field, cosine, sine_table):
    halfway = field.shape[-1] // 2
    former = field[..., :halfway]
    latter = field[..., halfway:]
    cos_b = cosine[:, None, :]
    sin_b = sine_table[:, None, :]
    return jnp.concatenate(
        [former * cos_b + latter * sin_b, latter * cos_b - former * sin_b], axis=-1
    )


def norm_back(grad, normed, inv_scale, factor):
    lead_axes = tuple(range(grad.ndim - 1))
    factor_grad = jnp.sum(grad * normed, axis=lead_axes)
    scaled = grad * factor
    return (
        inv_scale * (scaled - normed * jnp.mean(scaled * normed, axis=-1, keepdims=True)),
        factor_grad,
    )


def gather_a2a(x, axis_name, size, axis):
    rep = jnp.broadcast_to(x[None], (size,) + x.shape)
    got = jnp.moveaxis(lax.all_to_all(rep, axis_name, 0, 0, tiled=True), 0, axis)
    return got.reshape(x.shape[:axis] + (size * x.shape[axis],) + x.shape[axis + 1 :])


def scatter_sum_a2a(x, axis_name, size, axis):
    parts = x.reshape(x.shape[:axis] + (size, x.shape[axis] // size) + x.shape[axis + 1 :])
    got = lax.all_to_all(parts, axis_name, axis, axis, tiled=True)
    return jnp.sum(got.astype(jnp.float32), axis=axis)


def per_device(
    hidden_in,
    block_map,
    doc_ids,
    routes,
    attn_gain,
    query_proj,
    key_proj,
    value_proj,
    query_gain,
    key_gain,
    out_proj,
    ffn_gain,
    router_proj,
    expert_gate,
    expert_up,
    expert_down,
    cotangent,
):
    tokens = hidden_in.shape[1]
    ctx_size = lax.axis_size("ctx")
    fsdp_size = lax.axis_size("fsdp")
    fsdp_index = lax.axis_index("fsdp")
    local_experts = expert_gate.shape[0]
    experts = local_experts * ctx_size
    capacity = min(tokens, 3 * tokens * TOP // (2 * experts))
    block_len = tokens // 2
    group_size = HEADS // KV_HEADS
    score_scale = HEAD_DIM ** (-0.5)
    heads_dev = HEADS // fsdp_size
    share = max(1, fsdp_size // KV_HEADS)
    kv_dev = max(1, heads_dev // group_size)
    group_dev = heads_dev // kv_dev
    d_part = D // fsdp_size
    seqs = fsdp_size
    group_rows = seqs * tokens

    ctx_index = lax.axis_index("ctx")
    own_blocks = lax.dynamic_slice_in_dim(block_map, 2 * ctx_index, 2, 0)
    offsets = jnp.arange(block_len, dtype=jnp.int32)
    local_pos = (own_blocks[:, None] * block_len + offsets[None, :]).reshape(-1)
    all_pos = (block_map[:, None] * block_len + offsets[None, :]).reshape(-1)
    cosine, sine_table = rotary(local_pos)
    hidden = hidden_in[0]
    first_scale = rms_scale(hidden)
    first_normed = hidden * first_scale
    first_input = (first_normed * attn_gain).astype(jnp.bfloat16)
    q_width, kv_width = heads_dev * HEAD_DIM, kv_dev * HEAD_DIM
    if share == 1:
        blocks = jnp.concatenate(
            [
                query_proj.reshape(d_part, fsdp_size, q_width),
                key_proj.reshape(d_part, fsdp_size, kv_width),
                value_proj.reshape(d_part, fsdp_size, kv_width),
            ],
            axis=2,
        )
        half = d_part // 2
        core = ctx_index % 2
        lanes = 128
        sent_rows = jnp.moveaxis(
            lax.dynamic_slice_in_dim(blocks, core * half, half, 0), 1, 0
        ).reshape(fsdp_size, -1, lanes)
        common = jnp.concatenate(
            [first_input.reshape(-1, lanes), doc_ids.astype(jnp.bfloat16).reshape(-1, lanes)],
            axis=0,
        )
        payload = jnp.concatenate(
            [sent_rows, jnp.broadcast_to(common[None], (fsdp_size,) + common.shape)], axis=1
        )
        got = lax.all_to_all(payload, "fsdp", 0, 0, tiled=True)
        w_rows = sent_rows.shape[1]
        h_rows = tokens * D // lanes
        mine = got[:, :w_rows].reshape(fsdp_size, half, -1)
        group_input = got[:, w_rows : w_rows + h_rows].reshape(group_rows, D)
        doc_rows = got[:, w_rows + h_rows :].reshape(fsdp_size, -1).astype(jnp.float32)
        other = lax.ppermute(mine, "ctx", [(i, i ^ 1) for i in range(ctx_size)])
        w_cols = jnp.where(
            core == 0, jnp.stack([mine, other], axis=1), jnp.stack([other, mine], axis=1)
        ).reshape(D, -1)
    else:
        group_input = gather_a2a(first_input, "fsdp", fsdp_size, 0)
        doc_rows = gather_a2a(doc_ids.astype(jnp.float32), "fsdp", fsdp_size, 0)
        kv_start = (fsdp_index // share) * HEAD_DIM
        w_cols = jnp.concatenate(
            [
                lax.all_to_all(query_proj, "fsdp", 1, 0, tiled=True),
                lax.dynamic_slice_in_dim(
                    lax.all_gather(key_proj, "fsdp", axis=0, tiled=True), kv_start, HEAD_DIM, 1
                ),
                lax.dynamic_slice_in_dim(
                    lax.all_gather(value_proj, "fsdp", axis=0, tiled=True), kv_start, HEAD_DIM, 1
                ),
            ],
            axis=1,
        )
    w_cols, expert_gate, expert_up, expert_down = lax.optimization_barrier(
        (w_cols, expert_gate, expert_up, expert_down)
    )
    docs_query = jnp.take(doc_rows, local_pos, axis=1)
    docs_key = jnp.take(doc_rows, all_pos, axis=1)
    visible = (all_pos[None, None, :] <= local_pos[None, :, None]) & (
        docs_key[:, None, :] == docs_query[:, :, None]
    )
    projected = matmul(group_input, w_cols)
    query_raw = projected[:, :q_width].reshape(seqs, tokens, heads_dev, HEAD_DIM)
    key_raw = projected[:, q_width : q_width + kv_width].reshape(seqs, tokens, kv_dev, HEAD_DIM)
    value_low = (
        projected[:, q_width + kv_width :]
        .astype(jnp.bfloat16)
        .reshape(seqs, tokens, kv_dev * HEAD_DIM)
    )
    query_scale = rms_scale(query_raw)
    query_normed = query_raw * query_scale
    query_rot = rotate(query_normed * query_gain, cosine, sine_table).astype(jnp.bfloat16)
    key_scale = rms_scale(key_raw)
    key_normed = key_raw * key_scale
    key_rot = (
        rotate(key_normed * key_gain, cosine, sine_table)
        .reshape(seqs, tokens, kv_dev * HEAD_DIM)
        .astype(jnp.bfloat16)
    )
    keys_all = gather_a2a(key_rot, "ctx", ctx_size, 1).reshape(seqs, -1, kv_dev, HEAD_DIM)
    values_all = gather_a2a(value_low, "ctx", ctx_size, 1).reshape(seqs, -1, kv_dev, HEAD_DIM)
    query_groups = query_rot.reshape(seqs, tokens, kv_dev, group_dev, HEAD_DIM)

    def masked_scores():
        scores = contract("stkgd,sjkd->skgtj", query_groups, keys_all) * score_scale
        return jnp.where(visible[:, None, None], scores, NEG_FILL)

    scores = masked_scores()
    peak = jnp.max(scores, axis=-1, keepdims=True)
    expo = jnp.exp(scores - peak)
    total = jnp.sum(expo, axis=-1, keepdims=True)
    probs = (expo / total).astype(jnp.bfloat16)
    log_sums = peak + jnp.log(total)
    attended = (
        contract("skgtj,sjkd->stkgd", probs, values_all)
        .astype(jnp.bfloat16)
        .reshape(group_rows, heads_dev * HEAD_DIM)
    )
    branch_parts = matmul(attended, out_proj).reshape(seqs, tokens, D)
    branch = scatter_sum_a2a(branch_parts.astype(jnp.bfloat16), "fsdp", fsdp_size, 0)[0]
    middle = hidden + branch
    second_scale = rms_scale(middle)
    second_normed = middle * second_scale
    second_input = (second_normed * ffn_gain).astype(jnp.bfloat16)
    w_gate, w_up, w_down, w_router = (
        lax.all_gather(expert_gate, "fsdp", axis=1, tiled=True),
        lax.all_gather(expert_up, "fsdp", axis=1, tiled=True),
        lax.all_gather(expert_down, "fsdp", axis=1, tiled=True),
        gather_a2a(router_proj, "fsdp", fsdp_size, 0),
    )
    logits = matmul(second_input, w_router)
    route_ids = routes[0]
    chosen = jnp.take_along_axis(logits, route_ids, axis=1)
    route_weights = jax.nn.softmax(chosen, axis=-1)
    flat_ids = route_ids.reshape(-1)
    expert_range = jnp.arange(experts, dtype=jnp.int32)
    one_hot = (flat_ids[:, None] == expert_range[None, :]).astype(jnp.int32)
    earlier = jnp.cumsum(one_hot, axis=0) - one_hot
    slot_index = jnp.sum(earlier * one_hot, axis=1)
    target = flat_ids * capacity + slot_index

    def dispatch(route_rows):
        buffer = jnp.zeros((experts * capacity, D), jnp.bfloat16).at[target].set(route_rows)
        return buffer.reshape(ctx_size, local_experts, capacity, D)

    def collect(returned):
        return jnp.take(returned.reshape(experts * capacity, D), target, axis=0)

    received = lax.all_to_all(
        dispatch(jnp.repeat(second_input, TOP, axis=0)),
        "ctx",
        split_axis=0,
        concat_axis=2,
        tiled=True,
    )[0]
    gate_val = contract("erd,edf->erf", received, w_gate)
    up_val = contract("erd,edf->erf", received, w_up)
    gate_sig = jax.nn.sigmoid(gate_val)
    hid_low = (gate_val * gate_sig * up_val).astype(jnp.bfloat16)
    expert_out = contract("erf,efd->erd", hid_low, w_down).astype(jnp.bfloat16)
    route_out = (
        collect(lax.all_to_all(expert_out[None], "ctx", split_axis=2, concat_axis=0, tiled=True))
        .reshape(tokens, TOP, D)
        .astype(jnp.float32)
    )
    layer_out = middle + jnp.einsum("tr,trd->td", route_weights, route_out)
    grad_out = cotangent[0]
    grad_weights = jnp.einsum("td,trd->tr", grad_out, route_out)
    grad_routes = (
        (route_weights[:, :, None] * grad_out[:, None, :])
        .astype(jnp.bfloat16)
        .reshape(tokens * TOP, D)
    )
    grad_expert = lax.all_to_all(
        dispatch(grad_routes), "ctx", split_axis=0, concat_axis=2, tiled=True
    )[0]
    grad_hid = contract("erd,efd->erf", grad_expert, w_down)
    down_grad_full = contract("erf,erd->efd", hid_low, grad_expert)
    grad_gate = (grad_hid * up_val * gate_sig * (1.0 + gate_val * (1.0 - gate_sig))).astype(
        jnp.bfloat16
    )
    grad_up = (grad_hid * gate_val * gate_sig).astype(jnp.bfloat16)
    gate_grad_full = contract("erd,erf->edf", received, grad_gate)
    up_grad_full = contract("erd,erf->edf", received, grad_up)
    grad_rows = (
        contract("erf,edf->erd", grad_gate, w_gate) + contract("erf,edf->erd", grad_up, w_up)
    ).astype(jnp.bfloat16)
    grad_copies = collect(
        lax.all_to_all(grad_rows[None], "ctx", split_axis=2, concat_axis=0, tiled=True)
    ).reshape(tokens, TOP, D)
    grad_chosen = route_weights * (
        grad_weights - jnp.sum(route_weights * grad_weights, axis=-1, keepdims=True)
    )
    route_hot = (route_ids[:, :, None] == expert_range[None, None, :]).astype(jnp.float32)
    grad_logits = jnp.einsum("tr,tre->te", grad_chosen, route_hot).astype(jnp.bfloat16)
    router_grad_full = contract("td,te->de", second_input, grad_logits)
    grad_second = jnp.sum(grad_copies.astype(jnp.float32), axis=1) + contract(
        "te,de->td", grad_logits, w_router
    )
    grad_middle, ffn_gain_grad = norm_back(grad_second, second_normed, second_scale, ffn_gain)
    grad_middle = grad_middle + grad_out

    grad_branch = gather_a2a(grad_middle.astype(jnp.bfloat16), "fsdp", fsdp_size, 0)
    out_grad_part = contract("tq,td->qd", attended, grad_branch)
    grad_attended = contract("td,qd->tq", grad_branch, out_proj).astype(jnp.bfloat16)
    grad_groups = grad_attended.reshape(seqs, tokens, kv_dev, group_dev, HEAD_DIM)

    probs_back = jnp.exp(masked_scores() - log_sums)
    grad_probs = contract("stkgd,sjkd->skgtj", grad_groups, values_all)
    delta = jnp.sum(probs_back * grad_probs, axis=-1, keepdims=True)
    grad_scores = (probs_back * (grad_probs - delta)).astype(jnp.bfloat16)
    grad_qgroups = contract("skgtj,sjkd->stkgd", grad_scores, keys_all) * score_scale
    grad_kheads = contract("skgtj,stkgd->sjkd", grad_scores, query_groups) * score_scale
    grad_vheads = contract("skgtj,stkgd->sjkd", probs_back.astype(jnp.bfloat16), grad_groups)

    def kv_reduce(grads):
        summed = scatter_sum_a2a(
            grads.reshape(seqs, -1, kv_dev * HEAD_DIM).astype(jnp.bfloat16), "ctx", ctx_size, 1
        )
        total = summed
        for step in range(1, share):
            pairs = [
                (i, (i // share) * share + (i % share + step) % share) for i in range(fsdp_size)
            ]
            total = total + lax.ppermute(summed, "fsdp", pairs)
        return total

    grad_key_rot = kv_reduce(grad_kheads)
    grad_value = kv_reduce(grad_vheads)
    grad_query_rot = grad_qgroups.reshape(seqs, tokens, heads_dev, HEAD_DIM)
    grad_query, query_gain_grad = norm_back(
        rotate_back(grad_query_rot, cosine, sine_table), query_normed, query_scale, query_gain
    )
    grad_key, key_gain_grad = norm_back(
        rotate_back(grad_key_rot.reshape(seqs, tokens, kv_dev, HEAD_DIM), cosine, sine_table),
        key_normed,
        key_scale,
        key_gain,
    )
    if share > 1:
        key_gain_grad = key_gain_grad * (fsdp_index % share == 0).astype(jnp.float32)
    grad_query = grad_query.reshape(group_rows, heads_dev * HEAD_DIM).astype(jnp.bfloat16)
    grad_key = grad_key.reshape(group_rows, kv_dev * HEAD_DIM).astype(jnp.bfloat16)
    grad_value = grad_value.reshape(group_rows, kv_dev * HEAD_DIM).astype(jnp.bfloat16)

    def gather_heads(parts):
        whole = parts.reshape(group_rows, -1)
        if share > 1:
            whole = whole.reshape(group_rows, KV_HEADS, share, HEAD_DIM)[:, :, 0]
            whole = whole.reshape(group_rows, KV_HEADS * HEAD_DIM)
        return whole

    joined = gather_a2a(
        jnp.concatenate([grad_query, grad_key, grad_value], axis=1)[:, None], "fsdp", fsdp_size, 1
    )
    query_all = joined[:, :, :q_width].reshape(group_rows, -1)
    key_all = gather_heads(joined[:, :, q_width : q_width + kv_width])
    value_all = gather_heads(joined[:, :, q_width + kv_width :])
    input_part = lax.dynamic_slice_in_dim(group_input, fsdp_index * d_part, d_part, 1)
    query_grad_part = contract("td,tq->dq", input_part, query_all)
    key_grad_part = contract("td,tq->dq", input_part, key_all)
    value_grad_part = contract("td,tq->dq", input_part, value_all)
    grad_first_cols = (
        contract("tq,dq->td", query_all, query_proj)
        + contract("tq,dq->td", key_all, key_proj)
        + contract("tq,dq->td", value_all, value_proj)
    )
    grad_first = lax.all_to_all(
        grad_first_cols.reshape(seqs, tokens, d_part), "fsdp", 0, 2, tiled=True
    )[0]
    grad_hidden, attn_gain_grad = norm_back(grad_first, first_normed, first_scale, attn_gain)
    grad_hidden = grad_hidden + grad_middle
    gate_grad, up_grad, down_grad = (
        lax.psum_scatter(
            full.astype(jnp.bfloat16), "fsdp", scatter_dimension=1, tiled=True
        ).astype(jnp.float32)
        for full in (gate_grad_full, up_grad_full, down_grad_full)
    )
    router_shard = scatter_sum_a2a(router_grad_full, "fsdp", fsdp_size, 0)
    out_grad = lax.psum(out_grad_part.astype(jnp.bfloat16), "ctx").astype(jnp.float32)
    query_grad_part, out_grad = lax.optimization_barrier((query_grad_part, out_grad))
    query_grad, key_grad, value_grad, router_grad = (
        lax.psum(query_grad_part.astype(jnp.bfloat16), "ctx").astype(jnp.float32),
        lax.psum(key_grad_part.astype(jnp.bfloat16), "ctx").astype(jnp.float32),
        lax.psum(value_grad_part.astype(jnp.bfloat16), "ctx").astype(jnp.float32),
        jnp.sum(gather_a2a(router_shard[None], "ctx", ctx_size, 0), axis=0),
    )
    attn_gain_total, query_gain_total, key_gain_total, ffn_gain_total = lax.psum(
        (attn_gain_grad, query_gain_grad, key_gain_grad, ffn_gain_grad), ("ctx", "fsdp")
    )
    return (
        layer_out[None],
        grad_hidden[None],
        attn_gain_total,
        query_grad,
        key_grad,
        value_grad,
        query_gain_total,
        key_gain_total,
        out_grad,
        ffn_gain_total,
        router_grad,
        gate_grad,
        up_grad,
        down_grad,
    )


def solution(mesh):
    placed = (
        P("fsdp", "ctx", None),
        P(),
        P("fsdp", None),
        P("fsdp", "ctx", None),
        P(),
        P("fsdp", None),
        P("fsdp", None),
        P("fsdp", None),
        P(),
        P(),
        P("fsdp", None),
        P(),
        P("fsdp", None),
        P("ctx", "fsdp", None),
        P("ctx", "fsdp", None),
        P("ctx", "fsdp", None),
        P("fsdp", "ctx", None),
    )
    return jax.shard_map(
        per_device,
        mesh=mesh,
        in_specs=placed,
        out_specs=(
            P("fsdp", "ctx", None),
            P("fsdp", "ctx", None),
            P(),
            P("fsdp", None),
            P("fsdp", None),
            P("fsdp", None),
            P(),
            P(),
            P("fsdp", None),
            P(),
            P("fsdp", None),
            P("ctx", "fsdp", None),
            P("ctx", "fsdp", None),
            P("ctx", "fsdp", None),
        ),
        check_vma=False,
    )
```

```python
import jax
import jax.numpy as jnp
from jax import lax
from jax.sharding import PartitionSpec as P


D = 2048
HEADS = 32
KV_HEADS = 4
HEAD_DIM = 128
TOP = 8


EPSILON = 1e-06
ROPE_BASE = 1000000.0
NEG_FILL = -1e30


def matmul(left, right):
    return jnp.dot(left, right, preferred_element_type=jnp.float32)


def contract(form, left, right):
    return jnp.einsum(form, left, right, preferred_element_type=jnp.float32)


def rms_scale(field):
    return lax.rsqrt(jnp.mean(field * field, axis=-1, keepdims=True) + EPSILON)


def rotary(positions):
    halfway = HEAD_DIM // 2
    inverse = ROPE_BASE ** (-2.0 * jnp.arange(halfway, dtype=jnp.float32) / HEAD_DIM)
    angle = positions.astype(jnp.float32)[:, None] * inverse[None, :]
    return (jnp.cos(angle), jnp.sin(angle))


def rotate(field, cosine, sine_table):
    halfway = field.shape[-1] // 2
    former = field[..., :halfway]
    latter = field[..., halfway:]
    cos_b = cosine[:, None, :]
    sin_b = sine_table[:, None, :]
    return jnp.concatenate(
        [former * cos_b - latter * sin_b, latter * cos_b + former * sin_b], axis=-1
    )


def rotate_back(field, cosine, sine_table):
    halfway = field.shape[-1] // 2
    former = field[..., :halfway]
    latter = field[..., halfway:]
    cos_b = cosine[:, None, :]
    sin_b = sine_table[:, None, :]
    return jnp.concatenate(
        [former * cos_b + latter * sin_b, latter * cos_b - former * sin_b], axis=-1
    )


def norm_back(grad, normed, inv_scale, factor):
    lead_axes = tuple(range(grad.ndim - 1))
    factor_grad = jnp.sum(grad * normed, axis=lead_axes)
    scaled = grad * factor
    return (
        inv_scale * (scaled - normed * jnp.mean(scaled * normed, axis=-1, keepdims=True)),
        factor_grad,
    )


def gather_a2a(x, axis_name, size, axis):
    rep = jnp.broadcast_to(x[None], (size,) + x.shape)
    got = jnp.moveaxis(lax.all_to_all(rep, axis_name, 0, 0, tiled=True), 0, axis)
    return got.reshape(x.shape[:axis] + (size * x.shape[axis],) + x.shape[axis + 1 :])


def scatter_sum_a2a(x, axis_name, size, axis):
    parts = x.reshape(x.shape[:axis] + (size, x.shape[axis] // size) + x.shape[axis + 1 :])
    got = lax.all_to_all(parts, axis_name, axis, axis, tiled=True)
    return jnp.sum(got.astype(jnp.float32), axis=axis)


def per_device(
    hidden_in,
    block_map,
    doc_ids,
    routes,
    attn_gain,
    query_proj,
    key_proj,
    value_proj,
    query_gain,
    key_gain,
    out_proj,
    ffn_gain,
    router_proj,
    expert_gate,
    expert_up,
    expert_down,
    cotangent,
):
    tokens = hidden_in.shape[1]
    ctx_size = lax.axis_size("ctx")
    fsdp_size = lax.axis_size("fsdp")
    fsdp_index = lax.axis_index("fsdp")
    local_experts = expert_gate.shape[0]
    experts = local_experts * ctx_size
    capacity = min(tokens, 3 * tokens * TOP // (2 * experts))
    block_len = tokens // 2
    group_size = HEADS // KV_HEADS
    score_scale = HEAD_DIM ** (-0.5)
    heads_dev = HEADS // fsdp_size
    share = max(1, fsdp_size // KV_HEADS)
    kv_dev = max(1, heads_dev // group_size)
    group_dev = heads_dev // kv_dev
    d_part = D // fsdp_size
    seqs = fsdp_size
    group_rows = seqs * tokens

    ctx_index = lax.axis_index("ctx")
    own_blocks = lax.dynamic_slice_in_dim(block_map, 2 * ctx_index, 2, 0)
    offsets = jnp.arange(block_len, dtype=jnp.int32)
    local_pos = (own_blocks[:, None] * block_len + offsets[None, :]).reshape(-1)
    all_pos = (block_map[:, None] * block_len + offsets[None, :]).reshape(-1)
    cosine, sine_table = rotary(local_pos)
    hidden = hidden_in[0]
    first_scale = rms_scale(hidden)
    first_normed = hidden * first_scale
    first_input = (first_normed * attn_gain).astype(jnp.bfloat16)
    q_width, kv_width = heads_dev * HEAD_DIM, kv_dev * HEAD_DIM
    if share == 1:
        blocks = jnp.concatenate(
            [
                query_proj.reshape(d_part, fsdp_size, q_width),
                key_proj.reshape(d_part, fsdp_size, kv_width),
                value_proj.reshape(d_part, fsdp_size, kv_width),
            ],
            axis=2,
        )
        half = d_part // 2
        core = ctx_index % 2
        lanes = 128
        sent_rows = jnp.moveaxis(
            lax.dynamic_slice_in_dim(blocks, core * half, half, 0), 1, 0
        ).reshape(fsdp_size, -1, lanes)
        common = jnp.concatenate(
            [first_input.reshape(-1, lanes), doc_ids.astype(jnp.bfloat16).reshape(-1, lanes)],
            axis=0,
        )
        payload = jnp.concatenate(
            [sent_rows, jnp.broadcast_to(common[None], (fsdp_size,) + common.shape)], axis=1
        )
        got = lax.all_to_all(payload, "fsdp", 0, 0, tiled=True)
        w_rows = sent_rows.shape[1]
        h_rows = tokens * D // lanes
        mine = got[:, :w_rows].reshape(fsdp_size, half, -1)
        group_input = got[:, w_rows : w_rows + h_rows].reshape(group_rows, D)
        doc_rows = got[:, w_rows + h_rows :].reshape(fsdp_size, -1).astype(jnp.float32)
        other = lax.ppermute(mine, "ctx", [(i, i ^ 1) for i in range(ctx_size)])
        w_cols = jnp.where(
            core == 0, jnp.stack([mine, other], axis=1), jnp.stack([other, mine], axis=1)
        ).reshape(D, -1)
    else:
        group_input = gather_a2a(first_input, "fsdp", fsdp_size, 0)
        doc_rows = gather_a2a(doc_ids.astype(jnp.float32), "fsdp", fsdp_size, 0)
        kv_start = (fsdp_index // share) * HEAD_DIM
        w_cols = jnp.concatenate(
            [
                lax.all_to_all(query_proj, "fsdp", 1, 0, tiled=True),
                lax.dynamic_slice_in_dim(
                    lax.all_gather(key_proj, "fsdp", axis=0, tiled=True), kv_start, HEAD_DIM, 1
                ),
                lax.dynamic_slice_in_dim(
                    lax.all_gather(value_proj, "fsdp", axis=0, tiled=True), kv_start, HEAD_DIM, 1
                ),
            ],
            axis=1,
        )
    w_cols, expert_gate, expert_up, expert_down = lax.optimization_barrier(
        (w_cols, expert_gate, expert_up, expert_down)
    )
    docs_query = jnp.take(doc_rows, local_pos, axis=1)
    docs_key = jnp.take(doc_rows, all_pos, axis=1)
    visible = (all_pos[None, None, :] <= local_pos[None, :, None]) & (
        docs_key[:, None, :] == docs_query[:, :, None]
    )
    projected = matmul(group_input, w_cols)
    query_raw = projected[:, :q_width].reshape(seqs, tokens, heads_dev, HEAD_DIM)
    key_raw = projected[:, q_width : q_width + kv_width].reshape(seqs, tokens, kv_dev, HEAD_DIM)
    value_low = (
        projected[:, q_width + kv_width :]
        .astype(jnp.bfloat16)
        .reshape(seqs, tokens, kv_dev * HEAD_DIM)
    )
    query_scale = rms_scale(query_raw)
    query_normed = query_raw * query_scale
    query_rot = rotate(query_normed * query_gain, cosine, sine_table).astype(jnp.bfloat16)
    key_scale = rms_scale(key_raw)
    key_normed = key_raw * key_scale
    key_rot = (
        rotate(key_normed * key_gain, cosine, sine_table)
        .reshape(seqs, tokens, kv_dev * HEAD_DIM)
        .astype(jnp.bfloat16)
    )
    keys_all = gather_a2a(key_rot, "ctx", ctx_size, 1).reshape(seqs, -1, kv_dev, HEAD_DIM)
    values_all = gather_a2a(value_low, "ctx", ctx_size, 1).reshape(seqs, -1, kv_dev, HEAD_DIM)
    query_groups = query_rot.reshape(seqs, tokens, kv_dev, group_dev, HEAD_DIM)

    def masked_scores():
        scores = contract("stkgd,sjkd->skgtj", query_groups, keys_all) * score_scale
        return jnp.where(visible[:, None, None], scores, NEG_FILL)

    scores = masked_scores()
    peak = jnp.max(scores, axis=-1, keepdims=True)
    expo = jnp.exp(scores - peak)
    total = jnp.sum(expo, axis=-1, keepdims=True)
    probs = (expo / total).astype(jnp.bfloat16)
    log_sums = peak + jnp.log(total)
    attended = (
        contract("skgtj,sjkd->stkgd", probs, values_all)
        .astype(jnp.bfloat16)
        .reshape(group_rows, heads_dev * HEAD_DIM)
    )
    branch_parts = matmul(attended, out_proj).reshape(seqs, tokens, D)
    branch = scatter_sum_a2a(branch_parts.astype(jnp.bfloat16), "fsdp", fsdp_size, 0)[0]
    middle = hidden + branch
    second_scale = rms_scale(middle)
    second_normed = middle * second_scale
    second_input = (second_normed * ffn_gain).astype(jnp.bfloat16)
    w_gate, w_up, w_down, w_router = (
        lax.all_gather(expert_gate, "fsdp", axis=1, tiled=True),
        lax.all_gather(expert_up, "fsdp", axis=1, tiled=True),
        lax.all_gather(expert_down, "fsdp", axis=1, tiled=True),
        gather_a2a(router_proj, "fsdp", fsdp_size, 0),
    )
    logits = matmul(second_input, w_router)
    route_ids = routes[0]
    chosen = jnp.take_along_axis(logits, route_ids, axis=1)
    route_weights = jax.nn.softmax(chosen, axis=-1)
    flat_ids = route_ids.reshape(-1)
    expert_range = jnp.arange(experts, dtype=jnp.int32)
    one_hot = (flat_ids[:, None] == expert_range[None, :]).astype(jnp.int32)
    earlier = jnp.cumsum(one_hot, axis=0) - one_hot
    slot_index = jnp.sum(earlier * one_hot, axis=1)
    target = flat_ids * capacity + slot_index

    def dispatch(route_rows):
        buffer = jnp.zeros((experts * capacity, D), jnp.bfloat16).at[target].set(route_rows)
        return buffer.reshape(ctx_size, local_experts, capacity, D)

    def to_experts(buffer):
        got = lax.all_to_all(buffer, "ctx", 0, 0, tiled=True)
        return got.transpose(1, 0, 2, 3).reshape(local_experts, ctx_size * capacity, D)

    def from_experts(rows):
        parts = rows.reshape(local_experts, ctx_size, capacity, D).transpose(1, 0, 2, 3)
        back = lax.all_to_all(parts, "ctx", 0, 0, tiled=True)
        return back.reshape(experts * capacity, D)

    def collect(returned):
        return jnp.take(returned, target, axis=0)

    received = to_experts(dispatch(jnp.repeat(second_input, TOP, axis=0)))
    gate_val = contract("erd,edf->erf", received, w_gate)
    up_val = contract("erd,edf->erf", received, w_up)
    gate_sig = jax.nn.sigmoid(gate_val)
    hid_low = (gate_val * gate_sig * up_val).astype(jnp.bfloat16)
    expert_out = contract("erf,efd->erd", hid_low, w_down).astype(jnp.bfloat16)
    route_out = (
        collect(from_experts(expert_out))
        .reshape(tokens, TOP, D)
        .astype(jnp.float32)
    )
    layer_out = middle + jnp.einsum("tr,trd->td", route_weights, route_out)
    grad_out = cotangent[0]
    grad_weights = jnp.einsum("td,trd->tr", grad_out, route_out)
    grad_routes = (
        (route_weights[:, :, None] * grad_out[:, None, :])
        .astype(jnp.bfloat16)
        .reshape(tokens * TOP, D)
    )
    grad_expert = to_experts(dispatch(grad_routes))
    grad_hid = contract("erd,efd->erf", grad_expert, w_down)
    down_grad_full = contract("erf,erd->efd", hid_low, grad_expert)
    grad_gate = (grad_hid * up_val * gate_sig * (1.0 + gate_val * (1.0 - gate_sig))).astype(
        jnp.bfloat16
    )
    grad_up = (grad_hid * gate_val * gate_sig).astype(jnp.bfloat16)
    gate_grad_full = contract("erd,erf->edf", received, grad_gate)
    up_grad_full = contract("erd,erf->edf", received, grad_up)
    grad_rows = (
        contract("erf,edf->erd", grad_gate, w_gate) + contract("erf,edf->erd", grad_up, w_up)
    ).astype(jnp.bfloat16)
    grad_copies = collect(from_experts(grad_rows)).reshape(tokens, TOP, D)
    grad_chosen = route_weights * (
        grad_weights - jnp.sum(route_weights * grad_weights, axis=-1, keepdims=True)
    )
    route_hot = (route_ids[:, :, None] == expert_range[None, None, :]).astype(jnp.float32)
    grad_logits = jnp.einsum("tr,tre->te", grad_chosen, route_hot).astype(jnp.bfloat16)
    router_grad_full = contract("td,te->de", second_input, grad_logits)
    grad_second = jnp.sum(grad_copies.astype(jnp.float32), axis=1) + contract(
        "te,de->td", grad_logits, w_router
    )
    grad_middle, ffn_gain_grad = norm_back(grad_second, second_normed, second_scale, ffn_gain)
    grad_middle = grad_middle + grad_out

    grad_branch = gather_a2a(grad_middle.astype(jnp.bfloat16), "fsdp", fsdp_size, 0)
    out_grad_part = contract("tq,td->qd", attended, grad_branch)
    grad_attended = contract("td,qd->tq", grad_branch, out_proj).astype(jnp.bfloat16)
    grad_groups = grad_attended.reshape(seqs, tokens, kv_dev, group_dev, HEAD_DIM)

    probs_back = jnp.exp(masked_scores() - log_sums)
    grad_probs = contract("stkgd,sjkd->skgtj", grad_groups, values_all)
    delta = jnp.sum(probs_back * grad_probs, axis=-1, keepdims=True)
    grad_scores = (probs_back * (grad_probs - delta)).astype(jnp.bfloat16)
    grad_qgroups = contract("skgtj,sjkd->stkgd", grad_scores, keys_all) * score_scale
    grad_kheads = contract("skgtj,stkgd->sjkd", grad_scores, query_groups) * score_scale
    grad_vheads = contract("skgtj,stkgd->sjkd", probs_back.astype(jnp.bfloat16), grad_groups)

    def kv_reduce(grads):
        summed = scatter_sum_a2a(
            grads.reshape(seqs, -1, kv_dev * HEAD_DIM).astype(jnp.bfloat16), "ctx", ctx_size, 1
        )
        total = summed
        for step in range(1, share):
            pairs = [
                (i, (i // share) * share + (i % share + step) % share) for i in range(fsdp_size)
            ]
            total = total + lax.ppermute(summed, "fsdp", pairs)
        return total

    grad_key_rot = kv_reduce(grad_kheads)
    grad_value = kv_reduce(grad_vheads)
    grad_query_rot = grad_qgroups.reshape(seqs, tokens, heads_dev, HEAD_DIM)
    grad_query, query_gain_grad = norm_back(
        rotate_back(grad_query_rot, cosine, sine_table), query_normed, query_scale, query_gain
    )
    grad_key, key_gain_grad = norm_back(
        rotate_back(grad_key_rot.reshape(seqs, tokens, kv_dev, HEAD_DIM), cosine, sine_table),
        key_normed,
        key_scale,
        key_gain,
    )
    if share > 1:
        key_gain_grad = key_gain_grad * (fsdp_index % share == 0).astype(jnp.float32)
    grad_query = grad_query.reshape(group_rows, heads_dev * HEAD_DIM).astype(jnp.bfloat16)
    grad_key = grad_key.reshape(group_rows, kv_dev * HEAD_DIM).astype(jnp.bfloat16)
    grad_value = grad_value.reshape(group_rows, kv_dev * HEAD_DIM).astype(jnp.bfloat16)

    def gather_heads(parts):
        whole = parts.reshape(group_rows, -1)
        if share > 1:
            whole = whole.reshape(group_rows, KV_HEADS, share, HEAD_DIM)[:, :, 0]
            whole = whole.reshape(group_rows, KV_HEADS * HEAD_DIM)
        return whole

    joined = gather_a2a(
        jnp.concatenate([grad_query, grad_key, grad_value], axis=1)[:, None], "fsdp", fsdp_size, 1
    )
    query_all = joined[:, :, :q_width].reshape(group_rows, -1)
    key_all = gather_heads(joined[:, :, q_width : q_width + kv_width])
    value_all = gather_heads(joined[:, :, q_width + kv_width :])
    input_part = lax.dynamic_slice_in_dim(group_input, fsdp_index * d_part, d_part, 1)
    query_grad_part = contract("td,tq->dq", input_part, query_all)
    key_grad_part = contract("td,tq->dq", input_part, key_all)
    value_grad_part = contract("td,tq->dq", input_part, value_all)
    grad_first_cols = (
        contract("tq,dq->td", query_all, query_proj)
        + contract("tq,dq->td", key_all, key_proj)
        + contract("tq,dq->td", value_all, value_proj)
    )
    grad_first = lax.all_to_all(
        grad_first_cols.reshape(seqs, tokens, d_part), "fsdp", 0, 2, tiled=True
    )[0]
    grad_hidden, attn_gain_grad = norm_back(grad_first, first_normed, first_scale, attn_gain)
    grad_hidden = grad_hidden + grad_middle
    gate_grad, up_grad, down_grad = (
        lax.psum_scatter(
            full.astype(jnp.bfloat16), "fsdp", scatter_dimension=1, tiled=True
        ).astype(jnp.float32)
        for full in (gate_grad_full, up_grad_full, down_grad_full)
    )
    router_shard = scatter_sum_a2a(router_grad_full, "fsdp", fsdp_size, 0)
    out_grad = lax.psum(out_grad_part, "ctx")
    query_grad, key_grad, value_grad = (
        lax.psum(part.astype(jnp.bfloat16), "ctx").astype(jnp.float32)
        for part in (query_grad_part, key_grad_part, value_grad_part)
    )
    router_grad = jnp.sum(gather_a2a(router_shard[None], "ctx", ctx_size, 0), axis=0)
    attn_gain_total, query_gain_total, key_gain_total, ffn_gain_total = lax.psum(
        (attn_gain_grad, query_gain_grad, key_gain_grad, ffn_gain_grad), ("ctx", "fsdp")
    )
    return (
        layer_out[None],
        grad_hidden[None],
        attn_gain_total,
        query_grad,
        key_grad,
        value_grad,
        query_gain_total,
        key_gain_total,
        out_grad,
        ffn_gain_total,
        router_grad,
        gate_grad,
        up_grad,
        down_grad,
    )


def solution(mesh):
    placed = (
        P("fsdp", "ctx", None),
        P(),
        P("fsdp", None),
        P("fsdp", "ctx", None),
        P(),
        P("fsdp", None),
        P("fsdp", None),
        P("fsdp", None),
        P(),
        P(),
        P("fsdp", None),
        P(),
        P("fsdp", None),
        P("ctx", "fsdp", None),
        P("ctx", "fsdp", None),
        P("ctx", "fsdp", None),
        P("fsdp", "ctx", None),
    )
    return jax.shard_map(
        per_device,
        mesh=mesh,
        in_specs=placed,
        out_specs=(
            P("fsdp", "ctx", None),
            P("fsdp", "ctx", None),
            P(),
            P("fsdp", None),
            P("fsdp", None),
            P("fsdp", None),
            P(),
            P(),
            P("fsdp", None),
            P(),
            P("fsdp", None),
            P("ctx", "fsdp", None),
            P("ctx", "fsdp", None),
            P("ctx", "fsdp", None),
        ),
        check_vma=False,
    )
```

```python
import jax
import jax.numpy as jnp
from jax import lax
from jax.sharding import PartitionSpec as P


D = 2048
HEADS = 32
KV_HEADS = 4
HEAD_DIM = 128
TOP = 8


EPSILON = 1e-06
ROPE_BASE = 1000000.0
NEG_FILL = -1e30


def matmul(left, right):
    return jnp.dot(left, right, preferred_element_type=jnp.float32)


def contract(form, left, right):
    return jnp.einsum(form, left, right, preferred_element_type=jnp.float32)


def rms_scale(field):
    return lax.rsqrt(jnp.mean(field * field, axis=-1, keepdims=True) + EPSILON)


def rotary(positions):
    halfway = HEAD_DIM // 2
    inverse = ROPE_BASE ** (-2.0 * jnp.arange(halfway, dtype=jnp.float32) / HEAD_DIM)
    angle = positions.astype(jnp.float32)[:, None] * inverse[None, :]
    return (jnp.cos(angle), jnp.sin(angle))


def rotate(field, cosine, sine_table):
    halfway = field.shape[-1] // 2
    former = field[..., :halfway]
    latter = field[..., halfway:]
    cos_b = cosine[:, None, :]
    sin_b = sine_table[:, None, :]
    return jnp.concatenate(
        [former * cos_b - latter * sin_b, latter * cos_b + former * sin_b], axis=-1
    )


def rotate_back(field, cosine, sine_table):
    halfway = field.shape[-1] // 2
    former = field[..., :halfway]
    latter = field[..., halfway:]
    cos_b = cosine[:, None, :]
    sin_b = sine_table[:, None, :]
    return jnp.concatenate(
        [former * cos_b + latter * sin_b, latter * cos_b - former * sin_b], axis=-1
    )


def norm_back(grad, normed, inv_scale, factor):
    lead_axes = tuple(range(grad.ndim - 1))
    factor_grad = jnp.sum(grad * normed, axis=lead_axes)
    scaled = grad * factor
    return (
        inv_scale * (scaled - normed * jnp.mean(scaled * normed, axis=-1, keepdims=True)),
        factor_grad,
    )


def gather_a2a(x, axis_name, size, axis):
    rep = jnp.broadcast_to(x[None], (size,) + x.shape)
    got = jnp.moveaxis(lax.all_to_all(rep, axis_name, 0, 0, tiled=True), 0, axis)
    return got.reshape(x.shape[:axis] + (size * x.shape[axis],) + x.shape[axis + 1 :])


def scatter_sum_a2a(x, axis_name, size, axis):
    parts = x.reshape(x.shape[:axis] + (size, x.shape[axis] // size) + x.shape[axis + 1 :])
    got = lax.all_to_all(parts, axis_name, axis, axis, tiled=True)
    return jnp.sum(got.astype(jnp.float32), axis=axis)


def per_device(
    hidden_in,
    block_map,
    doc_ids,
    routes,
    attn_gain,
    query_proj,
    key_proj,
    value_proj,
    query_gain,
    key_gain,
    out_proj,
    ffn_gain,
    router_proj,
    expert_gate,
    expert_up,
    expert_down,
    cotangent,
):
    tokens = hidden_in.shape[1]
    ctx_size = lax.axis_size("ctx")
    fsdp_size = lax.axis_size("fsdp")
    fsdp_index = lax.axis_index("fsdp")
    local_experts = expert_gate.shape[0]
    experts = local_experts * ctx_size
    capacity = min(tokens, 3 * tokens * TOP // (2 * experts))
    block_len = tokens // 2
    group_size = HEADS // KV_HEADS
    score_scale = HEAD_DIM ** (-0.5)
    heads_dev = HEADS // fsdp_size
    share = max(1, fsdp_size // KV_HEADS)
    kv_dev = max(1, heads_dev // group_size)
    group_dev = heads_dev // kv_dev
    d_part = D // fsdp_size
    seqs = fsdp_size
    group_rows = seqs * tokens

    ctx_index = lax.axis_index("ctx")
    own_blocks = lax.dynamic_slice_in_dim(block_map, 2 * ctx_index, 2, 0)
    offsets = jnp.arange(block_len, dtype=jnp.int32)
    local_pos = (own_blocks[:, None] * block_len + offsets[None, :]).reshape(-1)
    all_pos = (block_map[:, None] * block_len + offsets[None, :]).reshape(-1)
    cosine, sine_table = rotary(local_pos)
    hidden = hidden_in[0]
    first_scale = rms_scale(hidden)
    first_normed = hidden * first_scale
    first_input = (first_normed * attn_gain).astype(jnp.bfloat16)
    q_width, kv_width = heads_dev * HEAD_DIM, kv_dev * HEAD_DIM
    if share == 1:
        blocks = jnp.concatenate(
            [
                query_proj.reshape(d_part, fsdp_size, q_width),
                key_proj.reshape(d_part, fsdp_size, kv_width),
                value_proj.reshape(d_part, fsdp_size, kv_width),
            ],
            axis=2,
        )
        half = d_part // 2
        core = ctx_index % 2
        lanes = 128
        sent_rows = jnp.moveaxis(
            lax.dynamic_slice_in_dim(blocks, core * half, half, 0), 1, 0
        ).reshape(fsdp_size, -1, lanes)
        common = doc_ids.astype(jnp.bfloat16).reshape(-1, lanes)
        payload = jnp.concatenate(
            [sent_rows, jnp.broadcast_to(common[None], (fsdp_size,) + common.shape)], axis=1
        )
        got = lax.all_to_all(payload, "fsdp", 0, 0, tiled=True)
        w_rows = sent_rows.shape[1]
        mine = got[:, :w_rows].reshape(fsdp_size, half, -1)
        doc_rows = got[:, w_rows:].reshape(fsdp_size, -1).astype(jnp.float32)
        group_input = lax.all_gather(first_input, "fsdp", axis=0, tiled=True)
        other = lax.ppermute(mine, "ctx", [(i, i ^ 1) for i in range(ctx_size)])
        w_cols = jnp.where(
            core == 0, jnp.stack([mine, other], axis=1), jnp.stack([other, mine], axis=1)
        ).reshape(D, -1)
    else:
        group_input = gather_a2a(first_input, "fsdp", fsdp_size, 0)
        doc_rows = gather_a2a(doc_ids.astype(jnp.float32), "fsdp", fsdp_size, 0)
        kv_start = (fsdp_index // share) * HEAD_DIM
        w_cols = jnp.concatenate(
            [
                lax.all_to_all(query_proj, "fsdp", 1, 0, tiled=True),
                lax.dynamic_slice_in_dim(
                    lax.all_gather(key_proj, "fsdp", axis=0, tiled=True), kv_start, HEAD_DIM, 1
                ),
                lax.dynamic_slice_in_dim(
                    lax.all_gather(value_proj, "fsdp", axis=0, tiled=True), kv_start, HEAD_DIM, 1
                ),
            ],
            axis=1,
        )
    w_cols, expert_gate, expert_up, expert_down = lax.optimization_barrier(
        (w_cols, expert_gate, expert_up, expert_down)
    )
    docs_query = jnp.take(doc_rows, local_pos, axis=1)
    docs_key = jnp.take(doc_rows, all_pos, axis=1)
    visible = (all_pos[None, None, :] <= local_pos[None, :, None]) & (
        docs_key[:, None, :] == docs_query[:, :, None]
    )
    projected = matmul(group_input, w_cols)
    query_raw = projected[:, :q_width].reshape(seqs, tokens, heads_dev, HEAD_DIM)
    key_raw = projected[:, q_width : q_width + kv_width].reshape(seqs, tokens, kv_dev, HEAD_DIM)
    value_low = (
        projected[:, q_width + kv_width :]
        .astype(jnp.bfloat16)
        .reshape(seqs, tokens, kv_dev * HEAD_DIM)
    )
    query_scale = rms_scale(query_raw)
    query_normed = query_raw * query_scale
    query_rot = rotate(query_normed * query_gain, cosine, sine_table).astype(jnp.bfloat16)
    key_scale = rms_scale(key_raw)
    key_normed = key_raw * key_scale
    key_rot = (
        rotate(key_normed * key_gain, cosine, sine_table)
        .reshape(seqs, tokens, kv_dev * HEAD_DIM)
        .astype(jnp.bfloat16)
    )
    keys_all = gather_a2a(key_rot, "ctx", ctx_size, 1).reshape(seqs, -1, kv_dev, HEAD_DIM)
    values_all = gather_a2a(value_low, "ctx", ctx_size, 1).reshape(seqs, -1, kv_dev, HEAD_DIM)
    query_groups = query_rot.reshape(seqs, tokens, kv_dev, group_dev, HEAD_DIM)

    def masked_scores():
        scores = contract("stkgd,sjkd->skgtj", query_groups, keys_all) * score_scale
        return jnp.where(visible[:, None, None], scores, NEG_FILL)

    scores = masked_scores()
    peak = jnp.max(scores, axis=-1, keepdims=True)
    expo = jnp.exp(scores - peak)
    total = jnp.sum(expo, axis=-1, keepdims=True)
    probs = (expo / total).astype(jnp.bfloat16)
    log_sums = peak + jnp.log(total)
    attended = (
        contract("skgtj,sjkd->stkgd", probs, values_all)
        .astype(jnp.bfloat16)
        .reshape(group_rows, heads_dev * HEAD_DIM)
    )
    branch_parts = matmul(attended, out_proj).reshape(seqs, tokens, D)
    branch = scatter_sum_a2a(branch_parts.astype(jnp.bfloat16), "fsdp", fsdp_size, 0)[0]
    middle = hidden + branch
    second_scale = rms_scale(middle)
    second_normed = middle * second_scale
    second_input = (second_normed * ffn_gain).astype(jnp.bfloat16)
    w_gate, w_up, w_down, w_router = (
        lax.all_gather(expert_gate, "fsdp", axis=1, tiled=True),
        lax.all_gather(expert_up, "fsdp", axis=1, tiled=True),
        lax.all_gather(expert_down, "fsdp", axis=1, tiled=True),
        gather_a2a(router_proj, "fsdp", fsdp_size, 0),
    )
    logits = matmul(second_input, w_router)
    route_ids = routes[0]
    chosen = jnp.take_along_axis(logits, route_ids, axis=1)
    route_weights = jax.nn.softmax(chosen, axis=-1)
    flat_ids = route_ids.reshape(-1)
    expert_range = jnp.arange(experts, dtype=jnp.int32)
    one_hot = (flat_ids[:, None] == expert_range[None, :]).astype(jnp.int32)
    earlier = jnp.cumsum(one_hot, axis=0) - one_hot
    slot_index = jnp.sum(earlier * one_hot, axis=1)
    target = flat_ids * capacity + slot_index

    def dispatch(route_rows):
        buffer = jnp.zeros((experts * capacity, D), jnp.bfloat16).at[target].set(route_rows)
        return buffer.reshape(ctx_size, local_experts, capacity, D)

    def to_experts(buffer):
        got = lax.all_to_all(buffer, "ctx", 0, 0, tiled=True)
        return got.transpose(1, 0, 2, 3).reshape(local_experts, ctx_size * capacity, D)

    def from_experts(rows):
        parts = rows.reshape(local_experts, ctx_size, capacity, D).transpose(1, 0, 2, 3)
        back = lax.all_to_all(parts, "ctx", 0, 0, tiled=True)
        return back.reshape(experts * capacity, D)

    def collect(returned):
        return jnp.take(returned, target, axis=0)

    received = to_experts(dispatch(jnp.repeat(second_input, TOP, axis=0)))
    gate_val = contract("erd,edf->erf", received, w_gate)
    up_val = contract("erd,edf->erf", received, w_up)
    gate_sig = jax.nn.sigmoid(gate_val)
    hid_low = (gate_val * gate_sig * up_val).astype(jnp.bfloat16)
    expert_out = contract("erf,efd->erd", hid_low, w_down).astype(jnp.bfloat16)
    route_out = (
        collect(from_experts(expert_out))
        .reshape(tokens, TOP, D)
        .astype(jnp.float32)
    )
    layer_out = middle + jnp.einsum("tr,trd->td", route_weights, route_out)
    grad_out = cotangent[0]
    grad_weights = jnp.einsum("td,trd->tr", grad_out, route_out)
    grad_routes = (
        (route_weights[:, :, None] * grad_out[:, None, :])
        .astype(jnp.bfloat16)
        .reshape(tokens * TOP, D)
    )
    grad_expert = to_experts(dispatch(grad_routes))
    grad_hid = contract("erd,efd->erf", grad_expert, w_down)
    down_grad_full = contract("erf,erd->efd", hid_low, grad_expert)
    grad_gate = (grad_hid * up_val * gate_sig * (1.0 + gate_val * (1.0 - gate_sig))).astype(
        jnp.bfloat16
    )
    grad_up = (grad_hid * gate_val * gate_sig).astype(jnp.bfloat16)
    gate_grad_full = contract("erd,erf->edf", received, grad_gate)
    up_grad_full = contract("erd,erf->edf", received, grad_up)
    grad_rows = (
        contract("erf,edf->erd", grad_gate, w_gate) + contract("erf,edf->erd", grad_up, w_up)
    ).astype(jnp.bfloat16)
    grad_copies = collect(from_experts(grad_rows)).reshape(tokens, TOP, D)
    grad_chosen = route_weights * (
        grad_weights - jnp.sum(route_weights * grad_weights, axis=-1, keepdims=True)
    )
    route_hot = (route_ids[:, :, None] == expert_range[None, None, :]).astype(jnp.float32)
    grad_logits = jnp.einsum("tr,tre->te", grad_chosen, route_hot).astype(jnp.bfloat16)
    router_grad_full = contract("td,te->de", second_input, grad_logits)
    grad_second = jnp.sum(grad_copies.astype(jnp.float32), axis=1) + contract(
        "te,de->td", grad_logits, w_router
    )
    grad_middle, ffn_gain_grad = norm_back(grad_second, second_normed, second_scale, ffn_gain)
    grad_middle = grad_middle + grad_out

    grad_branch = gather_a2a(grad_middle.astype(jnp.bfloat16), "fsdp", fsdp_size, 0)
    out_grad_part = contract("tq,td->qd", attended, grad_branch)
    grad_attended = contract("td,qd->tq", grad_branch, out_proj).astype(jnp.bfloat16)
    grad_groups = grad_attended.reshape(seqs, tokens, kv_dev, group_dev, HEAD_DIM)

    probs_back = jnp.exp(masked_scores() - log_sums)
    grad_probs = contract("stkgd,sjkd->skgtj", grad_groups, values_all)
    delta = jnp.sum(probs_back * grad_probs, axis=-1, keepdims=True)
    grad_scores = (probs_back * (grad_probs - delta)).astype(jnp.bfloat16)
    grad_qgroups = contract("skgtj,sjkd->stkgd", grad_scores, keys_all) * score_scale
    grad_kheads = contract("skgtj,stkgd->sjkd", grad_scores, query_groups) * score_scale
    grad_vheads = contract("skgtj,stkgd->sjkd", probs_back.astype(jnp.bfloat16), grad_groups)

    def kv_reduce(grads):
        summed = scatter_sum_a2a(
            grads.reshape(seqs, -1, kv_dev * HEAD_DIM).astype(jnp.bfloat16), "ctx", ctx_size, 1
        )
        total = summed
        for step in range(1, share):
            pairs = [
                (i, (i // share) * share + (i % share + step) % share) for i in range(fsdp_size)
            ]
            total = total + lax.ppermute(summed, "fsdp", pairs)
        return total

    grad_key_rot = kv_reduce(grad_kheads)
    grad_value = kv_reduce(grad_vheads)
    grad_query_rot = grad_qgroups.reshape(seqs, tokens, heads_dev, HEAD_DIM)
    grad_query, query_gain_grad = norm_back(
        rotate_back(grad_query_rot, cosine, sine_table), query_normed, query_scale, query_gain
    )
    grad_key, key_gain_grad = norm_back(
        rotate_back(grad_key_rot.reshape(seqs, tokens, kv_dev, HEAD_DIM), cosine, sine_table),
        key_normed,
        key_scale,
        key_gain,
    )
    if share > 1:
        key_gain_grad = key_gain_grad * (fsdp_index % share == 0).astype(jnp.float32)
    grad_query = grad_query.reshape(group_rows, heads_dev * HEAD_DIM).astype(jnp.bfloat16)
    grad_key = grad_key.reshape(group_rows, kv_dev * HEAD_DIM).astype(jnp.bfloat16)
    grad_value = grad_value.reshape(group_rows, kv_dev * HEAD_DIM).astype(jnp.bfloat16)

    def gather_heads(parts):
        whole = parts.reshape(group_rows, -1)
        if share > 1:
            whole = whole.reshape(group_rows, KV_HEADS, share, HEAD_DIM)[:, :, 0]
            whole = whole.reshape(group_rows, KV_HEADS * HEAD_DIM)
        return whole

    joined = gather_a2a(
        jnp.concatenate([grad_query, grad_key, grad_value], axis=1)[:, None], "fsdp", fsdp_size, 1
    )
    query_all = joined[:, :, :q_width].reshape(group_rows, -1)
    key_all = gather_heads(joined[:, :, q_width : q_width + kv_width])
    value_all = gather_heads(joined[:, :, q_width + kv_width :])
    input_part = lax.dynamic_slice_in_dim(group_input, fsdp_index * d_part, d_part, 1)
    query_grad_part = contract("td,tq->dq", input_part, query_all)
    key_grad_part = contract("td,tq->dq", input_part, key_all)
    value_grad_part = contract("td,tq->dq", input_part, value_all)
    grad_first_cols = (
        contract("tq,dq->td", query_all, query_proj)
        + contract("tq,dq->td", key_all, key_proj)
        + contract("tq,dq->td", value_all, value_proj)
    )
    grad_first = lax.all_to_all(
        grad_first_cols.reshape(seqs, tokens, d_part), "fsdp", 0, 2, tiled=True
    )[0]
    grad_hidden, attn_gain_grad = norm_back(grad_first, first_normed, first_scale, attn_gain)
    grad_hidden = grad_hidden + grad_middle
    gate_grad, up_grad, down_grad = (
        lax.psum_scatter(
            full.astype(jnp.bfloat16), "fsdp", scatter_dimension=1, tiled=True
        ).astype(jnp.float32)
        for full in (gate_grad_full, up_grad_full, down_grad_full)
    )
    router_shard = scatter_sum_a2a(router_grad_full, "fsdp", fsdp_size, 0)
    out_grad = lax.psum(out_grad_part, "ctx")
    query_grad, key_grad, value_grad = (
        lax.psum(part.astype(jnp.bfloat16), "ctx").astype(jnp.float32)
        for part in (query_grad_part, key_grad_part, value_grad_part)
    )
    router_grad = jnp.sum(gather_a2a(router_shard[None], "ctx", ctx_size, 0), axis=0)
    attn_gain_total, query_gain_total, key_gain_total, ffn_gain_total = lax.psum(
        (attn_gain_grad, query_gain_grad, key_gain_grad, ffn_gain_grad), ("ctx", "fsdp")
    )
    return (
        layer_out[None],
        grad_hidden[None],
        attn_gain_total,
        query_grad,
        key_grad,
        value_grad,
        query_gain_total,
        key_gain_total,
        out_grad,
        ffn_gain_total,
        router_grad,
        gate_grad,
        up_grad,
        down_grad,
    )


def solution(mesh):
    placed = (
        P("fsdp", "ctx", None),
        P(),
        P("fsdp", None),
        P("fsdp", "ctx", None),
        P(),
        P("fsdp", None),
        P("fsdp", None),
        P("fsdp", None),
        P(),
        P(),
        P("fsdp", None),
        P(),
        P("fsdp", None),
        P("ctx", "fsdp", None),
        P("ctx", "fsdp", None),
        P("ctx", "fsdp", None),
        P("fsdp", "ctx", None),
    )
    return jax.shard_map(
        per_device,
        mesh=mesh,
        in_specs=placed,
        out_specs=(
            P("fsdp", "ctx", None),
            P("fsdp", "ctx", None),
            P(),
            P("fsdp", None),
            P("fsdp", None),
            P("fsdp", None),
            P(),
            P(),
            P("fsdp", None),
            P(),
            P("fsdp", None),
            P("ctx", "fsdp", None),
            P("ctx", "fsdp", None),
            P("ctx", "fsdp", None),
        ),
        check_vma=False,
    )
```

```python
import jax
import jax.numpy as jnp
from jax import lax
from jax.sharding import PartitionSpec as P


D = 2048
HEADS = 32
KV_HEADS = 4
HEAD_DIM = 128
TOP = 8


EPSILON = 1e-06
ROPE_BASE = 1000000.0
NEG_FILL = -1e30


def matmul(left, right):
    return jnp.dot(left, right, preferred_element_type=jnp.float32)


def contract(form, left, right):
    return jnp.einsum(form, left, right, preferred_element_type=jnp.float32)


def rms_scale(field):
    return lax.rsqrt(jnp.mean(field * field, axis=-1, keepdims=True) + EPSILON)


def rotary(positions):
    halfway = HEAD_DIM // 2
    inverse = ROPE_BASE ** (-2.0 * jnp.arange(halfway, dtype=jnp.float32) / HEAD_DIM)
    angle = positions.astype(jnp.float32)[:, None] * inverse[None, :]
    return (jnp.cos(angle), jnp.sin(angle))


def rotate(field, cosine, sine_table):
    halfway = field.shape[-1] // 2
    former = field[..., :halfway]
    latter = field[..., halfway:]
    cos_b = cosine[:, None, :]
    sin_b = sine_table[:, None, :]
    return jnp.concatenate(
        [former * cos_b - latter * sin_b, latter * cos_b + former * sin_b], axis=-1
    )


def rotate_back(field, cosine, sine_table):
    halfway = field.shape[-1] // 2
    former = field[..., :halfway]
    latter = field[..., halfway:]
    cos_b = cosine[:, None, :]
    sin_b = sine_table[:, None, :]
    return jnp.concatenate(
        [former * cos_b + latter * sin_b, latter * cos_b - former * sin_b], axis=-1
    )


def norm_back(grad, normed, inv_scale, factor):
    lead_axes = tuple(range(grad.ndim - 1))
    factor_grad = jnp.sum(grad * normed, axis=lead_axes)
    scaled = grad * factor
    return (
        inv_scale * (scaled - normed * jnp.mean(scaled * normed, axis=-1, keepdims=True)),
        factor_grad,
    )


def gather_a2a(x, axis_name, size, axis):
    rep = jnp.broadcast_to(x[None], (size,) + x.shape)
    got = jnp.moveaxis(lax.all_to_all(rep, axis_name, 0, 0, tiled=True), 0, axis)
    return got.reshape(x.shape[:axis] + (size * x.shape[axis],) + x.shape[axis + 1 :])


def scatter_sum_a2a(x, axis_name, size, axis):
    parts = x.reshape(x.shape[:axis] + (size, x.shape[axis] // size) + x.shape[axis + 1 :])
    got = lax.all_to_all(parts, axis_name, axis, axis, tiled=True)
    return jnp.sum(got.astype(jnp.float32), axis=axis)


def per_device(
    hidden_in,
    block_map,
    doc_ids,
    routes,
    attn_gain,
    query_proj,
    key_proj,
    value_proj,
    query_gain,
    key_gain,
    out_proj,
    ffn_gain,
    router_proj,
    expert_gate,
    expert_up,
    expert_down,
    cotangent,
):
    tokens = hidden_in.shape[1]
    ctx_size = lax.axis_size("ctx")
    fsdp_size = lax.axis_size("fsdp")
    fsdp_index = lax.axis_index("fsdp")
    local_experts = expert_gate.shape[0]
    experts = local_experts * ctx_size
    capacity = min(tokens, 3 * tokens * TOP // (2 * experts))
    block_len = tokens // 2
    group_size = HEADS // KV_HEADS
    score_scale = HEAD_DIM ** (-0.5)
    heads_dev = HEADS // fsdp_size
    share = max(1, fsdp_size // KV_HEADS)
    kv_dev = max(1, heads_dev // group_size)
    group_dev = heads_dev // kv_dev
    d_part = D // fsdp_size
    seqs = fsdp_size
    group_rows = seqs * tokens

    ctx_index = lax.axis_index("ctx")
    own_blocks = lax.dynamic_slice_in_dim(block_map, 2 * ctx_index, 2, 0)
    offsets = jnp.arange(block_len, dtype=jnp.int32)
    local_pos = (own_blocks[:, None] * block_len + offsets[None, :]).reshape(-1)
    all_pos = (block_map[:, None] * block_len + offsets[None, :]).reshape(-1)
    cosine, sine_table = rotary(local_pos)
    hidden = hidden_in[0]
    first_scale = rms_scale(hidden)
    first_normed = hidden * first_scale
    first_input = (first_normed * attn_gain).astype(jnp.bfloat16)
    q_width, kv_width = heads_dev * HEAD_DIM, kv_dev * HEAD_DIM
    if share == 1:
        blocks = jnp.concatenate(
            [
                query_proj.reshape(d_part, fsdp_size, q_width),
                key_proj.reshape(d_part, fsdp_size, kv_width),
                value_proj.reshape(d_part, fsdp_size, kv_width),
            ],
            axis=2,
        )
        half = d_part // 2
        core = ctx_index % 2
        lanes = 128
        sent_rows = jnp.moveaxis(
            lax.dynamic_slice_in_dim(blocks, core * half, half, 0), 1, 0
        ).reshape(fsdp_size, -1, lanes)
        common = doc_ids.astype(jnp.bfloat16).reshape(-1, lanes)
        payload = jnp.concatenate(
            [sent_rows, jnp.broadcast_to(common[None], (fsdp_size,) + common.shape)], axis=1
        )
        got = lax.all_to_all(payload, "fsdp", 0, 0, tiled=True)
        w_rows = sent_rows.shape[1]
        mine = got[:, :w_rows].reshape(fsdp_size, half, -1)
        doc_rows = got[:, w_rows:].reshape(fsdp_size, -1).astype(jnp.float32)
        group_input = lax.all_gather(first_input, "fsdp", axis=0, tiled=True)
        other = lax.ppermute(mine, "ctx", [(i, i ^ 1) for i in range(ctx_size)])
        w_cols = jnp.where(
            core == 0, jnp.stack([mine, other], axis=1), jnp.stack([other, mine], axis=1)
        ).reshape(D, -1)
    else:
        group_input = gather_a2a(first_input, "fsdp", fsdp_size, 0)
        doc_rows = gather_a2a(doc_ids.astype(jnp.float32), "fsdp", fsdp_size, 0)
        kv_start = (fsdp_index // share) * HEAD_DIM
        w_cols = jnp.concatenate(
            [
                lax.all_to_all(query_proj, "fsdp", 1, 0, tiled=True),
                lax.dynamic_slice_in_dim(
                    lax.all_gather(key_proj, "fsdp", axis=0, tiled=True), kv_start, HEAD_DIM, 1
                ),
                lax.dynamic_slice_in_dim(
                    lax.all_gather(value_proj, "fsdp", axis=0, tiled=True), kv_start, HEAD_DIM, 1
                ),
            ],
            axis=1,
        )
    w_cols, expert_gate, expert_up, expert_down = lax.optimization_barrier(
        (w_cols, expert_gate, expert_up, expert_down)
    )
    docs_query = jnp.take(doc_rows, local_pos, axis=1)
    docs_key = jnp.take(doc_rows, all_pos, axis=1)
    visible = (all_pos[None, None, :] <= local_pos[None, :, None]) & (
        docs_key[:, None, :] == docs_query[:, :, None]
    )
    projected = matmul(group_input, w_cols)
    query_raw = projected[:, :q_width].reshape(seqs, tokens, heads_dev, HEAD_DIM)
    key_raw = projected[:, q_width : q_width + kv_width].reshape(seqs, tokens, kv_dev, HEAD_DIM)
    value_low = (
        projected[:, q_width + kv_width :]
        .astype(jnp.bfloat16)
        .reshape(seqs, tokens, kv_dev * HEAD_DIM)
    )
    query_scale = rms_scale(query_raw)
    query_normed = query_raw * query_scale
    query_rot = rotate(query_normed * query_gain, cosine, sine_table).astype(jnp.bfloat16)
    key_scale = rms_scale(key_raw)
    key_normed = key_raw * key_scale
    key_rot = (
        rotate(key_normed * key_gain, cosine, sine_table)
        .reshape(seqs, tokens, kv_dev * HEAD_DIM)
        .astype(jnp.bfloat16)
    )
    keys_all = gather_a2a(key_rot, "ctx", ctx_size, 1).reshape(seqs, -1, kv_dev, HEAD_DIM)
    values_all = gather_a2a(value_low, "ctx", ctx_size, 1).reshape(seqs, -1, kv_dev, HEAD_DIM)
    query_groups = query_rot.reshape(seqs, tokens, kv_dev, group_dev, HEAD_DIM)

    def masked_scores():
        scores = contract("stkgd,sjkd->skgtj", query_groups, keys_all) * score_scale
        return jnp.where(visible[:, None, None], scores, NEG_FILL)

    scores = masked_scores()
    peak = jnp.max(scores, axis=-1, keepdims=True)
    expo = jnp.exp(scores - peak)
    total = jnp.sum(expo, axis=-1, keepdims=True)
    probs_full = expo / total
    probs = probs_full.astype(jnp.bfloat16)
    attended = (
        contract("skgtj,sjkd->stkgd", probs, values_all)
        .astype(jnp.bfloat16)
        .reshape(group_rows, heads_dev * HEAD_DIM)
    )
    branch_parts = matmul(attended, out_proj).reshape(seqs, tokens, D)
    branch = scatter_sum_a2a(branch_parts.astype(jnp.bfloat16), "fsdp", fsdp_size, 0)[0]
    middle = hidden + branch
    second_scale = rms_scale(middle)
    second_normed = middle * second_scale
    second_input = (second_normed * ffn_gain).astype(jnp.bfloat16)
    shards = (expert_gate, expert_up, expert_down)
    packed = jnp.concatenate([w.reshape(w.shape[0], -1, 128) for w in shards], axis=1)
    gathered = lax.all_gather(packed, "fsdp", axis=0, tiled=False)
    unpacked, offset = [], 0
    for w in shards:
        size = w.shape[1] * w.shape[2] // 128
        piece = gathered[:, :, offset : offset + size].reshape((fsdp_size,) + w.shape)
        unpacked.append(
            jnp.moveaxis(piece, 0, 1).reshape(w.shape[0], fsdp_size * w.shape[1], w.shape[2])
        )
        offset += size
    w_gate, w_up, w_down = unpacked
    w_router = gather_a2a(router_proj, "fsdp", fsdp_size, 0)
    logits = matmul(second_input, w_router)
    route_ids = routes[0]
    chosen = jnp.take_along_axis(logits, route_ids, axis=1)
    route_weights = jax.nn.softmax(chosen, axis=-1)
    flat_ids = route_ids.reshape(-1)
    expert_range = jnp.arange(experts, dtype=jnp.int32)
    one_hot = (flat_ids[:, None] == expert_range[None, :]).astype(jnp.int32)
    earlier = jnp.cumsum(one_hot, axis=0) - one_hot
    slot_index = jnp.sum(earlier * one_hot, axis=1)
    target = flat_ids * capacity + slot_index

    def dispatch(route_rows):
        buffer = jnp.zeros((experts * capacity, D), jnp.bfloat16).at[target].set(route_rows)
        return buffer.reshape(ctx_size, local_experts, capacity, D)

    def to_experts(buffer):
        got = lax.all_to_all(buffer, "ctx", 0, 0, tiled=True)
        return got.transpose(1, 0, 2, 3).reshape(local_experts, ctx_size * capacity, D)

    def from_experts(rows):
        parts = rows.reshape(local_experts, ctx_size, capacity, D).transpose(1, 0, 2, 3)
        back = lax.all_to_all(parts, "ctx", 0, 0, tiled=True)
        return back.reshape(experts * capacity, D)

    def collect(returned):
        return jnp.take(returned, target, axis=0)

    received = to_experts(dispatch(jnp.repeat(second_input, TOP, axis=0)))
    gate_val = contract("erd,edf->erf", received, w_gate)
    up_val = contract("erd,edf->erf", received, w_up)
    gate_sig = jax.nn.sigmoid(gate_val)
    hid_low = (gate_val * gate_sig * up_val).astype(jnp.bfloat16)
    expert_out = contract("erf,efd->erd", hid_low, w_down).astype(jnp.bfloat16)
    route_out = (
        collect(from_experts(expert_out))
        .reshape(tokens, TOP, D)
        .astype(jnp.float32)
    )
    layer_out = middle + jnp.einsum("tr,trd->td", route_weights, route_out)
    grad_out = cotangent[0]
    grad_weights = jnp.einsum("td,trd->tr", grad_out, route_out)
    grad_routes = (
        (route_weights[:, :, None] * grad_out[:, None, :])
        .astype(jnp.bfloat16)
        .reshape(tokens * TOP, D)
    )
    grad_expert = to_experts(dispatch(grad_routes))
    grad_hid = contract("erd,efd->erf", grad_expert, w_down)
    down_grad_full = contract("erf,erd->efd", hid_low, grad_expert)
    grad_gate = (grad_hid * up_val * gate_sig * (1.0 + gate_val * (1.0 - gate_sig))).astype(
        jnp.bfloat16
    )
    grad_up = (grad_hid * gate_val * gate_sig).astype(jnp.bfloat16)
    gate_grad_full = contract("erd,erf->edf", received, grad_gate)
    up_grad_full = contract("erd,erf->edf", received, grad_up)
    grad_rows = (
        contract("erf,edf->erd", grad_gate, w_gate) + contract("erf,edf->erd", grad_up, w_up)
    ).astype(jnp.bfloat16)
    grad_copies = collect(from_experts(grad_rows)).reshape(tokens, TOP, D)
    grad_chosen = route_weights * (
        grad_weights - jnp.sum(route_weights * grad_weights, axis=-1, keepdims=True)
    )
    route_hot = (route_ids[:, :, None] == expert_range[None, None, :]).astype(jnp.float32)
    grad_logits = jnp.einsum("tr,tre->te", grad_chosen, route_hot).astype(jnp.bfloat16)
    router_grad_full = contract("td,te->de", second_input, grad_logits)
    grad_second = jnp.sum(grad_copies.astype(jnp.float32), axis=1) + contract(
        "te,de->td", grad_logits, w_router
    )
    grad_middle, ffn_gain_grad = norm_back(grad_second, second_normed, second_scale, ffn_gain)
    grad_middle = grad_middle + grad_out

    grad_branch = gather_a2a(grad_middle.astype(jnp.bfloat16), "fsdp", fsdp_size, 0)
    out_grad_part = contract("tq,td->qd", attended, grad_branch)
    grad_attended = contract("td,qd->tq", grad_branch, out_proj).astype(jnp.bfloat16)
    grad_groups = grad_attended.reshape(seqs, tokens, kv_dev, group_dev, HEAD_DIM)

    probs_back = probs_full
    grad_probs = contract("stkgd,sjkd->skgtj", grad_groups, values_all)
    delta = jnp.sum(probs_back * grad_probs, axis=-1, keepdims=True)
    grad_scores = (probs_back * (grad_probs - delta)).astype(jnp.bfloat16)
    grad_qgroups = contract("skgtj,sjkd->stkgd", grad_scores, keys_all) * score_scale
    grad_kheads = contract("skgtj,stkgd->sjkd", grad_scores, query_groups) * score_scale
    grad_vheads = contract("skgtj,stkgd->sjkd", probs_back.astype(jnp.bfloat16), grad_groups)

    def kv_reduce(grads):
        summed = scatter_sum_a2a(
            grads.reshape(seqs, -1, kv_dev * HEAD_DIM).astype(jnp.bfloat16), "ctx", ctx_size, 1
        )
        total = summed
        for step in range(1, share):
            pairs = [
                (i, (i // share) * share + (i % share + step) % share) for i in range(fsdp_size)
            ]
            total = total + lax.ppermute(summed, "fsdp", pairs)
        return total

    grad_key_rot = kv_reduce(grad_kheads)
    grad_value = kv_reduce(grad_vheads)
    grad_query_rot = grad_qgroups.reshape(seqs, tokens, heads_dev, HEAD_DIM)
    grad_query, query_gain_grad = norm_back(
        rotate_back(grad_query_rot, cosine, sine_table), query_normed, query_scale, query_gain
    )
    grad_key, key_gain_grad = norm_back(
        rotate_back(grad_key_rot.reshape(seqs, tokens, kv_dev, HEAD_DIM), cosine, sine_table),
        key_normed,
        key_scale,
        key_gain,
    )
    if share > 1:
        key_gain_grad = key_gain_grad * (fsdp_index % share == 0).astype(jnp.float32)
    grad_query = grad_query.reshape(group_rows, heads_dev * HEAD_DIM).astype(jnp.bfloat16)
    grad_key = grad_key.reshape(group_rows, kv_dev * HEAD_DIM).astype(jnp.bfloat16)
    grad_value = grad_value.reshape(group_rows, kv_dev * HEAD_DIM).astype(jnp.bfloat16)

    def gather_heads(parts):
        whole = parts.reshape(group_rows, -1)
        if share > 1:
            whole = whole.reshape(group_rows, KV_HEADS, share, HEAD_DIM)[:, :, 0]
            whole = whole.reshape(group_rows, KV_HEADS * HEAD_DIM)
        return whole

    joined = gather_a2a(
        jnp.concatenate([grad_query, grad_key, grad_value], axis=1)[:, None], "fsdp", fsdp_size, 1
    )
    query_all = joined[:, :, :q_width].reshape(group_rows, -1)
    key_all = gather_heads(joined[:, :, q_width : q_width + kv_width])
    value_all = gather_heads(joined[:, :, q_width + kv_width :])
    input_part = lax.dynamic_slice_in_dim(group_input, fsdp_index * d_part, d_part, 1)
    query_grad_part = contract("td,tq->dq", input_part, query_all)
    key_grad_part = contract("td,tq->dq", input_part, key_all)
    value_grad_part = contract("td,tq->dq", input_part, value_all)
    grad_first_cols = (
        contract("tq,dq->td", query_all, query_proj)
        + contract("tq,dq->td", key_all, key_proj)
        + contract("tq,dq->td", value_all, value_proj)
    )
    grad_first = lax.all_to_all(
        grad_first_cols.reshape(seqs, tokens, d_part), "fsdp", 0, 2, tiled=True
    )[0]
    grad_hidden, attn_gain_grad = norm_back(grad_first, first_normed, first_scale, attn_gain)
    grad_hidden = grad_hidden + grad_middle

    def by_owner(full):
        count, rows, cols = full.shape
        part = full.astype(jnp.bfloat16).reshape(count, fsdp_size, rows // fsdp_size, cols)
        return jnp.moveaxis(part, 1, 0).reshape(fsdp_size, count, -1, 128)

    fulls = (gate_grad_full, up_grad_full, down_grad_full)
    summed = lax.psum_scatter(
        jnp.concatenate([by_owner(g) for g in fulls], axis=2),
        "fsdp",
        scatter_dimension=0,
        tiled=True,
    )[0]
    owned, offset = [], 0
    for shard in shards:
        size = shard.shape[1] * shard.shape[2] // 128
        owned.append(summed[:, offset : offset + size].reshape(shard.shape).astype(jnp.float32))
        offset += size
    gate_grad, up_grad, down_grad = owned
    router_shard = scatter_sum_a2a(router_grad_full, "fsdp", fsdp_size, 0)
    out_grad = lax.psum(out_grad_part, "ctx")
    query_grad, key_grad, value_grad = (
        lax.psum(part.astype(jnp.bfloat16), "ctx").astype(jnp.float32)
        for part in (query_grad_part, key_grad_part, value_grad_part)
    )
    router_grad = jnp.sum(gather_a2a(router_shard[None], "ctx", ctx_size, 0), axis=0)
    attn_gain_total, query_gain_total, key_gain_total, ffn_gain_total = lax.psum(
        (attn_gain_grad, query_gain_grad, key_gain_grad, ffn_gain_grad), ("ctx", "fsdp")
    )
    return (
        layer_out[None],
        grad_hidden[None],
        attn_gain_total,
        query_grad,
        key_grad,
        value_grad,
        query_gain_total,
        key_gain_total,
        out_grad,
        ffn_gain_total,
        router_grad,
        gate_grad,
        up_grad,
        down_grad,
    )


def solution(mesh):
    placed = (
        P("fsdp", "ctx", None),
        P(),
        P("fsdp", None),
        P("fsdp", "ctx", None),
        P(),
        P("fsdp", None),
        P("fsdp", None),
        P("fsdp", None),
        P(),
        P(),
        P("fsdp", None),
        P(),
        P("fsdp", None),
        P("ctx", "fsdp", None),
        P("ctx", "fsdp", None),
        P("ctx", "fsdp", None),
        P("fsdp", "ctx", None),
    )
    return jax.shard_map(
        per_device,
        mesh=mesh,
        in_specs=placed,
        out_specs=(
            P("fsdp", "ctx", None),
            P("fsdp", "ctx", None),
            P(),
            P("fsdp", None),
            P("fsdp", None),
            P("fsdp", None),
            P(),
            P(),
            P("fsdp", None),
            P(),
            P("fsdp", None),
            P("ctx", "fsdp", None),
            P("ctx", "fsdp", None),
            P("ctx", "fsdp", None),
        ),
        check_vma=False,
    )
```

```python
import jax
import jax.numpy as jnp
from jax import lax
from jax.sharding import PartitionSpec as P


D = 2048
HEADS = 32
KV_HEADS = 4
HEAD_DIM = 128
TOP = 8


EPSILON = 1e-06
ROPE_BASE = 1000000.0
NEG_FILL = -1e30


def matmul(left, right):
    return jnp.dot(left, right, preferred_element_type=jnp.float32)


def contract(form, left, right):
    return jnp.einsum(form, left, right, preferred_element_type=jnp.float32)


def rms_scale(field):
    return lax.rsqrt(jnp.mean(field * field, axis=-1, keepdims=True) + EPSILON)


def rotary(positions):
    halfway = HEAD_DIM // 2
    inverse = ROPE_BASE ** (-2.0 * jnp.arange(halfway, dtype=jnp.float32) / HEAD_DIM)
    angle = positions.astype(jnp.float32)[:, None] * inverse[None, :]
    return (jnp.cos(angle), jnp.sin(angle))


def rotate(field, cosine, sine_table):
    halfway = field.shape[-1] // 2
    former = field[..., :halfway]
    latter = field[..., halfway:]
    cos_b = cosine[:, None, :]
    sin_b = sine_table[:, None, :]
    return jnp.concatenate(
        [former * cos_b - latter * sin_b, latter * cos_b + former * sin_b], axis=-1
    )


def rotate_back(field, cosine, sine_table):
    halfway = field.shape[-1] // 2
    former = field[..., :halfway]
    latter = field[..., halfway:]
    cos_b = cosine[:, None, :]
    sin_b = sine_table[:, None, :]
    return jnp.concatenate(
        [former * cos_b + latter * sin_b, latter * cos_b - former * sin_b], axis=-1
    )


def norm_back(grad, normed, inv_scale, factor):
    lead_axes = tuple(range(grad.ndim - 1))
    factor_grad = jnp.sum(grad * normed, axis=lead_axes)
    scaled = grad * factor
    return (
        inv_scale * (scaled - normed * jnp.mean(scaled * normed, axis=-1, keepdims=True)),
        factor_grad,
    )


def gather_a2a(x, axis_name, size, axis):
    rep = jnp.broadcast_to(x[None], (size,) + x.shape)
    got = jnp.moveaxis(lax.all_to_all(rep, axis_name, 0, 0, tiled=True), 0, axis)
    return got.reshape(x.shape[:axis] + (size * x.shape[axis],) + x.shape[axis + 1 :])


def scatter_sum_a2a(x, axis_name, size, axis):
    parts = x.reshape(x.shape[:axis] + (size, x.shape[axis] // size) + x.shape[axis + 1 :])
    got = lax.all_to_all(parts, axis_name, axis, axis, tiled=True)
    return jnp.sum(got.astype(jnp.float32), axis=axis)


def per_device(
    hidden_in,
    block_map,
    doc_ids,
    routes,
    attn_gain,
    query_proj,
    key_proj,
    value_proj,
    query_gain,
    key_gain,
    out_proj,
    ffn_gain,
    router_proj,
    expert_gate,
    expert_up,
    expert_down,
    cotangent,
):
    tokens = hidden_in.shape[1]
    ctx_size = lax.axis_size("ctx")
    fsdp_size = lax.axis_size("fsdp")
    fsdp_index = lax.axis_index("fsdp")
    local_experts = expert_gate.shape[0]
    experts = local_experts * ctx_size
    capacity = min(tokens, 3 * tokens * TOP // (2 * experts))
    block_len = tokens // 2
    group_size = HEADS // KV_HEADS
    score_scale = HEAD_DIM ** (-0.5)
    heads_dev = HEADS // fsdp_size
    share = max(1, fsdp_size // KV_HEADS)
    kv_dev = max(1, heads_dev // group_size)
    group_dev = heads_dev // kv_dev
    d_part = D // fsdp_size
    seqs = fsdp_size
    group_rows = seqs * tokens

    ctx_index = lax.axis_index("ctx")
    own_blocks = lax.dynamic_slice_in_dim(block_map, 2 * ctx_index, 2, 0)
    offsets = jnp.arange(block_len, dtype=jnp.int32)
    local_pos = (own_blocks[:, None] * block_len + offsets[None, :]).reshape(-1)
    all_pos = (block_map[:, None] * block_len + offsets[None, :]).reshape(-1)
    cosine, sine_table = rotary(local_pos)
    hidden = hidden_in[0]
    first_scale = rms_scale(hidden)
    first_normed = hidden * first_scale
    first_input = (first_normed * attn_gain).astype(jnp.bfloat16)
    q_width, kv_width = heads_dev * HEAD_DIM, kv_dev * HEAD_DIM
    if share == 1:
        blocks = jnp.concatenate(
            [
                query_proj.reshape(d_part, fsdp_size, q_width),
                key_proj.reshape(d_part, fsdp_size, kv_width),
                value_proj.reshape(d_part, fsdp_size, kv_width),
            ],
            axis=2,
        )
        half = d_part // 2
        core = ctx_index % 2
        lanes = 128
        sent_rows = jnp.moveaxis(
            lax.dynamic_slice_in_dim(blocks, core * half, half, 0), 1, 0
        ).reshape(fsdp_size, -1, lanes)
        common = doc_ids.astype(jnp.bfloat16).reshape(-1, lanes)
        payload = jnp.concatenate(
            [sent_rows, jnp.broadcast_to(common[None], (fsdp_size,) + common.shape)], axis=1
        )
        got = lax.all_to_all(payload, "fsdp", 0, 0, tiled=True)
        w_rows = sent_rows.shape[1]
        mine = got[:, :w_rows].reshape(fsdp_size, half, -1)
        doc_rows = got[:, w_rows:].reshape(fsdp_size, -1).astype(jnp.float32)
        group_input = lax.all_gather(first_input, "fsdp", axis=0, tiled=True)
        other = lax.ppermute(mine, "ctx", [(i, i ^ 1) for i in range(ctx_size)])
        w_cols = jnp.where(
            core == 0, jnp.stack([mine, other], axis=1), jnp.stack([other, mine], axis=1)
        ).reshape(D, -1)
    else:
        group_input = gather_a2a(first_input, "fsdp", fsdp_size, 0)
        doc_rows = gather_a2a(doc_ids.astype(jnp.float32), "fsdp", fsdp_size, 0)
        kv_start = (fsdp_index // share) * HEAD_DIM
        w_cols = jnp.concatenate(
            [
                lax.all_to_all(query_proj, "fsdp", 1, 0, tiled=True),
                lax.dynamic_slice_in_dim(
                    lax.all_gather(key_proj, "fsdp", axis=0, tiled=True), kv_start, HEAD_DIM, 1
                ),
                lax.dynamic_slice_in_dim(
                    lax.all_gather(value_proj, "fsdp", axis=0, tiled=True), kv_start, HEAD_DIM, 1
                ),
            ],
            axis=1,
        )
    w_cols, expert_gate, expert_up, expert_down = lax.optimization_barrier(
        (w_cols, expert_gate, expert_up, expert_down)
    )
    docs_query = jnp.take(doc_rows, local_pos, axis=1)
    docs_key = jnp.take(doc_rows, all_pos, axis=1)
    visible = (all_pos[None, None, :] <= local_pos[None, :, None]) & (
        docs_key[:, None, :] == docs_query[:, :, None]
    )
    projected = matmul(group_input, w_cols)
    query_raw = projected[:, :q_width].reshape(seqs, tokens, heads_dev, HEAD_DIM)
    key_raw = projected[:, q_width : q_width + kv_width].reshape(seqs, tokens, kv_dev, HEAD_DIM)
    value_low = (
        projected[:, q_width + kv_width :]
        .astype(jnp.bfloat16)
        .reshape(seqs, tokens, kv_dev * HEAD_DIM)
    )
    query_scale = rms_scale(query_raw)
    query_normed = query_raw * query_scale
    query_rot = rotate(query_normed * query_gain, cosine, sine_table).astype(jnp.bfloat16)
    key_scale = rms_scale(key_raw)
    key_normed = key_raw * key_scale
    key_rot = (
        rotate(key_normed * key_gain, cosine, sine_table)
        .reshape(seqs, tokens, kv_dev * HEAD_DIM)
        .astype(jnp.bfloat16)
    )
    keys_all = gather_a2a(key_rot, "ctx", ctx_size, 1).reshape(seqs, -1, kv_dev, HEAD_DIM)
    values_all = gather_a2a(value_low, "ctx", ctx_size, 1).reshape(seqs, -1, kv_dev, HEAD_DIM)
    query_groups = query_rot.reshape(seqs, tokens, kv_dev, group_dev, HEAD_DIM)

    def masked_scores():
        scores = contract("stkgd,sjkd->skgtj", query_groups, keys_all) * score_scale
        return jnp.where(visible[:, None, None], scores, NEG_FILL)

    scores = masked_scores()
    peak = jnp.max(scores, axis=-1, keepdims=True)
    expo = jnp.exp(scores - peak)
    total = jnp.sum(expo, axis=-1, keepdims=True)
    probs_full = expo / total
    probs = probs_full.astype(jnp.bfloat16)
    attended = (
        contract("skgtj,sjkd->stkgd", probs, values_all)
        .astype(jnp.bfloat16)
        .reshape(group_rows, heads_dev * HEAD_DIM)
    )
    branch_parts = matmul(attended, out_proj).reshape(seqs, tokens, D)
    branch = scatter_sum_a2a(branch_parts.astype(jnp.bfloat16), "fsdp", fsdp_size, 0)[0]
    middle = hidden + branch
    second_scale = rms_scale(middle)
    second_normed = middle * second_scale
    second_input = (second_normed * ffn_gain).astype(jnp.bfloat16)
    gate_up = lax.all_gather(jnp.stack([expert_gate, expert_up]), "fsdp", axis=2, tiled=True)
    w_gate, w_up, w_down, w_router = (
        gate_up[0],
        gate_up[1],
        lax.all_gather(expert_down, "fsdp", axis=1, tiled=True),
        gather_a2a(router_proj, "fsdp", fsdp_size, 0),
    )
    logits = matmul(second_input, w_router)
    route_ids = routes[0]
    chosen = jnp.take_along_axis(logits, route_ids, axis=1)
    route_weights = jax.nn.softmax(chosen, axis=-1)
    flat_ids = route_ids.reshape(-1)
    expert_range = jnp.arange(experts, dtype=jnp.int32)
    one_hot = (flat_ids[:, None] == expert_range[None, :]).astype(jnp.int32)
    earlier = jnp.cumsum(one_hot, axis=0) - one_hot
    slot_index = jnp.sum(earlier * one_hot, axis=1)
    target = flat_ids * capacity + slot_index

    def dispatch(route_rows):
        buffer = jnp.zeros((experts * capacity, D), jnp.bfloat16).at[target].set(route_rows)
        return buffer.reshape(ctx_size, local_experts, capacity, D)

    def to_experts(buffer):
        got = lax.all_to_all(buffer, "ctx", 0, 0, tiled=True)
        return got.transpose(1, 0, 2, 3).reshape(local_experts, ctx_size * capacity, D)

    def from_experts(rows):
        parts = rows.reshape(local_experts, ctx_size, capacity, D).transpose(1, 0, 2, 3)
        back = lax.all_to_all(parts, "ctx", 0, 0, tiled=True)
        return back.reshape(experts * capacity, D)

    def collect(returned):
        return jnp.take(returned, target, axis=0)

    received = to_experts(dispatch(jnp.repeat(second_input, TOP, axis=0)))
    gate_val = contract("erd,edf->erf", received, w_gate)
    up_val = contract("erd,edf->erf", received, w_up)
    gate_sig = jax.nn.sigmoid(gate_val)
    hid_low = (gate_val * gate_sig * up_val).astype(jnp.bfloat16)
    expert_out = contract("erf,efd->erd", hid_low, w_down).astype(jnp.bfloat16)
    route_out = (
        collect(from_experts(expert_out))
        .reshape(tokens, TOP, D)
        .astype(jnp.float32)
    )
    layer_out = middle + jnp.einsum("tr,trd->td", route_weights, route_out)
    grad_out = cotangent[0]
    grad_weights = jnp.einsum("td,trd->tr", grad_out, route_out)
    grad_routes = (
        (route_weights[:, :, None] * grad_out[:, None, :])
        .astype(jnp.bfloat16)
        .reshape(tokens * TOP, D)
    )
    grad_expert = to_experts(dispatch(grad_routes))
    grad_hid = contract("erd,efd->erf", grad_expert, w_down)
    down_grad_full = contract("erf,erd->efd", hid_low, grad_expert)
    grad_gate = (grad_hid * up_val * gate_sig * (1.0 + gate_val * (1.0 - gate_sig))).astype(
        jnp.bfloat16
    )
    grad_up = (grad_hid * gate_val * gate_sig).astype(jnp.bfloat16)
    gate_grad_full = contract("erd,erf->edf", received, grad_gate)
    up_grad_full = contract("erd,erf->edf", received, grad_up)
    grad_rows = (
        contract("erf,edf->erd", grad_gate, w_gate) + contract("erf,edf->erd", grad_up, w_up)
    ).astype(jnp.bfloat16)
    grad_copies = collect(from_experts(grad_rows)).reshape(tokens, TOP, D)
    grad_chosen = route_weights * (
        grad_weights - jnp.sum(route_weights * grad_weights, axis=-1, keepdims=True)
    )
    route_hot = (route_ids[:, :, None] == expert_range[None, None, :]).astype(jnp.float32)
    grad_logits = jnp.einsum("tr,tre->te", grad_chosen, route_hot).astype(jnp.bfloat16)
    router_grad_full = contract("td,te->de", second_input, grad_logits)
    grad_second = jnp.sum(grad_copies.astype(jnp.float32), axis=1) + contract(
        "te,de->td", grad_logits, w_router
    )
    grad_middle, ffn_gain_grad = norm_back(grad_second, second_normed, second_scale, ffn_gain)
    grad_middle = grad_middle + grad_out

    grad_branch = gather_a2a(grad_middle.astype(jnp.bfloat16), "fsdp", fsdp_size, 0)
    out_grad_part = contract("tq,td->qd", attended, grad_branch)
    grad_attended = contract("td,qd->tq", grad_branch, out_proj).astype(jnp.bfloat16)
    grad_groups = grad_attended.reshape(seqs, tokens, kv_dev, group_dev, HEAD_DIM)

    probs_back = probs_full
    grad_probs = contract("stkgd,sjkd->skgtj", grad_groups, values_all)
    delta = jnp.sum(probs_back * grad_probs, axis=-1, keepdims=True)
    grad_scores = (probs_back * (grad_probs - delta)).astype(jnp.bfloat16)
    grad_qgroups = contract("skgtj,sjkd->stkgd", grad_scores, keys_all) * score_scale
    grad_kheads = contract("skgtj,stkgd->sjkd", grad_scores, query_groups) * score_scale
    grad_vheads = contract("skgtj,stkgd->sjkd", probs_back.astype(jnp.bfloat16), grad_groups)

    def kv_reduce(grads):
        summed = scatter_sum_a2a(
            grads.reshape(seqs, -1, kv_dev * HEAD_DIM).astype(jnp.bfloat16), "ctx", ctx_size, 1
        )
        total = summed
        for step in range(1, share):
            pairs = [
                (i, (i // share) * share + (i % share + step) % share) for i in range(fsdp_size)
            ]
            total = total + lax.ppermute(summed, "fsdp", pairs)
        return total

    grad_key_rot = kv_reduce(grad_kheads)
    grad_value = kv_reduce(grad_vheads)
    grad_query_rot = grad_qgroups.reshape(seqs, tokens, heads_dev, HEAD_DIM)
    grad_query, query_gain_grad = norm_back(
        rotate_back(grad_query_rot, cosine, sine_table), query_normed, query_scale, query_gain
    )
    grad_key, key_gain_grad = norm_back(
        rotate_back(grad_key_rot.reshape(seqs, tokens, kv_dev, HEAD_DIM), cosine, sine_table),
        key_normed,
        key_scale,
        key_gain,
    )
    if share > 1:
        key_gain_grad = key_gain_grad * (fsdp_index % share == 0).astype(jnp.float32)
    grad_query = grad_query.reshape(group_rows, heads_dev * HEAD_DIM).astype(jnp.bfloat16)
    grad_key = grad_key.reshape(group_rows, kv_dev * HEAD_DIM).astype(jnp.bfloat16)
    grad_value = grad_value.reshape(group_rows, kv_dev * HEAD_DIM).astype(jnp.bfloat16)

    def gather_heads(parts):
        whole = parts.reshape(group_rows, -1)
        if share > 1:
            whole = whole.reshape(group_rows, KV_HEADS, share, HEAD_DIM)[:, :, 0]
            whole = whole.reshape(group_rows, KV_HEADS * HEAD_DIM)
        return whole

    joined = gather_a2a(
        jnp.concatenate([grad_query, grad_key, grad_value], axis=1)[:, None], "fsdp", fsdp_size, 1
    )
    query_all = joined[:, :, :q_width].reshape(group_rows, -1)
    key_all = gather_heads(joined[:, :, q_width : q_width + kv_width])
    value_all = gather_heads(joined[:, :, q_width + kv_width :])
    input_part = lax.dynamic_slice_in_dim(group_input, fsdp_index * d_part, d_part, 1)
    query_grad_part = contract("td,tq->dq", input_part, query_all)
    key_grad_part = contract("td,tq->dq", input_part, key_all)
    value_grad_part = contract("td,tq->dq", input_part, value_all)
    grad_first_cols = (
        contract("tq,dq->td", query_all, query_proj)
        + contract("tq,dq->td", key_all, key_proj)
        + contract("tq,dq->td", value_all, value_proj)
    )
    grad_first = lax.all_to_all(
        grad_first_cols.reshape(seqs, tokens, d_part), "fsdp", 0, 2, tiled=True
    )[0]
    grad_hidden, attn_gain_grad = norm_back(grad_first, first_normed, first_scale, attn_gain)
    grad_hidden = grad_hidden + grad_middle
    down_grad = lax.psum_scatter(
        down_grad_full.astype(jnp.bfloat16), "fsdp", scatter_dimension=1, tiled=True
    ).astype(jnp.float32)
    gate_up_grad = lax.psum_scatter(
        jnp.stack([gate_grad_full, up_grad_full]).astype(jnp.bfloat16),
        "fsdp",
        scatter_dimension=2,
        tiled=True,
    ).astype(jnp.float32)
    gate_grad, up_grad = gate_up_grad[0], gate_up_grad[1]
    router_shard = scatter_sum_a2a(router_grad_full, "fsdp", fsdp_size, 0)
    out_grad = lax.psum(out_grad_part, "ctx")
    query_grad, key_grad, value_grad = (
        lax.psum(part.astype(jnp.bfloat16), "ctx").astype(jnp.float32)
        for part in (query_grad_part, key_grad_part, value_grad_part)
    )
    router_grad = jnp.sum(gather_a2a(router_shard[None], "ctx", ctx_size, 0), axis=0)
    attn_gain_total, query_gain_total, key_gain_total, ffn_gain_total = lax.psum(
        (attn_gain_grad, query_gain_grad, key_gain_grad, ffn_gain_grad), ("ctx", "fsdp")
    )
    return (
        layer_out[None],
        grad_hidden[None],
        attn_gain_total,
        query_grad,
        key_grad,
        value_grad,
        query_gain_total,
        key_gain_total,
        out_grad,
        ffn_gain_total,
        router_grad,
        gate_grad,
        up_grad,
        down_grad,
    )


def solution(mesh):
    placed = (
        P("fsdp", "ctx", None),
        P(),
        P("fsdp", None),
        P("fsdp", "ctx", None),
        P(),
        P("fsdp", None),
        P("fsdp", None),
        P("fsdp", None),
        P(),
        P(),
        P("fsdp", None),
        P(),
        P("fsdp", None),
        P("ctx", "fsdp", None),
        P("ctx", "fsdp", None),
        P("ctx", "fsdp", None),
        P("fsdp", "ctx", None),
    )
    return jax.shard_map(
        per_device,
        mesh=mesh,
        in_specs=placed,
        out_specs=(
            P("fsdp", "ctx", None),
            P("fsdp", "ctx", None),
            P(),
            P("fsdp", None),
            P("fsdp", None),
            P("fsdp", None),
            P(),
            P(),
            P("fsdp", None),
            P(),
            P("fsdp", None),
            P("ctx", "fsdp", None),
            P("ctx", "fsdp", None),
            P("ctx", "fsdp", None),
        ),
        check_vma=False,
    )
```

```python
import jax
import jax.numpy as jnp
from jax import lax
from jax.sharding import PartitionSpec as P


D = 2048
HEADS = 32
KV_HEADS = 4
HEAD_DIM = 128
TOP = 8


EPSILON = 1e-06
ROPE_BASE = 1000000.0
NEG_FILL = -1e30


def matmul(left, right):
    return jnp.dot(left, right, preferred_element_type=jnp.float32)


def contract(form, left, right):
    return jnp.einsum(form, left, right, preferred_element_type=jnp.float32)


def rms_scale(field):
    return lax.rsqrt(jnp.mean(field * field, axis=-1, keepdims=True) + EPSILON)


def rotary(positions):
    halfway = HEAD_DIM // 2
    inverse = ROPE_BASE ** (-2.0 * jnp.arange(halfway, dtype=jnp.float32) / HEAD_DIM)
    angle = positions.astype(jnp.float32)[:, None] * inverse[None, :]
    return (jnp.cos(angle), jnp.sin(angle))


def rotate(field, cosine, sine_table):
    halfway = field.shape[-1] // 2
    former = field[..., :halfway]
    latter = field[..., halfway:]
    cos_b = cosine[:, None, :]
    sin_b = sine_table[:, None, :]
    return jnp.concatenate(
        [former * cos_b - latter * sin_b, latter * cos_b + former * sin_b], axis=-1
    )


def rotate_back(field, cosine, sine_table):
    halfway = field.shape[-1] // 2
    former = field[..., :halfway]
    latter = field[..., halfway:]
    cos_b = cosine[:, None, :]
    sin_b = sine_table[:, None, :]
    return jnp.concatenate(
        [former * cos_b + latter * sin_b, latter * cos_b - former * sin_b], axis=-1
    )


def norm_back(grad, normed, inv_scale, factor):
    lead_axes = tuple(range(grad.ndim - 1))
    factor_grad = jnp.sum(grad * normed, axis=lead_axes)
    scaled = grad * factor
    return (
        inv_scale * (scaled - normed * jnp.mean(scaled * normed, axis=-1, keepdims=True)),
        factor_grad,
    )


def gather_a2a(x, axis_name, size, axis):
    rep = jnp.broadcast_to(x[None], (size,) + x.shape)
    got = jnp.moveaxis(lax.all_to_all(rep, axis_name, 0, 0, tiled=True), 0, axis)
    return got.reshape(x.shape[:axis] + (size * x.shape[axis],) + x.shape[axis + 1 :])


def scatter_sum_a2a(x, axis_name, size, axis):
    parts = x.reshape(x.shape[:axis] + (size, x.shape[axis] // size) + x.shape[axis + 1 :])
    got = lax.all_to_all(parts, axis_name, axis, axis, tiled=True)
    return jnp.sum(got.astype(jnp.float32), axis=axis)


def per_device(
    hidden_in,
    block_map,
    doc_ids,
    routes,
    attn_gain,
    query_proj,
    key_proj,
    value_proj,
    query_gain,
    key_gain,
    out_proj,
    ffn_gain,
    router_proj,
    expert_gate,
    expert_up,
    expert_down,
    cotangent,
):
    tokens = hidden_in.shape[1]
    ctx_size = lax.axis_size("ctx")
    fsdp_size = lax.axis_size("fsdp")
    fsdp_index = lax.axis_index("fsdp")
    local_experts = expert_gate.shape[0]
    experts = local_experts * ctx_size
    capacity = min(tokens, 3 * tokens * TOP // (2 * experts))
    block_len = tokens // 2
    group_size = HEADS // KV_HEADS
    score_scale = HEAD_DIM ** (-0.5)
    heads_dev = HEADS // fsdp_size
    share = max(1, fsdp_size // KV_HEADS)
    kv_dev = max(1, heads_dev // group_size)
    group_dev = heads_dev // kv_dev
    d_part = D // fsdp_size
    seqs = fsdp_size
    group_rows = seqs * tokens

    ctx_index = lax.axis_index("ctx")
    own_blocks = lax.dynamic_slice_in_dim(block_map, 2 * ctx_index, 2, 0)
    offsets = jnp.arange(block_len, dtype=jnp.int32)
    local_pos = (own_blocks[:, None] * block_len + offsets[None, :]).reshape(-1)
    all_pos = (block_map[:, None] * block_len + offsets[None, :]).reshape(-1)
    cosine, sine_table = rotary(local_pos)
    hidden = hidden_in[0]
    first_scale = rms_scale(hidden)
    first_normed = hidden * first_scale
    first_input = (first_normed * attn_gain).astype(jnp.bfloat16)
    q_width, kv_width = heads_dev * HEAD_DIM, kv_dev * HEAD_DIM
    if share == 1:
        blocks = jnp.concatenate(
            [
                query_proj.reshape(d_part, fsdp_size, q_width),
                key_proj.reshape(d_part, fsdp_size, kv_width),
                value_proj.reshape(d_part, fsdp_size, kv_width),
            ],
            axis=2,
        )
        half = d_part // 2
        core = ctx_index % 2
        lanes = 128
        sent_rows = jnp.moveaxis(
            lax.dynamic_slice_in_dim(blocks, core * half, half, 0), 1, 0
        ).reshape(fsdp_size, -1, lanes)
        common = doc_ids.astype(jnp.bfloat16).reshape(-1, lanes)
        payload = jnp.concatenate(
            [sent_rows, jnp.broadcast_to(common[None], (fsdp_size,) + common.shape)], axis=1
        )
        got = lax.all_to_all(payload, "fsdp", 0, 0, tiled=True)
        w_rows = sent_rows.shape[1]
        mine = got[:, :w_rows].reshape(fsdp_size, half, -1)
        doc_rows = got[:, w_rows:].reshape(fsdp_size, -1).astype(jnp.float32)
        group_input = lax.all_gather(first_input, "fsdp", axis=0, tiled=True)
        other = lax.ppermute(mine, "ctx", [(i, i ^ 1) for i in range(ctx_size)])
        w_cols = jnp.where(
            core == 0, jnp.stack([mine, other], axis=1), jnp.stack([other, mine], axis=1)
        ).reshape(D, -1)
    else:
        group_input = gather_a2a(first_input, "fsdp", fsdp_size, 0)
        doc_rows = gather_a2a(doc_ids.astype(jnp.float32), "fsdp", fsdp_size, 0)
        kv_start = (fsdp_index // share) * HEAD_DIM
        w_cols = jnp.concatenate(
            [
                lax.all_to_all(query_proj, "fsdp", 1, 0, tiled=True),
                lax.dynamic_slice_in_dim(
                    lax.all_gather(key_proj, "fsdp", axis=0, tiled=True), kv_start, HEAD_DIM, 1
                ),
                lax.dynamic_slice_in_dim(
                    lax.all_gather(value_proj, "fsdp", axis=0, tiled=True), kv_start, HEAD_DIM, 1
                ),
            ],
            axis=1,
        )
    w_cols, expert_gate, expert_up, expert_down = lax.optimization_barrier(
        (w_cols, expert_gate, expert_up, expert_down)
    )
    docs_query = jnp.take(doc_rows, local_pos, axis=1)
    docs_key = jnp.take(doc_rows, all_pos, axis=1)
    visible = (all_pos[None, None, :] <= local_pos[None, :, None]) & (
        docs_key[:, None, :] == docs_query[:, :, None]
    )
    projected = matmul(group_input, w_cols)
    query_raw = projected[:, :q_width].reshape(seqs, tokens, heads_dev, HEAD_DIM)
    key_raw = projected[:, q_width : q_width + kv_width].reshape(seqs, tokens, kv_dev, HEAD_DIM)
    value_low = (
        projected[:, q_width + kv_width :]
        .astype(jnp.bfloat16)
        .reshape(seqs, tokens, kv_dev * HEAD_DIM)
    )
    query_scale = rms_scale(query_raw)
    query_normed = query_raw * query_scale
    query_rot = rotate(query_normed * query_gain, cosine, sine_table).astype(jnp.bfloat16)
    key_scale = rms_scale(key_raw)
    key_normed = key_raw * key_scale
    key_rot = (
        rotate(key_normed * key_gain, cosine, sine_table)
        .reshape(seqs, tokens, kv_dev * HEAD_DIM)
        .astype(jnp.bfloat16)
    )
    keys_all = gather_a2a(key_rot, "ctx", ctx_size, 1).reshape(seqs, -1, kv_dev, HEAD_DIM)
    values_all = gather_a2a(value_low, "ctx", ctx_size, 1).reshape(seqs, -1, kv_dev, HEAD_DIM)
    query_groups = query_rot.reshape(seqs, tokens, kv_dev, group_dev, HEAD_DIM)

    def masked_scores():
        scores = contract("stkgd,sjkd->skgtj", query_groups, keys_all) * score_scale
        return jnp.where(visible[:, None, None], scores, NEG_FILL)

    scores = masked_scores()
    peak = jnp.max(scores, axis=-1, keepdims=True)
    expo = jnp.exp(scores - peak)
    total = jnp.sum(expo, axis=-1, keepdims=True)
    probs_full = expo / total
    probs = probs_full.astype(jnp.bfloat16)
    attended = (
        contract("skgtj,sjkd->stkgd", probs, values_all)
        .astype(jnp.bfloat16)
        .reshape(group_rows, heads_dev * HEAD_DIM)
    )
    branch_parts = matmul(attended, out_proj).reshape(seqs, tokens, D)
    branch = scatter_sum_a2a(branch_parts.astype(jnp.bfloat16), "fsdp", fsdp_size, 0)[0]
    middle = hidden + branch
    second_scale = rms_scale(middle)
    second_normed = middle * second_scale
    second_input = (second_normed * ffn_gain).astype(jnp.bfloat16)
    w_gate, w_up, w_down, w_router = (
        lax.all_gather(expert_gate, "fsdp", axis=1, tiled=True),
        lax.all_gather(expert_up, "fsdp", axis=1, tiled=True),
        lax.all_gather(expert_down, "fsdp", axis=1, tiled=True),
        gather_a2a(router_proj, "fsdp", fsdp_size, 0),
    )
    logits = matmul(second_input, w_router)
    route_ids = routes[0]
    chosen = jnp.take_along_axis(logits, route_ids, axis=1)
    route_weights = jax.nn.softmax(chosen, axis=-1)
    flat_ids = route_ids.reshape(-1)
    expert_range = jnp.arange(experts, dtype=jnp.int32)
    one_hot = (flat_ids[:, None] == expert_range[None, :]).astype(jnp.int32)
    earlier = jnp.cumsum(one_hot, axis=0) - one_hot
    slot_index = jnp.sum(earlier * one_hot, axis=1)
    target = flat_ids * capacity + slot_index

    def dispatch(route_rows):
        buffer = jnp.zeros((experts * capacity, D), jnp.bfloat16).at[target].set(route_rows)
        return buffer.reshape(ctx_size, local_experts, capacity, D)

    def to_experts(buffer):
        got = lax.all_to_all(buffer, "ctx", 0, 0, tiled=True)
        return got.transpose(1, 0, 2, 3).reshape(local_experts, ctx_size * capacity, D)

    def from_experts(rows):
        parts = rows.reshape(local_experts, ctx_size, capacity, D).transpose(1, 0, 2, 3)
        back = lax.all_to_all(parts, "ctx", 0, 0, tiled=True)
        return back.reshape(experts * capacity, D)

    def collect(returned):
        return jnp.take(returned, target, axis=0)

    received = to_experts(dispatch(jnp.repeat(second_input, TOP, axis=0)))
    gate_val = contract("erd,edf->erf", received, w_gate)
    up_val = contract("erd,edf->erf", received, w_up)
    gate_sig = jax.nn.sigmoid(gate_val)
    hid_low = (gate_val * gate_sig * up_val).astype(jnp.bfloat16)
    expert_out = contract("erf,efd->erd", hid_low, w_down).astype(jnp.bfloat16)
    route_out = (
        collect(from_experts(expert_out))
        .reshape(tokens, TOP, D)
        .astype(jnp.float32)
    )
    layer_out = middle + jnp.einsum("tr,trd->td", route_weights, route_out)
    grad_out = cotangent[0]
    grad_weights = jnp.einsum("td,trd->tr", grad_out, route_out)
    grad_routes = (
        (route_weights[:, :, None] * grad_out[:, None, :])
        .astype(jnp.bfloat16)
        .reshape(tokens * TOP, D)
    )
    grad_expert = to_experts(dispatch(grad_routes))
    grad_hid = contract("erd,efd->erf", grad_expert, w_down)
    down_grad_full = contract("erf,erd->efd", hid_low, grad_expert)
    grad_gate = (grad_hid * up_val * gate_sig * (1.0 + gate_val * (1.0 - gate_sig))).astype(
        jnp.bfloat16
    )
    grad_up = (grad_hid * gate_val * gate_sig).astype(jnp.bfloat16)
    gate_grad_full = contract("erd,erf->edf", received, grad_gate)
    up_grad_full = contract("erd,erf->edf", received, grad_up)
    grad_rows = (
        contract("erf,edf->erd", grad_gate, w_gate) + contract("erf,edf->erd", grad_up, w_up)
    ).astype(jnp.bfloat16)
    grad_copies = collect(from_experts(grad_rows)).reshape(tokens, TOP, D)
    grad_chosen = route_weights * (
        grad_weights - jnp.sum(route_weights * grad_weights, axis=-1, keepdims=True)
    )
    route_hot = (route_ids[:, :, None] == expert_range[None, None, :]).astype(jnp.float32)
    grad_logits = jnp.einsum("tr,tre->te", grad_chosen, route_hot).astype(jnp.bfloat16)
    router_grad_full = contract("td,te->de", second_input, grad_logits)
    grad_second = jnp.sum(grad_copies.astype(jnp.float32), axis=1) + contract(
        "te,de->td", grad_logits, w_router
    )
    grad_middle, ffn_gain_grad = norm_back(grad_second, second_normed, second_scale, ffn_gain)
    grad_middle = grad_middle + grad_out

    grad_branch = gather_a2a(grad_middle.astype(jnp.bfloat16), "fsdp", fsdp_size, 0)
    out_grad_part = contract("tq,td->qd", attended, grad_branch)
    grad_attended = contract("td,qd->tq", grad_branch, out_proj).astype(jnp.bfloat16)
    grad_groups = grad_attended.reshape(seqs, tokens, kv_dev, group_dev, HEAD_DIM)

    probs_back = probs_full
    grad_probs = contract("stkgd,sjkd->skgtj", grad_groups, values_all)
    delta = jnp.sum(probs_back * grad_probs, axis=-1, keepdims=True)
    grad_scores = (probs_back * (grad_probs - delta)).astype(jnp.bfloat16)
    grad_qgroups = contract("skgtj,sjkd->stkgd", grad_scores, keys_all) * score_scale
    grad_kheads = contract("skgtj,stkgd->sjkd", grad_scores, query_groups) * score_scale
    grad_vheads = contract("skgtj,stkgd->sjkd", probs_back.astype(jnp.bfloat16), grad_groups)

    def kv_reduce(grads):
        summed = scatter_sum_a2a(
            grads.reshape(seqs, -1, kv_dev * HEAD_DIM).astype(jnp.bfloat16), "ctx", ctx_size, 1
        )
        total = summed
        for step in range(1, share):
            pairs = [
                (i, (i // share) * share + (i % share + step) % share) for i in range(fsdp_size)
            ]
            total = total + lax.ppermute(summed, "fsdp", pairs)
        return total

    grad_key_rot = kv_reduce(grad_kheads)
    grad_value = kv_reduce(grad_vheads)
    grad_query_rot = grad_qgroups.reshape(seqs, tokens, heads_dev, HEAD_DIM)
    grad_query, query_gain_grad = norm_back(
        rotate_back(grad_query_rot, cosine, sine_table), query_normed, query_scale, query_gain
    )
    grad_key, key_gain_grad = norm_back(
        rotate_back(grad_key_rot.reshape(seqs, tokens, kv_dev, HEAD_DIM), cosine, sine_table),
        key_normed,
        key_scale,
        key_gain,
    )
    if share > 1:
        key_gain_grad = key_gain_grad * (fsdp_index % share == 0).astype(jnp.float32)
    grad_query = grad_query.reshape(group_rows, heads_dev * HEAD_DIM).astype(jnp.bfloat16)
    grad_key = grad_key.reshape(group_rows, kv_dev * HEAD_DIM).astype(jnp.bfloat16)
    grad_value = grad_value.reshape(group_rows, kv_dev * HEAD_DIM).astype(jnp.bfloat16)

    def gather_heads(parts):
        whole = parts.reshape(group_rows, -1)
        if share > 1:
            whole = whole.reshape(group_rows, KV_HEADS, share, HEAD_DIM)[:, :, 0]
            whole = whole.reshape(group_rows, KV_HEADS * HEAD_DIM)
        return whole

    joined = gather_a2a(
        jnp.concatenate([grad_query, grad_key, grad_value], axis=1)[:, None], "fsdp", fsdp_size, 1
    )
    query_all = joined[:, :, :q_width].reshape(group_rows, -1)
    key_all = gather_heads(joined[:, :, q_width : q_width + kv_width])
    value_all = gather_heads(joined[:, :, q_width + kv_width :])
    input_part = lax.dynamic_slice_in_dim(group_input, fsdp_index * d_part, d_part, 1)
    query_grad_part = contract("td,tq->dq", input_part, query_all)
    key_grad_part = contract("td,tq->dq", input_part, key_all)
    value_grad_part = contract("td,tq->dq", input_part, value_all)
    grad_first_cols = (
        contract("tq,dq->td", query_all, query_proj)
        + contract("tq,dq->td", key_all, key_proj)
        + contract("tq,dq->td", value_all, value_proj)
    )
    grad_first = lax.all_to_all(
        grad_first_cols.reshape(seqs, tokens, d_part).astype(jnp.bfloat16), "fsdp", 0, 2, tiled=True
    )[0].astype(jnp.float32)
    grad_hidden, attn_gain_grad = norm_back(grad_first, first_normed, first_scale, attn_gain)
    grad_hidden = grad_hidden + grad_middle
    gate_grad, up_grad, down_grad = (
        lax.psum_scatter(
            full.astype(jnp.bfloat16), "fsdp", scatter_dimension=1, tiled=True
        ).astype(jnp.float32)
        for full in (gate_grad_full, up_grad_full, down_grad_full)
    )
    router_shard = scatter_sum_a2a(router_grad_full, "fsdp", fsdp_size, 0)
    out_grad = lax.psum(out_grad_part, "ctx")
    query_grad, key_grad, value_grad = (
        lax.psum(part.astype(jnp.bfloat16), "ctx").astype(jnp.float32)
        for part in (query_grad_part, key_grad_part, value_grad_part)
    )
    router_grad = jnp.sum(gather_a2a(router_shard[None], "ctx", ctx_size, 0), axis=0)
    attn_gain_total, query_gain_total, key_gain_total, ffn_gain_total = lax.psum(
        (attn_gain_grad, query_gain_grad, key_gain_grad, ffn_gain_grad), ("ctx", "fsdp")
    )
    return (
        layer_out[None],
        grad_hidden[None],
        attn_gain_total,
        query_grad,
        key_grad,
        value_grad,
        query_gain_total,
        key_gain_total,
        out_grad,
        ffn_gain_total,
        router_grad,
        gate_grad,
        up_grad,
        down_grad,
    )


def solution(mesh):
    placed = (
        P("fsdp", "ctx", None),
        P(),
        P("fsdp", None),
        P("fsdp", "ctx", None),
        P(),
        P("fsdp", None),
        P("fsdp", None),
        P("fsdp", None),
        P(),
        P(),
        P("fsdp", None),
        P(),
        P("fsdp", None),
        P("ctx", "fsdp", None),
        P("ctx", "fsdp", None),
        P("ctx", "fsdp", None),
        P("fsdp", "ctx", None),
    )
    return jax.shard_map(
        per_device,
        mesh=mesh,
        in_specs=placed,
        out_specs=(
            P("fsdp", "ctx", None),
            P("fsdp", "ctx", None),
            P(),
            P("fsdp", None),
            P("fsdp", None),
            P("fsdp", None),
            P(),
            P(),
            P("fsdp", None),
            P(),
            P("fsdp", None),
            P("ctx", "fsdp", None),
            P("ctx", "fsdp", None),
            P("ctx", "fsdp", None),
        ),
        check_vma=False,
    )
```
